256 devices in a mesh: gx: 16 (over y, x), gy: 16 (over z, core).
Axes of the slice: x: 4, y: 4, z: 8, core: 2. Of those that a mesh axis runs over, the one named last changes fastest.
Arguments:
- forcing: float32 [4, 2, 1024, 2048], P(None, None, 'gx', 'gy'), may hold values from -18 to 18
- observed: float32 [4, 2, 1024, 2048], P(None, None, 'gx', 'gy'), may hold values from -6 to 6
- viscosity: float32 [1024, 2048], P('gx', 'gy'), may hold values from 0.05 to 0.5
- friction: float32 [1024, 2048], P('gx', 'gy'), may hold values from 0.2 to 2
- ice_mask: int32 [1024, 2048], P('gx', 'gy'), may hold values from 0 to 2
- dirichlet: int32 [1024, 2048], P('gx', 'gy'), may hold values 0 or 1
Outputs:
- velocity: float32 [4, 2, 1024, 2048], P(None, None, 'gx', 'gy')
- gradient: float32 [1024, 2048], P('gx', 'gy')
The draws below stay inside these ranges and needn't reach their ends.
All inputs are finite; a program needn't handle non-finite values. No bound on the sum of `dirichlet` on one device may be relied on, other than what follows from the above.
Results may differ from the reference program's by a relative error of at most 0.00002.
Values sent between devices are 32-bit elements; how exact they have to be, the bound alone decides.
No kernel may reach another device: no remote copies, remote signals or barrier semaphores. Data moves between devices by JAX's collectives and lax.ppermute only.
A program may use at most 64 MiB of HBM per device.

```python
import math
import jax
import jax.numpy as jnp

EPOCHS = 4
SWEEPS = 3
NX = 1024
NY = 2048


def place_ends(entries, key, least, top_value):
    place = [jax.random.randint(jax.random.fold_in(key, axis), (), 0, length) for axis, length in enumerate(entries.shape)]
    widest = entries.shape.index(max(entries.shape))
    neighbour = place[:widest] + [(place[widest] + 1) % entries.shape[widest]] + place[widest + 1:]
    return entries.at[tuple(place)].set(least).at[tuple(neighbour)].set(top_value)


def levels(key, shape, pieces, smallest, top_value):
    factor_of = 1.0
    for axis_at, blocks in pieces:
        steps = jax.random.uniform(jax.random.fold_in(jax.random.fold_in(key, 6), axis_at), (blocks,), jnp.float32, smallest / len(pieces), top_value / len(pieces))
        factor_of = factor_of * jnp.repeat(jnp.exp(steps), shape[axis_at] // blocks).reshape((-1,) + (1,) * (len(shape) - 1 - axis_at))
    return factor_of


def scatter_about(rng, dims, spread, limit, cuts=(), held_as=jnp.bfloat16):
    array = spread * jax.random.normal(rng, dims, jnp.float32)
    if cuts:
        array = array * levels(rng, dims, cuts, -0.22, 0.18)
    return jnp.clip(array, -limit, limit).astype(held_as)


def setup_inputs(seed: int = 0) -> dict:
    seeds = jax.random.split(jax.random.key(seed), 7)
    return {
        "forcing": scatter_about(seeds[0], (EPOCHS, 2, NX, NY), 3.0, 18.0, ((2, 16), (3, 16)), jnp.float32),
        "observed": scatter_about(seeds[1], (EPOCHS, 2, NX, NY), 1.0, 6.0, ((2, 16), (3, 16)), jnp.float32),
        "viscosity": jnp.clip(jnp.exp(math.log(0.5) - 2.3025851 * jax.random.uniform(seeds[2], (NX, NY), jnp.float32) ** levels(seeds[2], (NX, NY), ((0, 16), (1, 16)), -0.2, 0.2)), 0.05, 0.5),
        "friction": jnp.clip(jnp.exp(math.log(2.0) - 2.3025851 * jax.random.uniform(seeds[3], (NX, NY), jnp.float32) ** levels(seeds[3], (NX, NY), ((0, 16), (1, 16)), -0.2, 0.2)), 0.2, 2.0),
        "ice_mask": place_ends(jax.random.randint(seeds[4], (NX, NY), 0, 3), jax.random.fold_in(seeds[4], 1), 0, 2).astype(jnp.int32),
        "dirichlet": place_ends((jax.random.randint(seeds[5], (NX, NY), 0, 16) < 1).astype(jnp.int32), jax.random.fold_in(seeds[5], 1), 0, 1),
    }


UPPER_BOUND = 2.4
LOWER_BOUND = 0.05
FREE_DRAG = 4.0


def face_values(eta_ext):
    centre = eta_ext[1:-1, 1:-1]
    north = eta_ext[2:, 1:-1]
    south = eta_ext[:-2, 1:-1]
    east = eta_ext[1:-1, 2:]
    west = eta_ext[1:-1, :-2]
    return north, south, east, west, 0.5 * (centre + north), 0.5 * (centre + south), 0.5 * (centre + east), 0.5 * (centre + west)


def stencil_apply(field, eta_ext, node_drag):
    north, south, east, west, face_np, face_sm, face_ep, face_wm = face_values(eta_ext)
    along_u = field[:, 0]
    along_v = field[:, 1]

    def normal_part(values, weight_rows, weight_cols):
        middle = values[:, 1:-1, 1:-1]
        rows_part = face_np * (values[:, 2:, 1:-1] - middle) - face_sm * (middle - values[:, :-2, 1:-1])
        cols_part = face_ep * (values[:, 1:-1, 2:] - middle) - face_wm * (middle - values[:, 1:-1, :-2])
        return weight_rows * rows_part + weight_cols * cols_part

    def cross_part(values, weight_rows, weight_cols):
        slope_cols = 0.5 * (values[:, :, 2:] - values[:, :, :-2])
        slope_rows = 0.5 * (values[:, 2:, :] - values[:, :-2, :])
        first = 0.5 * weight_rows * (north * slope_cols[:, 2:, :] - south * slope_cols[:, :-2, :])
        second = 0.5 * weight_cols * (east * slope_rows[:, :, 2:] - west * slope_rows[:, :, :-2])
        return first + second

    image_u = node_drag * along_u[:, 1:-1, 1:-1] - normal_part(along_u, 4.0, 1.0) - cross_part(along_v, 2.0, 1.0)
    image_v = node_drag * along_v[:, 1:-1, 1:-1] - normal_part(along_v, 1.0, 4.0) - cross_part(along_u, 1.0, 2.0)
    return jnp.stack([image_u, image_v], axis=1)


def diagonal_terms(eta_ext, node_drag):
    north, south, east, west, face_np, face_sm, face_ep, face_wm = face_values(eta_ext)
    rows_sum = face_np + face_sm
    cols_sum = face_ep + face_wm
    return jnp.stack([4.0 * rows_sum + cols_sum + node_drag, rows_sum + 4.0 * cols_sum + node_drag], axis=0)


def chebyshev_sweeps(rhs, eta_pad, node_drag, inverse_diag):
    centre_value = 0.5 * (UPPER_BOUND + LOWER_BOUND)
    half_width = 0.5 * (UPPER_BOUND - LOWER_BOUND)
    ratio_value = centre_value / half_width
    weight_now = 1.0 / ratio_value
    residual = rhs
    direction = inverse_diag * residual / centre_value
    iterate = jnp.zeros_like(rhs)
    for sweep_no in range(SWEEPS + 1):
        iterate = iterate + direction
        if sweep_no < SWEEPS:
            padded = jnp.pad(direction, ((0, 0), (0, 0), (1, 1), (1, 1)))
            residual = residual - stencil_apply(padded, eta_pad, node_drag)
            weight_next = 1.0 / (2.0 * ratio_value - weight_now)
            direction = (weight_next * weight_now) * direction + (2.0 * weight_next / half_width) * (inverse_diag * residual)
            weight_now = weight_next
    return iterate


def reference(forcing, observed, viscosity, friction, ice_mask, dirichlet):
    release = (1 - dirichlet).astype(jnp.float32)
    element_drag = jnp.where(ice_mask == 2, friction, jnp.where(ice_mask == 0, FREE_DRAG, 0.0)).astype(jnp.float32)
    drag_pad = jnp.pad(element_drag, ((1, 0), (1, 0)))
    node_drag = 0.25 * (drag_pad[:-1, :-1] + drag_pad[1:, :-1] + drag_pad[:-1, 1:] + drag_pad[1:, 1:])
    eta_pad = jnp.pad(viscosity, 1)
    inverse_diag = release / (diagonal_terms(eta_pad, node_drag) + 1.0 - release)
    velocity = chebyshev_sweeps(release * forcing, eta_pad, node_drag, inverse_diag)
    misfit = release * (velocity - observed)
    adjoint = chebyshev_sweeps(misfit, eta_pad, node_drag, inverse_diag)
    product = jnp.sum(adjoint * velocity, axis=(0, 1))
    prod_pad = jnp.pad(product, ((0, 1), (0, 1)))
    rows_sum = prod_pad[:-1] + prod_pad[1:]
    total = rows_sum[:, :-1] + rows_sum[:, 1:]
    grounded = (ice_mask == 2).astype(jnp.float32)
    gradient = -0.25 * grounded * total
    return velocity, gradient
```

```python
import jax
import jax.numpy as jnp
from jax import lax
from jax.sharding import PartitionSpec as P

SWEEPS = 3
EPOCHS = 4

UPPER_BOUND = 2.4
LOWER_BOUND = 0.05
FREE_DRAG = 4.0

HALO = 2 * SWEEPS + 2


def extended(shard, axis, dim, width):
    size, length = lax.axis_size(axis), shard.shape[dim]
    up = [(i, i + 1) for i in range(size - 1)]
    down = [(i + 1, i) for i in range(size - 1)]
    last = lax.slice_in_dim(shard, length - width, length, axis=dim)
    initial = lax.slice_in_dim(shard, 0, width, axis=dim)
    before = lax.ppermute(last, axis, up)
    after = lax.ppermute(initial, axis, down)
    return jnp.concatenate([before, shard, after], axis=dim)


def sh(x, di, dj):
    rows, cols = x.shape[-2:]
    pad = [(0, 0)] * (x.ndim - 2) + [(max(-di, 0), max(di, 0)), (max(-dj, 0), max(dj, 0))]
    xp = jnp.pad(x, pad)
    a, b = max(di, 0), max(dj, 0)
    return xp[..., a : a + rows, b : b + cols]


def face_values(eta):
    north = sh(eta, 1, 0)
    south = sh(eta, -1, 0)
    east = sh(eta, 0, 1)
    west = sh(eta, 0, -1)
    return (
        north,
        south,
        east,
        west,
        0.5 * (eta + north),
        0.5 * (eta + south),
        0.5 * (eta + east),
        0.5 * (eta + west),
    )


def stencil_apply(field, faces, node_drag):
    north, south, east, west, face_np, face_sm, face_ep, face_wm = faces
    along_u = field[:, 0]
    along_v = field[:, 1]

    def normal_part(values, weight_rows, weight_cols):
        middle = values
        rows_part = face_np * (sh(values, 1, 0) - middle) - face_sm * (middle - sh(values, -1, 0))
        cols_part = face_ep * (sh(values, 0, 1) - middle) - face_wm * (middle - sh(values, 0, -1))
        return weight_rows * rows_part + weight_cols * cols_part

    def cross_part(values, weight_rows, weight_cols):
        slope_cols = 0.5 * (sh(values, 0, 1) - sh(values, 0, -1))
        slope_rows = 0.5 * (sh(values, 1, 0) - sh(values, -1, 0))
        first = 0.5 * weight_rows * (north * sh(slope_cols, 1, 0) - south * sh(slope_cols, -1, 0))
        second = 0.5 * weight_cols * (east * sh(slope_rows, 0, 1) - west * sh(slope_rows, 0, -1))
        return first + second

    image_u = node_drag * along_u - normal_part(along_u, 4.0, 1.0) - cross_part(along_v, 2.0, 1.0)
    image_v = node_drag * along_v - normal_part(along_v, 1.0, 4.0) - cross_part(along_u, 1.0, 2.0)
    return jnp.stack([image_u, image_v], axis=1)


def diagonal_terms(faces, node_drag):
    north, south, east, west, face_np, face_sm, face_ep, face_wm = faces
    rows_sum = face_np + face_sm
    cols_sum = face_ep + face_wm
    return jnp.stack(
        [4.0 * rows_sum + cols_sum + node_drag, rows_sum + 4.0 * cols_sum + node_drag], axis=0
    )


def chebyshev(rhs, faces, node_drag, inverse_diag):
    centre_value = 0.5 * (UPPER_BOUND + LOWER_BOUND)
    half_width = 0.5 * (UPPER_BOUND - LOWER_BOUND)
    ratio_value = centre_value / half_width
    weight_now = 1.0 / ratio_value
    residual = rhs
    direction = inverse_diag * residual / centre_value
    iterate = jnp.zeros_like(rhs)
    for sweep_no in range(SWEEPS + 1):
        iterate = iterate + direction
        if sweep_no < SWEEPS:
            residual = residual - stencil_apply(direction, faces, node_drag)
            weight_next = 1.0 / (2.0 * ratio_value - weight_now)
            scaled = inverse_diag * residual
            direction = (
                weight_next * weight_now * direction + 2.0 * weight_next / half_width * scaled
            )
            weight_now = weight_next
    return iterate


def body(forcing, observed, viscosity, friction, ice_mask, dirichlet):
    epochs, comps, rows, cols = forcing.shape
    h = HALO
    release = (1 - dirichlet).astype(jnp.float32)
    element_drag = jnp.where(ice_mask == 2, friction, jnp.where(ice_mask == 0, FREE_DRAG, 0.0))
    planes = jnp.concatenate(
        [
            forcing.reshape(epochs * comps, rows, cols),
            observed.reshape(epochs * comps, rows, cols),
            jnp.stack([viscosity, release, element_drag]),
        ]
    )
    planes = extended(planes, "gx", 1, h)
    planes = extended(planes, "gy", 2, h)
    n = epochs * comps
    forcing_x = planes[:n].reshape(epochs, comps, rows + 2 * h, cols + 2 * h)
    observed_x = planes[n : 2 * n].reshape(epochs, comps, rows + 2 * h, cols + 2 * h)
    eta = planes[2 * n]
    free = planes[2 * n + 1]
    drag = planes[2 * n + 2]
    node_drag = 0.25 * (sh(drag, -1, -1) + sh(drag, 0, -1) + sh(drag, -1, 0) + drag)
    faces = face_values(eta)
    inverse_diag = free / (diagonal_terms(faces, node_drag) + 1.0 - free)
    velocity = chebyshev(free * forcing_x, faces, node_drag, inverse_diag)
    misfit = free * (velocity - observed_x)
    adjoint = chebyshev(misfit, faces, node_drag, inverse_diag)
    product = jnp.sum(adjoint * velocity, axis=(0, 1))
    rows_sum = product + sh(product, 1, 0)
    total = rows_sum + sh(rows_sum, 0, 1)
    total = total[h : h + rows, h : h + cols]
    grounded = (ice_mask == 2).astype(jnp.float32)
    gradient = -0.25 * grounded * total
    return (velocity[:, :, h : h + rows, h : h + cols], gradient)


def solution(mesh):
    return jax.shard_map(
        body,
        mesh=mesh,
        in_specs=(
            P(None, None, "gx", "gy"),
            P(None, None, "gx", "gy"),
            P("gx", "gy"),
            P("gx", "gy"),
            P("gx", "gy"),
            P("gx", "gy"),
        ),
        out_specs=(P(None, None, "gx", "gy"), P("gx", "gy")),
        check_vma=False,
    )
```

```python
import functools

import jax
import jax.numpy as jnp
from jax import lax
from jax.experimental import pallas as pl
from jax.experimental.pallas import tpu as pltpu
from jax.sharding import PartitionSpec as P

SWEEPS = 3

UPPER_BOUND = 2.4
LOWER_BOUND = 0.05
FREE_DRAG = 4.0

HALO = 2 * SWEEPS + 2


def exchange(slab_low, slab_high, axis):
    size = lax.axis_size(axis)
    up = [(i, i + 1) for i in range(size - 1)]
    down = [(i + 1, i) for i in range(size - 1)]
    after = lax.ppermute(slab_low, axis, down)
    before = lax.ppermute(slab_high, axis, up)
    return after, before


def sh(x, di, dj):
    if di:
        x = pltpu.roll(x, (-di) % x.shape[0], 0)
    if dj:
        x = pltpu.roll(x, (-dj) % x.shape[1], 1)
    return x


def stencil_pair(u, v, c):
    north, south, east, west, face_np, face_sm, face_ep, face_wm, node_drag = c

    def normal_part(values, weight_rows, weight_cols):
        middle = values
        rows_part = face_np * (sh(values, 1, 0) - middle) - face_sm * (middle - sh(values, -1, 0))
        cols_part = face_ep * (sh(values, 0, 1) - middle) - face_wm * (middle - sh(values, 0, -1))
        return weight_rows * rows_part + weight_cols * cols_part

    def cross_part(values, weight_rows, weight_cols):
        slope_cols = 0.5 * (sh(values, 0, 1) - sh(values, 0, -1))
        slope_rows = 0.5 * (sh(values, 1, 0) - sh(values, -1, 0))
        first = 0.5 * weight_rows * (north * sh(slope_cols, 1, 0) - south * sh(slope_cols, -1, 0))
        second = 0.5 * weight_cols * (east * sh(slope_rows, 0, 1) - west * sh(slope_rows, 0, -1))
        return first + second

    image_u = node_drag * u - normal_part(u, 4.0, 1.0) - cross_part(v, 2.0, 1.0)
    image_v = node_drag * v - normal_part(v, 1.0, 4.0) - cross_part(u, 1.0, 2.0)
    return image_u, image_v


def chebyshev_pair(rhs_u, rhs_v, c, inv_u, inv_v):
    centre_value = 0.5 * (UPPER_BOUND + LOWER_BOUND)
    half_width = 0.5 * (UPPER_BOUND - LOWER_BOUND)
    ratio_value = centre_value / half_width
    weight_now = 1.0 / ratio_value
    res_u, res_v = rhs_u, rhs_v
    dir_u = inv_u * res_u / centre_value
    dir_v = inv_v * res_v / centre_value
    it_u = jnp.zeros_like(rhs_u)
    it_v = jnp.zeros_like(rhs_v)
    for sweep_no in range(SWEEPS + 1):
        it_u = it_u + dir_u
        it_v = it_v + dir_v
        if sweep_no < SWEEPS:
            img_u, img_v = stencil_pair(dir_u, dir_v, c)
            res_u = res_u - img_u
            res_v = res_v - img_v
            weight_next = 1.0 / (2.0 * ratio_value - weight_now)
            a = weight_next * weight_now
            b = 2.0 * weight_next / half_width
            dir_u = a * dir_u + b * (inv_u * res_u)
            dir_v = a * dir_v + b * (inv_v * res_v)
            weight_now = weight_next
    return it_u, it_v


def kernel(
    f_ref, o_ref, eta_ref, free_ref, drag_ref, ice_ref, ra_ref, rb_ref, cx_ref,
    vel_ref, grad_ref,
    field_ref, coef_ref, prod_ref,
):
    epochs, comps, rows, cols = f_ref.shape
    h = HALO
    n = epochs * comps

    def assemble(dst, centre, p):
        dst[0:rows, 0:cols] = centre
        dst[rows : rows + h, 0:cols] = ra_ref[p]
        dst[rows + h : rows + 2 * h, 0:cols] = rb_ref[p]
        dst[:, cols:] = cx_ref[p]

    assemble(field_ref.at[0], eta_ref[...], 2 * n)
    assemble(field_ref.at[1], free_ref[...], 2 * n + 1)
    assemble(field_ref.at[2], drag_ref[...], 2 * n + 2)
    eta = field_ref[0]
    free = field_ref[1]
    drag = field_ref[2]
    node_drag = 0.25 * (sh(drag, -1, -1) + sh(drag, 0, -1) + sh(drag, -1, 0) + drag)
    north = sh(eta, 1, 0)
    south = sh(eta, -1, 0)
    east = sh(eta, 0, 1)
    west = sh(eta, 0, -1)
    face_np = 0.5 * (eta + north)
    face_sm = 0.5 * (eta + south)
    face_ep = 0.5 * (eta + east)
    face_wm = 0.5 * (eta + west)
    rows_sum = face_np + face_sm
    cols_sum = face_ep + face_wm
    inv_u = free / (4.0 * rows_sum + cols_sum + node_drag + 1.0 - free)
    inv_v = free / (rows_sum + 4.0 * cols_sum + node_drag + 1.0 - free)
    for k, val in enumerate(
        [north, south, east, west, face_np, face_sm, face_ep, face_wm, node_drag, inv_u, inv_v, free]
    ):
        coef_ref[k] = val
    prod_ref[...] = jnp.zeros_like(prod_ref)

    def epoch(e, carry):
        for comp in range(comps):
            p = e * comps + comp
            assemble(field_ref.at[3 + comp], f_ref[e, comp], p)
            assemble(field_ref.at[3 + comps + comp], o_ref[e, comp], n + p)
        c = tuple(coef_ref[k] for k in range(9))
        inv_u = coef_ref[9]
        inv_v = coef_ref[10]
        free = coef_ref[11]
        vel_u, vel_v = chebyshev_pair(free * field_ref[3], free * field_ref[4], c, inv_u, inv_v)
        vel_ref[e, 0] = vel_u[0:rows, 0:cols]
        vel_ref[e, 1] = vel_v[0:rows, 0:cols]
        mis_u = free * (vel_u - field_ref[5])
        mis_v = free * (vel_v - field_ref[6])
        adj_u, adj_v = chebyshev_pair(mis_u, mis_v, c, inv_u, inv_v)
        prod_ref[...] += adj_u * vel_u + adj_v * vel_v
        return carry

    lax.fori_loop(0, epochs, epoch, 0)
    product = prod_ref[...]
    rows_sum = product + sh(product, 1, 0)
    total = rows_sum + sh(rows_sum, 0, 1)
    grounded = (ice_ref[...] == 2).astype(jnp.float32)
    grad_ref[...] = -0.25 * grounded * total[0:rows, 0:cols]


def local_solve(forcing, observed, eta, free, drag, ice_mask, ra, rb, cx):
    epochs, comps, rows, cols = forcing.shape
    full = (rows + 2 * HALO, 2 * cols)
    vmem = pl.BlockSpec(memory_space=pltpu.VMEM)
    nodes = full[0] * full[1]
    return pl.pallas_call(
        kernel,
        out_shape=(
            jax.ShapeDtypeStruct(forcing.shape, jnp.float32),
            jax.ShapeDtypeStruct((rows, cols), jnp.float32),
        ),
        in_specs=[vmem] * 9,
        out_specs=(vmem, vmem),
        scratch_shapes=[
            pltpu.VMEM((3 + 2 * comps,) + full, jnp.float32),
            pltpu.VMEM((12,) + full, jnp.float32),
            pltpu.VMEM(full, jnp.float32),
        ],
        cost_estimate=pl.CostEstimate(
            flops=epochs * 2 * SWEEPS * comps * 60 * nodes,
            bytes_accessed=4 * (3 * epochs * comps + 40) * rows * cols,
            transcendentals=0,
        ),
    )(forcing, observed, eta, free, drag, ice_mask, ra, rb, cx)


def body(forcing, observed, viscosity, friction, ice_mask, dirichlet):
    epochs, comps, rows, cols = forcing.shape
    h = HALO
    n = epochs * comps
    release = (1 - dirichlet).astype(jnp.float32)
    element_drag = jnp.where(ice_mask == 2, friction, jnp.where(ice_mask == 0, FREE_DRAG, 0.0))

    def rows_of(lo, hi):
        return jnp.concatenate(
            [
                forcing[:, :, lo:hi].reshape(n, hi - lo, cols),
                observed[:, :, lo:hi].reshape(n, hi - lo, cols),
                jnp.stack([viscosity[lo:hi], release[lo:hi], element_drag[lo:hi]]),
            ]
        )

    ra, rb = exchange(rows_of(0, h), rows_of(rows - h, rows), "gx")

    def cols_of(lo, hi):
        centre = rows_of(0, rows)[:, :, lo:hi]
        return jnp.concatenate([centre, ra[:, :, lo:hi], rb[:, :, lo:hi]], axis=1)

    ca, cb = exchange(cols_of(0, h), cols_of(cols - h, cols), "gy")
    gap = jnp.zeros((ca.shape[0], ca.shape[1], cols - 2 * h), jnp.float32)
    cx = jnp.concatenate([ca, gap, cb], axis=2)
    return local_solve(forcing, observed, viscosity, release, element_drag, ice_mask, ra, rb, cx)


def solution(mesh):
    return jax.shard_map(
        body,
        mesh=mesh,
        in_specs=(
            P(None, None, "gx", "gy"),
            P(None, None, "gx", "gy"),
            P("gx", "gy"),
            P("gx", "gy"),
            P("gx", "gy"),
            P("gx", "gy"),
        ),
        out_specs=(P(None, None, "gx", "gy"), P("gx", "gy")),
        check_vma=False,
    )
```

```python
import functools

import jax
import jax.numpy as jnp
from jax import lax
from jax.experimental import pallas as pl
from jax.experimental.pallas import tpu as pltpu
from jax.sharding import PartitionSpec as P

SWEEPS = 3

UPPER_BOUND = 2.4
LOWER_BOUND = 0.05
FREE_DRAG = 4.0

HALO = 2 * SWEEPS + 2


def exchange(slab_low, slab_high, axis):
    size = lax.axis_size(axis)
    up = [(i, i + 1) for i in range(size - 1)]
    down = [(i + 1, i) for i in range(size - 1)]
    after = lax.ppermute(slab_low, axis, down)
    before = lax.ppermute(slab_high, axis, up)
    return after, before


def sh(x, di, dj):
    if di:
        x = pltpu.roll(x, (-di) % x.shape[0], 0)
    if dj:
        x = pltpu.roll(x, (-dj) % x.shape[1], 1)
    return x


def stencil_pair(u, v, c):
    north, south, east, west, face_np, face_sm, face_ep, face_wm, node_drag = c

    def normal_part(values, weight_rows, weight_cols):
        middle = values
        rows_part = face_np * (sh(values, 1, 0) - middle) - face_sm * (middle - sh(values, -1, 0))
        cols_part = face_ep * (sh(values, 0, 1) - middle) - face_wm * (middle - sh(values, 0, -1))
        return weight_rows * rows_part + weight_cols * cols_part

    def cross_part(values, weight_rows, weight_cols):
        slope_cols = 0.5 * (sh(values, 0, 1) - sh(values, 0, -1))
        slope_rows = 0.5 * (sh(values, 1, 0) - sh(values, -1, 0))
        first = 0.5 * weight_rows * (north * sh(slope_cols, 1, 0) - south * sh(slope_cols, -1, 0))
        second = 0.5 * weight_cols * (east * sh(slope_rows, 0, 1) - west * sh(slope_rows, 0, -1))
        return first + second

    image_u = node_drag * u - normal_part(u, 4.0, 1.0) - cross_part(v, 2.0, 1.0)
    image_v = node_drag * v - normal_part(v, 1.0, 4.0) - cross_part(u, 1.0, 2.0)
    return image_u, image_v


def chebyshev_pair(rhs_u, rhs_v, c, inv_u, inv_v):
    centre_value = 0.5 * (UPPER_BOUND + LOWER_BOUND)
    half_width = 0.5 * (UPPER_BOUND - LOWER_BOUND)
    ratio_value = centre_value / half_width
    weight_now = 1.0 / ratio_value
    res_u, res_v = rhs_u, rhs_v
    dir_u = inv_u * res_u / centre_value
    dir_v = inv_v * res_v / centre_value
    it_u = jnp.zeros_like(rhs_u)
    it_v = jnp.zeros_like(rhs_v)
    for sweep_no in range(SWEEPS + 1):
        it_u = it_u + dir_u
        it_v = it_v + dir_v
        if sweep_no < SWEEPS:
            img_u, img_v = stencil_pair(dir_u, dir_v, c)
            res_u = res_u - img_u
            res_v = res_v - img_v
            weight_next = 1.0 / (2.0 * ratio_value - weight_now)
            a = weight_next * weight_now
            b = 2.0 * weight_next / half_width
            dir_u = a * dir_u + b * (inv_u * res_u)
            dir_v = a * dir_v + b * (inv_v * res_v)
            weight_now = weight_next
    return it_u, it_v


def kernel(
    f_ref, o_ref, eta_ref, free_ref, drag_ref, ice_ref, ra_ref, rb_ref, cx_ref,
    vel_ref, grad_ref,
    field_ref, coef_ref, prod_ref,
):
    epochs, comps, rows, cols = f_ref.shape
    h = HALO
    n = epochs * comps

    def assemble(dst, centre, p):
        dst[0:rows, 0:cols] = centre
        dst[rows : rows + h, 0:cols] = ra_ref[p]
        dst[rows + h : rows + 2 * h, 0:cols] = rb_ref[p]
        dst[:, cols:] = cx_ref[p]

    assemble(field_ref.at[0], eta_ref[...], 2 * n)
    assemble(field_ref.at[1], free_ref[...], 2 * n + 1)
    assemble(field_ref.at[2], drag_ref[...], 2 * n + 2)
    eta = field_ref[0]
    free = field_ref[1]
    drag = field_ref[2]
    node_drag = 0.25 * (sh(drag, -1, -1) + sh(drag, 0, -1) + sh(drag, -1, 0) + drag)
    north = sh(eta, 1, 0)
    south = sh(eta, -1, 0)
    east = sh(eta, 0, 1)
    west = sh(eta, 0, -1)
    face_np = 0.5 * (eta + north)
    face_sm = 0.5 * (eta + south)
    face_ep = 0.5 * (eta + east)
    face_wm = 0.5 * (eta + west)
    rows_sum = face_np + face_sm
    cols_sum = face_ep + face_wm
    inv_u = free / (4.0 * rows_sum + cols_sum + node_drag + 1.0 - free)
    inv_v = free / (rows_sum + 4.0 * cols_sum + node_drag + 1.0 - free)
    for k, val in enumerate(
        [north, south, east, west, face_np, face_sm, face_ep, face_wm, node_drag, inv_u, inv_v, free]
    ):
        coef_ref[k] = val
    prod_ref[...] = jnp.zeros_like(prod_ref)

    def epoch(e, carry):
        for comp in range(comps):
            p = e * comps + comp
            assemble(field_ref.at[3 + comp], f_ref[e, comp], p)
            assemble(field_ref.at[3 + comps + comp], o_ref[e, comp], n + p)
        c = tuple(coef_ref[k] for k in range(9))
        inv_u = coef_ref[9]
        inv_v = coef_ref[10]
        free = coef_ref[11]
        vel_u, vel_v = chebyshev_pair(free * field_ref[3], free * field_ref[4], c, inv_u, inv_v)
        vel_ref[e, 0] = vel_u[0:rows, 0:cols]
        vel_ref[e, 1] = vel_v[0:rows, 0:cols]
        mis_u = free * (vel_u - field_ref[5])
        mis_v = free * (vel_v - field_ref[6])
        adj_u, adj_v = chebyshev_pair(mis_u, mis_v, c, inv_u, inv_v)
        prod_ref[...] += adj_u * vel_u + adj_v * vel_v
        return carry

    lax.fori_loop(0, epochs, epoch, 0)
    product = prod_ref[...]
    rows_sum = product + sh(product, 1, 0)
    total = rows_sum + sh(rows_sum, 0, 1)
    grounded = (ice_ref[...] == 2).astype(jnp.float32)
    grad_ref[...] = -0.25 * grounded * total[0:rows, 0:cols]


def local_solve(forcing, observed, eta, free, drag, ice_mask, ra, rb, cx):
    epochs, comps, rows, cols = forcing.shape
    full = (rows + 2 * HALO, 2 * cols)
    vmem = pl.BlockSpec(memory_space=pltpu.VMEM)
    nodes = full[0] * full[1]
    return pl.pallas_call(
        kernel,
        out_shape=(
            jax.ShapeDtypeStruct(forcing.shape, jnp.float32),
            jax.ShapeDtypeStruct((rows, cols), jnp.float32),
        ),
        in_specs=[vmem] * 9,
        out_specs=(vmem, vmem),
        scratch_shapes=[
            pltpu.VMEM((3 + 2 * comps,) + full, jnp.float32),
            pltpu.VMEM((12,) + full, jnp.float32),
            pltpu.VMEM(full, jnp.float32),
        ],
        cost_estimate=pl.CostEstimate(
            flops=epochs * 2 * SWEEPS * comps * 60 * nodes,
            bytes_accessed=4 * (3 * epochs * comps + 40) * rows * cols,
            transcendentals=0,
        ),
    )(forcing, observed, eta, free, drag, ice_mask, ra, rb, cx)


def body(forcing, observed, viscosity, friction, ice_mask, dirichlet):
    epochs, comps, rows, cols = forcing.shape
    h = HALO
    n = epochs * comps
    release = (1 - dirichlet).astype(jnp.float32)
    element_drag = jnp.where(ice_mask == 2, friction, jnp.where(ice_mask == 0, FREE_DRAG, 0.0))
    size_x, size_y = lax.axis_size("gx"), lax.axis_size("gy")

    def piece(di, dj):
        r = (0, h) if di < 0 else ((rows - h, rows) if di > 0 else (0, rows))
        c = (0, h) if dj < 0 else ((cols - h, cols) if dj > 0 else (0, cols))
        return jnp.concatenate(
            [
                forcing[:, :, r[0] : r[1], c[0] : c[1]].reshape(n, r[1] - r[0], c[1] - c[0]),
                observed[:, :, r[0] : r[1], c[0] : c[1]].reshape(n, r[1] - r[0], c[1] - c[0]),
                jnp.stack(
                    [
                        viscosity[r[0] : r[1], c[0] : c[1]],
                        release[r[0] : r[1], c[0] : c[1]],
                        element_drag[r[0] : r[1], c[0] : c[1]],
                    ]
                ),
            ]
        )

    def recv(di, dj):
        pairs = []
        for a in range(size_x):
            for b in range(size_y):
                ta, tb = a + di, b + dj
                if 0 <= ta < size_x and 0 <= tb < size_y:
                    pairs.append((a * size_y + b, ta * size_y + tb))
        return lax.ppermute(piece(di, dj), ("gx", "gy"), pairs)

    got = {(di, dj): recv(di, dj) for di in (-1, 0, 1) for dj in (-1, 0, 1) if di or dj}
    ra, rb = got[(-1, 0)], got[(1, 0)]
    col_after = jnp.concatenate([got[(0, -1)], got[(-1, -1)], got[(1, -1)]], axis=1)
    col_before = jnp.concatenate([got[(0, 1)], got[(-1, 1)], got[(1, 1)]], axis=1)
    gap = jnp.zeros((col_after.shape[0], col_after.shape[1], cols - 2 * h), jnp.float32)
    cx = jnp.concatenate([col_after, gap, col_before], axis=2)
    return local_solve(forcing, observed, viscosity, release, element_drag, ice_mask, ra, rb, cx)


def solution(mesh):
    return jax.shard_map(
        body,
        mesh=mesh,
        in_specs=(
            P(None, None, "gx", "gy"),
            P(None, None, "gx", "gy"),
            P("gx", "gy"),
            P("gx", "gy"),
            P("gx", "gy"),
            P("gx", "gy"),
        ),
        out_specs=(P(None, None, "gx", "gy"), P("gx", "gy")),
        check_vma=False,
    )
```

```python
import functools

import jax
import jax.numpy as jnp
from jax import lax
from jax.experimental import pallas as pl
from jax.experimental.pallas import tpu as pltpu
from jax.sharding import PartitionSpec as P

SWEEPS = 3

UPPER_BOUND = 2.4
LOWER_BOUND = 0.05
FREE_DRAG = 4.0

HALO = 2 * SWEEPS + 2


def exchange(slab_low, slab_high, axis):
    size = lax.axis_size(axis)
    up = [(i, i + 1) for i in range(size - 1)]
    down = [(i + 1, i) for i in range(size - 1)]
    after = lax.ppermute(slab_low, axis, down)
    before = lax.ppermute(slab_high, axis, up)
    return after, before


def sh(x, di, dj):
    if di:
        x = pltpu.roll(x, (-di) % x.shape[0], 0)
    if dj:
        x = pltpu.roll(x, (-dj) % x.shape[1], 1)
    return x


def stencil_pair(u, v, c):
    north, south, east, west, face_np, face_sm, face_ep, face_wm, node_drag = c

    def normal_part(values, weight_rows, weight_cols):
        middle = values
        rows_part = face_np * (sh(values, 1, 0) - middle) - face_sm * (middle - sh(values, -1, 0))
        cols_part = face_ep * (sh(values, 0, 1) - middle) - face_wm * (middle - sh(values, 0, -1))
        return weight_rows * rows_part + weight_cols * cols_part

    def cross_part(values, weight_rows, weight_cols):
        slope_cols = 0.5 * (sh(values, 0, 1) - sh(values, 0, -1))
        slope_rows = 0.5 * (sh(values, 1, 0) - sh(values, -1, 0))
        first = 0.5 * weight_rows * (north * sh(slope_cols, 1, 0) - south * sh(slope_cols, -1, 0))
        second = 0.5 * weight_cols * (east * sh(slope_rows, 0, 1) - west * sh(slope_rows, 0, -1))
        return first + second

    image_u = node_drag * u - normal_part(u, 4.0, 1.0) - cross_part(v, 2.0, 1.0)
    image_v = node_drag * v - normal_part(v, 1.0, 4.0) - cross_part(u, 1.0, 2.0)
    return image_u, image_v


def chebyshev_pair(rhs_u, rhs_v, c, inv_u, inv_v):
    centre_value = 0.5 * (UPPER_BOUND + LOWER_BOUND)
    half_width = 0.5 * (UPPER_BOUND - LOWER_BOUND)
    ratio_value = centre_value / half_width
    weight_now = 1.0 / ratio_value
    res_u, res_v = rhs_u, rhs_v
    dir_u = inv_u * res_u / centre_value
    dir_v = inv_v * res_v / centre_value
    it_u = jnp.zeros_like(rhs_u)
    it_v = jnp.zeros_like(rhs_v)
    for sweep_no in range(SWEEPS + 1):
        it_u = it_u + dir_u
        it_v = it_v + dir_v
        if sweep_no < SWEEPS:
            img_u, img_v = stencil_pair(dir_u, dir_v, c)
            res_u = res_u - img_u
            res_v = res_v - img_v
            weight_next = 1.0 / (2.0 * ratio_value - weight_now)
            a = weight_next * weight_now
            b = 2.0 * weight_next / half_width
            dir_u = a * dir_u + b * (inv_u * res_u)
            dir_v = a * dir_v + b * (inv_v * res_v)
            weight_now = weight_next
    return it_u, it_v


def kernel(
    f_ref, o_ref, eta_ref, fd_ref, ice_ref, ra_ref, rb_ref, ca_ref, cb_ref,
    vel_ref, grad_ref,
    field_ref, coef_ref, prod_ref,
):
    epochs, comps, rows, cols = f_ref.shape
    h = HALO
    n = epochs * comps

    def assemble(dst, centre, p):
        dst[0:rows, 0:cols] = centre
        dst[rows : rows + h, 0:cols] = ra_ref[p]
        dst[rows + h : rows + 2 * h, 0:cols] = rb_ref[p]
        dst[:, cols : cols + h] = ca_ref[p]
        dst[:, 2 * cols - h :] = cb_ref[p]

    for k in range(field_ref.shape[0]):
        field_ref[k, :, cols + h : 2 * cols - h] = jnp.zeros((rows + 2 * h, cols - 2 * h), jnp.float32)
    assemble(field_ref.at[0], eta_ref[...], 2 * n)
    assemble(field_ref.at[1], fd_ref[0], 2 * n + 1)
    assemble(field_ref.at[2], fd_ref[1], 2 * n + 2)
    eta = field_ref[0]
    free = field_ref[1]
    drag = field_ref[2]
    node_drag = 0.25 * (sh(drag, -1, -1) + sh(drag, 0, -1) + sh(drag, -1, 0) + drag)
    north = sh(eta, 1, 0)
    south = sh(eta, -1, 0)
    east = sh(eta, 0, 1)
    west = sh(eta, 0, -1)
    face_np = 0.5 * (eta + north)
    face_sm = 0.5 * (eta + south)
    face_ep = 0.5 * (eta + east)
    face_wm = 0.5 * (eta + west)
    rows_sum = face_np + face_sm
    cols_sum = face_ep + face_wm
    inv_u = free / (4.0 * rows_sum + cols_sum + node_drag + 1.0 - free)
    inv_v = free / (rows_sum + 4.0 * cols_sum + node_drag + 1.0 - free)
    for k, val in enumerate(
        [north, south, east, west, face_np, face_sm, face_ep, face_wm, node_drag, inv_u, inv_v, free]
    ):
        coef_ref[k] = val
    prod_ref[...] = jnp.zeros_like(prod_ref)

    def epoch(e, carry):
        for comp in range(comps):
            p = e * comps + comp
            assemble(field_ref.at[3 + comp], f_ref[e, comp], p)
            assemble(field_ref.at[3 + comps + comp], o_ref[e, comp], n + p)
        c = tuple(coef_ref[k] for k in range(9))
        inv_u = coef_ref[9]
        inv_v = coef_ref[10]
        free = coef_ref[11]
        vel_u, vel_v = chebyshev_pair(free * field_ref[3], free * field_ref[4], c, inv_u, inv_v)
        vel_ref[e, 0] = vel_u[0:rows, 0:cols]
        vel_ref[e, 1] = vel_v[0:rows, 0:cols]
        mis_u = free * (vel_u - field_ref[5])
        mis_v = free * (vel_v - field_ref[6])
        adj_u, adj_v = chebyshev_pair(mis_u, mis_v, c, inv_u, inv_v)
        prod_ref[...] += adj_u * vel_u + adj_v * vel_v
        return carry

    lax.fori_loop(0, epochs, epoch, 0)
    product = prod_ref[...]
    rows_sum = product + sh(product, 1, 0)
    total = rows_sum + sh(rows_sum, 0, 1)
    grounded = (ice_ref[...] == 2).astype(jnp.float32)
    grad_ref[...] = -0.25 * grounded * total[0:rows, 0:cols]


def prep_kernel(f_ref, o_ref, eta_ref, fric_ref, ice_ref, dir_ref, lo_ref, hi_ref, fd_ref):
    epochs, comps, rows, cols = f_ref.shape
    h = HALO
    n = epochs * comps
    ice = ice_ref[...]
    free = (1 - dir_ref[...]).astype(jnp.float32)
    drag = jnp.where(ice == 2, fric_ref[...], jnp.where(ice == 0, FREE_DRAG, 0.0))
    fd_ref[0] = free
    fd_ref[1] = drag
    for e in range(epochs):
        for comp in range(comps):
            p = e * comps + comp
            lo_ref[p] = f_ref[e, comp, 0:h, :]
            hi_ref[p] = f_ref[e, comp, rows - h : rows, :]
            lo_ref[n + p] = o_ref[e, comp, 0:h, :]
            hi_ref[n + p] = o_ref[e, comp, rows - h : rows, :]
    for k, val in enumerate([eta_ref[...], free, drag]):
        lo_ref[2 * n + k] = val[0:h]
        hi_ref[2 * n + k] = val[rows - h : rows]


def prep(forcing, observed, viscosity, friction, ice_mask, dirichlet):
    epochs, comps, rows, cols = forcing.shape
    planes = 2 * epochs * comps + 3
    vmem = pl.BlockSpec(memory_space=pltpu.VMEM)
    slab = jax.ShapeDtypeStruct((planes, HALO, cols), jnp.float32)
    return pl.pallas_call(
        prep_kernel,
        out_shape=(slab, slab, jax.ShapeDtypeStruct((2, rows, cols), jnp.float32)),
        in_specs=[vmem] * 6,
        out_specs=(vmem, vmem, vmem),
    )(forcing, observed, viscosity, friction, ice_mask, dirichlet)


def local_solve(forcing, observed, eta, fd, ice_mask, ra, rb, ca, cb):
    epochs, comps, rows, cols = forcing.shape
    full = (rows + 2 * HALO, 2 * cols)
    vmem = pl.BlockSpec(memory_space=pltpu.VMEM)
    nodes = full[0] * full[1]
    return pl.pallas_call(
        kernel,
        out_shape=(
            jax.ShapeDtypeStruct(forcing.shape, jnp.float32),
            jax.ShapeDtypeStruct((rows, cols), jnp.float32),
        ),
        in_specs=[vmem] * 9,
        out_specs=(vmem, vmem),
        scratch_shapes=[
            pltpu.VMEM((3 + 2 * comps,) + full, jnp.float32),
            pltpu.VMEM((12,) + full, jnp.float32),
            pltpu.VMEM(full, jnp.float32),
        ],
        cost_estimate=pl.CostEstimate(
            flops=epochs * 2 * SWEEPS * comps * 60 * nodes,
            bytes_accessed=4 * (3 * epochs * comps + 40) * rows * cols,
            transcendentals=0,
        ),
    )(forcing, observed, eta, fd, ice_mask, ra, rb, ca, cb)


def body(forcing, observed, viscosity, friction, ice_mask, dirichlet):
    epochs, comps, rows, cols = forcing.shape
    h = HALO
    n = epochs * comps
    lo, hi, fd = prep(forcing, observed, viscosity, friction, ice_mask, dirichlet)
    ra, rb = exchange(lo, hi, "gx")

    def cols_of(a, b):
        centre = jnp.concatenate(
            [
                forcing[:, :, :, a:b].reshape(n, rows, b - a),
                observed[:, :, :, a:b].reshape(n, rows, b - a),
                viscosity[None, :, a:b],
                fd[:, :, a:b],
            ]
        )
        return jnp.concatenate([centre, ra[:, :, a:b], rb[:, :, a:b]], axis=1)

    ca, cb = exchange(cols_of(0, h), cols_of(cols - h, cols), "gy")
    return local_solve(forcing, observed, viscosity, fd, ice_mask, ra, rb, ca, cb)


def solution(mesh):
    return jax.shard_map(
        body,
        mesh=mesh,
        in_specs=(
            P(None, None, "gx", "gy"),
            P(None, None, "gx", "gy"),
            P("gx", "gy"),
            P("gx", "gy"),
            P("gx", "gy"),
            P("gx", "gy"),
        ),
        out_specs=(P(None, None, "gx", "gy"), P("gx", "gy")),
        check_vma=False,
    )
```

```python
import functools

import jax
import jax.numpy as jnp
from jax import lax
from jax.experimental import pallas as pl
from jax.experimental.pallas import tpu as pltpu
from jax.sharding import PartitionSpec as P

SWEEPS = 3

UPPER_BOUND = 2.4
LOWER_BOUND = 0.05
FREE_DRAG = 4.0

HALO = 2 * SWEEPS + 2


def exchange(slab_low, slab_high, axis):
    size = lax.axis_size(axis)
    up = [(i, i + 1) for i in range(size - 1)]
    down = [(i + 1, i) for i in range(size - 1)]
    after = lax.ppermute(slab_low, axis, down)
    before = lax.ppermute(slab_high, axis, up)
    return after, before


def sh(x, di, dj):
    if di:
        x = pltpu.roll(x, (-di) % x.shape[0], 0)
    if dj:
        x = pltpu.roll(x, (-dj) % x.shape[1], 1)
    return x


def stencil_pair(u, v, c):
    north, south, east, west, face_np, face_sm, face_ep, face_wm, node_drag = c

    def normal_part(values, weight_rows, weight_cols):
        middle = values
        rows_part = face_np * (sh(values, 1, 0) - middle) - face_sm * (middle - sh(values, -1, 0))
        cols_part = face_ep * (sh(values, 0, 1) - middle) - face_wm * (middle - sh(values, 0, -1))
        return weight_rows * rows_part + weight_cols * cols_part

    def cross_part(values, weight_rows, weight_cols):
        slope_cols = 0.5 * (sh(values, 0, 1) - sh(values, 0, -1))
        slope_rows = 0.5 * (sh(values, 1, 0) - sh(values, -1, 0))
        first = 0.5 * weight_rows * (north * sh(slope_cols, 1, 0) - south * sh(slope_cols, -1, 0))
        second = 0.5 * weight_cols * (east * sh(slope_rows, 0, 1) - west * sh(slope_rows, 0, -1))
        return first + second

    image_u = node_drag * u - normal_part(u, 4.0, 1.0) - cross_part(v, 2.0, 1.0)
    image_v = node_drag * v - normal_part(v, 1.0, 4.0) - cross_part(u, 1.0, 2.0)
    return image_u, image_v


def chebyshev_pair(rhs_u, rhs_v, c, inv_u, inv_v):
    centre_value = 0.5 * (UPPER_BOUND + LOWER_BOUND)
    half_width = 0.5 * (UPPER_BOUND - LOWER_BOUND)
    ratio_value = centre_value / half_width
    weight_now = 1.0 / ratio_value
    res_u, res_v = rhs_u, rhs_v
    dir_u = inv_u * res_u / centre_value
    dir_v = inv_v * res_v / centre_value
    it_u = jnp.zeros_like(rhs_u)
    it_v = jnp.zeros_like(rhs_v)
    for sweep_no in range(SWEEPS + 1):
        it_u = it_u + dir_u
        it_v = it_v + dir_v
        if sweep_no < SWEEPS:
            img_u, img_v = stencil_pair(dir_u, dir_v, c)
            res_u = res_u - img_u
            res_v = res_v - img_v
            weight_next = 1.0 / (2.0 * ratio_value - weight_now)
            a = weight_next * weight_now
            b = 2.0 * weight_next / half_width
            dir_u = a * dir_u + b * (inv_u * res_u)
            dir_v = a * dir_v + b * (inv_v * res_v)
            weight_now = weight_next
    return it_u, it_v


def copy_in(pairs, sem):
    copies = [pltpu.make_async_copy(src, dst, sem.at[i]) for i, (src, dst) in enumerate(pairs)]
    for c in copies:
        c.start()
    return copies


def kernel(
    f_hbm, o_hbm, eta_hbm, fd_hbm, ice_hbm, ra_hbm, rb_hbm, ca_hbm, cb_hbm,
    vel_ref, grad_ref,
    f_ref, o_ref, eta_ref, fd_ref, ice_ref, ra_ref, rb_ref, ca_ref, cb_ref,
    field_ref, coef_ref, prod_ref, sem,
):
    epochs, comps, rows, cols = f_ref.shape
    h = HALO
    n = epochs * comps
    copies = copy_in(
        [
            (eta_hbm, eta_ref), (fd_hbm, fd_ref), (ra_hbm, ra_ref), (rb_hbm, rb_ref),
            (ca_hbm, ca_ref), (cb_hbm, cb_ref), (f_hbm, f_ref), (o_hbm, o_ref), (ice_hbm, ice_ref),
        ],
        sem,
    )
    for k in range(field_ref.shape[0]):
        field_ref[k, :, cols + h : 2 * cols - h] = jnp.zeros((rows + 2 * h, cols - 2 * h), jnp.float32)
    for c in copies[:6]:
        c.wait()

    def assemble(dst, centre, p):
        dst[0:rows, 0:cols] = centre
        dst[rows : rows + h, 0:cols] = ra_ref[p]
        dst[rows + h : rows + 2 * h, 0:cols] = rb_ref[p]
        dst[:, cols : cols + h] = ca_ref[p].T[0 : rows + 2 * h, :]
        dst[:, 2 * cols - h :] = cb_ref[p].T[0 : rows + 2 * h, :]

    assemble(field_ref.at[0], eta_ref[...], 2 * n)
    assemble(field_ref.at[1], fd_ref[0], 2 * n + 1)
    assemble(field_ref.at[2], fd_ref[1], 2 * n + 2)
    eta = field_ref[0]
    free = field_ref[1]
    drag = field_ref[2]
    node_drag = 0.25 * (sh(drag, -1, -1) + sh(drag, 0, -1) + sh(drag, -1, 0) + drag)
    north = sh(eta, 1, 0)
    south = sh(eta, -1, 0)
    east = sh(eta, 0, 1)
    west = sh(eta, 0, -1)
    face_np = 0.5 * (eta + north)
    face_sm = 0.5 * (eta + south)
    face_ep = 0.5 * (eta + east)
    face_wm = 0.5 * (eta + west)
    rows_sum = face_np + face_sm
    cols_sum = face_ep + face_wm
    inv_u = free / (4.0 * rows_sum + cols_sum + node_drag + 1.0 - free)
    inv_v = free / (rows_sum + 4.0 * cols_sum + node_drag + 1.0 - free)
    for k, val in enumerate(
        [north, south, east, west, face_np, face_sm, face_ep, face_wm, node_drag, inv_u, inv_v, free]
    ):
        coef_ref[k] = val
    prod_ref[...] = jnp.zeros_like(prod_ref)
    for c in copies[6:]:
        c.wait()

    def epoch(e, carry):
        for comp in range(comps):
            p = e * comps + comp
            assemble(field_ref.at[3 + comp], f_ref[e, comp], p)
            assemble(field_ref.at[3 + comps + comp], o_ref[e, comp], n + p)
        c = tuple(coef_ref[k] for k in range(9))
        inv_u = coef_ref[9]
        inv_v = coef_ref[10]
        free = coef_ref[11]
        vel_u, vel_v = chebyshev_pair(free * field_ref[3], free * field_ref[4], c, inv_u, inv_v)
        vel_ref[e, 0] = vel_u[0:rows, 0:cols]
        vel_ref[e, 1] = vel_v[0:rows, 0:cols]
        mis_u = free * (vel_u - field_ref[5])
        mis_v = free * (vel_v - field_ref[6])
        adj_u, adj_v = chebyshev_pair(mis_u, mis_v, c, inv_u, inv_v)
        prod_ref[...] += adj_u * vel_u + adj_v * vel_v
        return carry

    lax.fori_loop(0, epochs, epoch, 0)
    product = prod_ref[...]
    rows_sum = product + sh(product, 1, 0)
    total = rows_sum + sh(rows_sum, 0, 1)
    grounded = (ice_ref[...] == 2).astype(jnp.float32)
    grad_ref[...] = -0.25 * grounded * total[0:rows, 0:cols]


def prep_kernel(
    f_hbm, o_hbm, eta_hbm, fric_hbm, ice_hbm, dir_hbm,
    lo_ref, hi_ref, clo_ref, chi_ref, fd_ref,
    f_ref, o_ref, eta_ref, fric_ref, ice_ref, dir_ref, sem,
):
    epochs, comps, rows, cols = f_ref.shape
    h = HALO
    n = epochs * comps
    copies = copy_in(
        [
            (ice_hbm, ice_ref), (dir_hbm, dir_ref), (fric_hbm, fric_ref), (eta_hbm, eta_ref),
            (f_hbm, f_ref), (o_hbm, o_ref),
        ],
        sem,
    )
    clo_ref[...] = jnp.zeros_like(clo_ref)
    chi_ref[...] = jnp.zeros_like(chi_ref)

    def put(p, val):
        lo_ref[p] = val[0:h]
        hi_ref[p] = val[rows - h : rows]
        t = val.T
        clo_ref[p, :, 0:rows] = t[0:h]
        chi_ref[p, :, 0:rows] = t[cols - h : cols]

    for c in copies[:4]:
        c.wait()
    ice = ice_ref[...]
    free = (1 - dir_ref[...]).astype(jnp.float32)
    drag = jnp.where(ice == 2, fric_ref[...], jnp.where(ice == 0, FREE_DRAG, 0.0))
    fd_ref[0] = free
    fd_ref[1] = drag
    for k, val in enumerate([eta_ref[...], free, drag]):
        put(2 * n + k, val)
    for c in copies[4:]:
        c.wait()
    for e in range(epochs):
        for comp in range(comps):
            p = e * comps + comp
            put(p, f_ref[e, comp])
            put(n + p, o_ref[e, comp])


def scratch_like(*arrays):
    return [pltpu.VMEM(a.shape, a.dtype) for a in arrays]


def prep(forcing, observed, viscosity, friction, ice_mask, dirichlet):
    epochs, comps, rows, cols = forcing.shape
    planes = 2 * epochs * comps + 3
    vmem = pl.BlockSpec(memory_space=pltpu.VMEM)
    anywhere = pl.BlockSpec(memory_space=pl.ANY)
    slab = jax.ShapeDtypeStruct((planes, HALO, cols), jnp.float32)
    args = (forcing, observed, viscosity, friction, ice_mask, dirichlet)
    return pl.pallas_call(
        prep_kernel,
        out_shape=(slab, slab, slab, slab, jax.ShapeDtypeStruct((2, rows, cols), jnp.float32)),
        in_specs=[anywhere] * 6,
        out_specs=(vmem,) * 5,
        scratch_shapes=scratch_like(*args) + [pltpu.SemaphoreType.DMA((6,))],
    )(*args)


def local_solve(forcing, observed, eta, fd, ice_mask, ra, rb, ca, cb):
    epochs, comps, rows, cols = forcing.shape
    full = (rows + 2 * HALO, 2 * cols)
    vmem = pl.BlockSpec(memory_space=pltpu.VMEM)
    anywhere = pl.BlockSpec(memory_space=pl.ANY)
    nodes = full[0] * full[1]
    args = (forcing, observed, eta, fd, ice_mask, ra, rb, ca, cb)
    return pl.pallas_call(
        kernel,
        out_shape=(
            jax.ShapeDtypeStruct(forcing.shape, jnp.float32),
            jax.ShapeDtypeStruct((rows, cols), jnp.float32),
        ),
        in_specs=[anywhere] * 9,
        out_specs=(vmem, vmem),
        scratch_shapes=scratch_like(*args)
        + [
            pltpu.VMEM((3 + 2 * comps,) + full, jnp.float32),
            pltpu.VMEM((12,) + full, jnp.float32),
            pltpu.VMEM(full, jnp.float32),
            pltpu.SemaphoreType.DMA((9,)),
        ],
        cost_estimate=pl.CostEstimate(
            flops=epochs * 2 * SWEEPS * comps * 60 * nodes,
            bytes_accessed=4 * (3 * epochs * comps + 40) * rows * cols,
            transcendentals=0,
        ),
    )(*args)


def body(forcing, observed, viscosity, friction, ice_mask, dirichlet):
    epochs, comps, rows, cols = forcing.shape
    h = HALO
    lo, hi, clo, chi, fd = prep(forcing, observed, viscosity, friction, ice_mask, dirichlet)
    ra, rb = exchange(lo, hi, "gx")

    def corners(slab, a, b):
        edge = jnp.concatenate([ra[:, :, a:b], rb[:, :, a:b]], axis=1)
        return lax.dynamic_update_slice(slab, jnp.swapaxes(edge, 1, 2), (0, 0, rows))

    ca, cb = exchange(corners(clo, 0, h), corners(chi, cols - h, cols), "gy")
    return local_solve(forcing, observed, viscosity, fd, ice_mask, ra, rb, ca, cb)


def solution(mesh):
    return jax.shard_map(
        body,
        mesh=mesh,
        in_specs=(
            P(None, None, "gx", "gy"),
            P(None, None, "gx", "gy"),
            P("gx", "gy"),
            P("gx", "gy"),
            P("gx", "gy"),
            P("gx", "gy"),
        ),
        out_specs=(P(None, None, "gx", "gy"), P("gx", "gy")),
        check_vma=False,
    )
```

```python
import functools

import jax
import jax.numpy as jnp
from jax import lax
from jax.experimental import pallas as pl
from jax.experimental.pallas import tpu as pltpu
from jax.sharding import PartitionSpec as P

SWEEPS = 3

UPPER_BOUND = 2.4
LOWER_BOUND = 0.05
FREE_DRAG = 4.0

HALO = 2 * SWEEPS + 2


def exchange(slab_low, slab_high, axis):
    size = lax.axis_size(axis)
    up = [(i, i + 1) for i in range(size - 1)]
    down = [(i + 1, i) for i in range(size - 1)]
    after = lax.ppermute(slab_low, axis, down)
    before = lax.ppermute(slab_high, axis, up)
    return after, before


def sh(x, di, dj):
    if di:
        x = pltpu.roll(x, (-di) % x.shape[0], 0)
    if dj:
        x = pltpu.roll(x, (-dj) % x.shape[1], 1)
    return x


def stencil_pair(u, v, c):
    north, south, east, west, face_np, face_sm, face_ep, face_wm, node_drag = c

    def normal_part(values, weight_rows, weight_cols):
        middle = values
        rows_part = face_np * (sh(values, 1, 0) - middle) - face_sm * (middle - sh(values, -1, 0))
        cols_part = face_ep * (sh(values, 0, 1) - middle) - face_wm * (middle - sh(values, 0, -1))
        return weight_rows * rows_part + weight_cols * cols_part

    def cross_part(values, weight_rows, weight_cols):
        slope_cols = 0.5 * (sh(values, 0, 1) - sh(values, 0, -1))
        slope_rows = 0.5 * (sh(values, 1, 0) - sh(values, -1, 0))
        first = 0.5 * weight_rows * (north * sh(slope_cols, 1, 0) - south * sh(slope_cols, -1, 0))
        second = 0.5 * weight_cols * (east * sh(slope_rows, 0, 1) - west * sh(slope_rows, 0, -1))
        return first + second

    image_u = node_drag * u - normal_part(u, 4.0, 1.0) - cross_part(v, 2.0, 1.0)
    image_v = node_drag * v - normal_part(v, 1.0, 4.0) - cross_part(u, 1.0, 2.0)
    return image_u, image_v


def chebyshev_pair(rhs_u, rhs_v, c, inv_u, inv_v):
    centre_value = 0.5 * (UPPER_BOUND + LOWER_BOUND)
    half_width = 0.5 * (UPPER_BOUND - LOWER_BOUND)
    ratio_value = centre_value / half_width
    weight_now = 1.0 / ratio_value
    res_u, res_v = rhs_u, rhs_v
    dir_u = inv_u * res_u / centre_value
    dir_v = inv_v * res_v / centre_value
    it_u = jnp.zeros_like(rhs_u)
    it_v = jnp.zeros_like(rhs_v)
    for sweep_no in range(SWEEPS + 1):
        it_u = it_u + dir_u
        it_v = it_v + dir_v
        if sweep_no < SWEEPS:
            img_u, img_v = stencil_pair(dir_u, dir_v, c)
            res_u = res_u - img_u
            res_v = res_v - img_v
            weight_next = 1.0 / (2.0 * ratio_value - weight_now)
            a = weight_next * weight_now
            b = 2.0 * weight_next / half_width
            dir_u = a * dir_u + b * (inv_u * res_u)
            dir_v = a * dir_v + b * (inv_v * res_v)
            weight_now = weight_next
    return it_u, it_v


def copy_in(pairs, sem):
    copies = [pltpu.make_async_copy(src, dst, sem.at[i]) for i, (src, dst) in enumerate(pairs)]
    for c in copies:
        c.start()
    return copies


def kernel(
    f_hbm, o_hbm, eta_hbm, fd_hbm, ice_hbm, ra_hbm, rb_hbm, ca_hbm, cb_hbm,
    vel_ref, grad_ref,
    f_ref, o_ref, eta_ref, fd_ref, ice_ref, ra_ref, rb_ref, ca_ref, cb_ref,
    field_ref, coef_ref, prod_ref, sem,
):
    epochs, comps, rows, cols = f_ref.shape
    h = HALO
    n = epochs * comps
    copies = copy_in(
        [
            (eta_hbm, eta_ref), (fd_hbm, fd_ref), (ra_hbm, ra_ref), (rb_hbm, rb_ref),
            (ca_hbm, ca_ref), (cb_hbm, cb_ref), (f_hbm, f_ref), (o_hbm, o_ref), (ice_hbm, ice_ref),
        ],
        sem,
    )
    for k in range(field_ref.shape[0]):
        field_ref[k, :, cols + h : 2 * cols - h] = jnp.zeros((rows + 2 * h, cols - 2 * h), jnp.float32)
    for c in copies[:6]:
        c.wait()

    def assemble(dst, centre, p):
        dst[0:rows, 0:cols] = centre
        dst[rows : rows + h, 0:cols] = ra_ref[p]
        dst[rows + h : rows + 2 * h, 0:cols] = rb_ref[p]
        dst[:, cols : cols + h] = ca_ref[p].T[0 : rows + 2 * h, :]
        dst[:, 2 * cols - h :] = cb_ref[p].T[0 : rows + 2 * h, :]

    assemble(field_ref.at[0], eta_ref[...], 2 * n)
    assemble(field_ref.at[1], fd_ref[0], 2 * n + 1)
    assemble(field_ref.at[2], fd_ref[1], 2 * n + 2)
    eta = field_ref[0]
    free = field_ref[1]
    drag = field_ref[2]
    node_drag = 0.25 * (sh(drag, -1, -1) + sh(drag, 0, -1) + sh(drag, -1, 0) + drag)
    north = sh(eta, 1, 0)
    south = sh(eta, -1, 0)
    east = sh(eta, 0, 1)
    west = sh(eta, 0, -1)
    face_np = 0.5 * (eta + north)
    face_sm = 0.5 * (eta + south)
    face_ep = 0.5 * (eta + east)
    face_wm = 0.5 * (eta + west)
    rows_sum = face_np + face_sm
    cols_sum = face_ep + face_wm
    inv_u = free / (4.0 * rows_sum + cols_sum + node_drag + 1.0 - free)
    inv_v = free / (rows_sum + 4.0 * cols_sum + node_drag + 1.0 - free)
    for k, val in enumerate(
        [north, south, east, west, face_np, face_sm, face_ep, face_wm, node_drag, inv_u, inv_v, free]
    ):
        coef_ref[k] = val
    prod_ref[...] = jnp.zeros_like(prod_ref)
    for c in copies[6:]:
        c.wait()

    def epoch(e, carry):
        for comp in range(comps):
            p = e * comps + comp
            assemble(field_ref.at[3 + comp], f_ref[e, comp], p)
            assemble(field_ref.at[3 + comps + comp], o_ref[e, comp], n + p)
        c = tuple(coef_ref[k] for k in range(9))
        inv_u = coef_ref[9]
        inv_v = coef_ref[10]
        free = coef_ref[11]
        vel_u, vel_v = chebyshev_pair(free * field_ref[3], free * field_ref[4], c, inv_u, inv_v)
        vel_ref[e, 0] = vel_u[0:rows, 0:cols]
        vel_ref[e, 1] = vel_v[0:rows, 0:cols]
        mis_u = free * (vel_u - field_ref[5])
        mis_v = free * (vel_v - field_ref[6])
        adj_u, adj_v = chebyshev_pair(mis_u, mis_v, c, inv_u, inv_v)
        prod_ref[...] += adj_u * vel_u + adj_v * vel_v
        return carry

    lax.fori_loop(0, epochs, epoch, 0)
    product = prod_ref[...]
    rows_sum = product + sh(product, 1, 0)
    total = rows_sum + sh(rows_sum, 0, 1)
    grounded = (ice_ref[...] == 2).astype(jnp.float32)
    grad_ref[...] = -0.25 * grounded * total[0:rows, 0:cols]


def prep_kernel(
    f_hbm, o_hbm, eta_hbm, fric_hbm, ice_hbm, dir_hbm,
    lo_hbm, hi_hbm, clo_hbm, chi_hbm, fd_hbm,
    f_ref, o_ref, eta_ref, fric_ref, ice_ref, dir_ref, lo_ref, hi_ref, clo_ref, chi_ref, fd_ref,
    sem, out_sem,
):
    epochs, comps, rows, cols = f_ref.shape
    h = HALO
    n = epochs * comps
    copies = copy_in(
        [
            (ice_hbm, ice_ref), (dir_hbm, dir_ref), (fric_hbm, fric_ref), (eta_hbm, eta_ref),
            (f_hbm, f_ref), (o_hbm, o_ref),
        ],
        sem,
    )
    for c in copies[:4]:
        c.wait()
    ice = ice_ref[...]
    free = (1 - dir_ref[...]).astype(jnp.float32)
    drag = jnp.where(ice == 2, fric_ref[...], jnp.where(ice == 0, FREE_DRAG, 0.0))
    fd_ref[0] = free
    fd_ref[1] = drag
    for c in copies[4:]:
        c.wait()
    planes = []
    for e in range(epochs):
        for comp in range(comps):
            planes.append(f_ref.at[e, comp])
    for e in range(epochs):
        for comp in range(comps):
            planes.append(o_ref.at[e, comp])
    for p, ref in enumerate(planes):
        lo_ref[p] = ref[0:h, :]
        hi_ref[p] = ref[rows - h : rows, :]
    for k, val in enumerate([eta_ref[...], free, drag]):
        lo_ref[2 * n + k] = val[0:h]
        hi_ref[2 * n + k] = val[rows - h : rows]
    out = copy_in([(lo_ref, lo_hbm), (hi_ref, hi_hbm), (fd_ref, fd_hbm)], out_sem)
    for p, ref in enumerate(planes):
        t = ref[...].T
        clo_ref[p] = t[0:h]
        chi_ref[p] = t[cols - h : cols]
    for k, val in enumerate([eta_ref[...], free, drag]):
        t = val.T
        clo_ref[2 * n + k] = t[0:h]
        chi_ref[2 * n + k] = t[cols - h : cols]
    out += copy_in([(clo_ref, clo_hbm), (chi_ref, chi_hbm)], out_sem.at[3:])
    for c in out:
        c.wait()


def scratch_like(*arrays):
    return [pltpu.VMEM(a.shape, a.dtype) for a in arrays]


def prep(forcing, observed, viscosity, friction, ice_mask, dirichlet):
    epochs, comps, rows, cols = forcing.shape
    planes = 2 * epochs * comps + 3
    hbm = pl.BlockSpec(memory_space=pltpu.HBM)
    slab = jax.ShapeDtypeStruct((planes, HALO, cols), jnp.float32)
    cslab = jax.ShapeDtypeStruct((planes, HALO, rows), jnp.float32)
    fd = jax.ShapeDtypeStruct((2, rows, cols), jnp.float32)
    outs = (slab, slab, cslab, cslab, fd)
    args = (forcing, observed, viscosity, friction, ice_mask, dirichlet)
    return pl.pallas_call(
        prep_kernel,
        out_shape=outs,
        in_specs=[hbm] * 6,
        out_specs=(hbm,) * 5,
        scratch_shapes=scratch_like(*args, *outs)
        + [pltpu.SemaphoreType.DMA((6,)), pltpu.SemaphoreType.DMA((5,))],
    )(*args)


def local_solve(forcing, observed, eta, fd, ice_mask, ra, rb, ca, cb):
    epochs, comps, rows, cols = forcing.shape
    full = (rows + 2 * HALO, 2 * cols)
    vmem = pl.BlockSpec(memory_space=pltpu.VMEM)
    anywhere = pl.BlockSpec(memory_space=pltpu.HBM)
    nodes = full[0] * full[1]
    args = (forcing, observed, eta, fd, ice_mask, ra, rb, ca, cb)
    return pl.pallas_call(
        kernel,
        out_shape=(
            jax.ShapeDtypeStruct(forcing.shape, jnp.float32),
            jax.ShapeDtypeStruct((rows, cols), jnp.float32),
        ),
        in_specs=[anywhere] * 9,
        out_specs=(vmem, vmem),
        scratch_shapes=scratch_like(*args)
        + [
            pltpu.VMEM((3 + 2 * comps,) + full, jnp.float32),
            pltpu.VMEM((12,) + full, jnp.float32),
            pltpu.VMEM(full, jnp.float32),
            pltpu.SemaphoreType.DMA((9,)),
        ],
        cost_estimate=pl.CostEstimate(
            flops=epochs * 2 * SWEEPS * comps * 60 * nodes,
            bytes_accessed=4 * (3 * epochs * comps + 40) * rows * cols,
            transcendentals=0,
        ),
    )(*args)


def body(forcing, observed, viscosity, friction, ice_mask, dirichlet):
    epochs, comps, rows, cols = forcing.shape
    h = HALO
    lo, hi, clo, chi, fd = prep(forcing, observed, viscosity, friction, ice_mask, dirichlet)
    ra, rb = exchange(lo, hi, "gx")

    def corners(slab, a, b):
        edge = jnp.concatenate([ra[:, :, a:b], rb[:, :, a:b]], axis=1)
        gap = jnp.zeros((slab.shape[0], h, cols - rows - 2 * h), jnp.float32)
        return jnp.concatenate([slab, jnp.swapaxes(edge, 1, 2), gap], axis=2)

    ca, cb = exchange(corners(clo, 0, h), corners(chi, cols - h, cols), "gy")
    return local_solve(forcing, observed, viscosity, fd, ice_mask, ra, rb, ca, cb)


def solution(mesh):
    return jax.shard_map(
        body,
        mesh=mesh,
        in_specs=(
            P(None, None, "gx", "gy"),
            P(None, None, "gx", "gy"),
            P("gx", "gy"),
            P("gx", "gy"),
            P("gx", "gy"),
            P("gx", "gy"),
        ),
        out_specs=(P(None, None, "gx", "gy"), P("gx", "gy")),
        check_vma=False,
    )
```

```python
import functools

import jax
import jax.numpy as jnp
from jax import lax
from jax.experimental import pallas as pl
from jax.experimental.pallas import tpu as pltpu
from jax.sharding import PartitionSpec as P

SWEEPS = 3

UPPER_BOUND = 2.4
LOWER_BOUND = 0.05
FREE_DRAG = 4.0

HALO = 2 * SWEEPS + 2


def exchange(slab_low, slab_high, axis):
    size = lax.axis_size(axis)
    up = [(i, i + 1) for i in range(size - 1)]
    down = [(i + 1, i) for i in range(size - 1)]
    after = lax.ppermute(slab_low, axis, down)
    before = lax.ppermute(slab_high, axis, up)
    return after, before


def sh(x, di, dj):
    if di:
        x = pltpu.roll(x, (-di) % x.shape[0], 0)
    if dj:
        x = pltpu.roll(x, (-dj) % x.shape[1], 1)
    return x


def stencil_pair(u, v, cu, cv):
    def rolled(x):
        x_n = sh(x, 1, 0)
        x_s = sh(x, -1, 0)
        return x_n, x_s, sh(x, 0, 1), sh(x, 0, -1), sh(x_n, 0, 1), sh(x_n, 0, -1), sh(x_s, 0, 1), sh(x_s, 0, -1)

    un, us, ue, uw, une, unw, use, usw = rolled(u)
    vn, vs, ve, vw, vne, vnw, vse, vsw = rolled(v)

    def image(c, x, xn, xs, xe, xw, yne, ynw, yse, ysw):
        own = c[0] * x + c[1] * xn + c[2] * xs + c[3] * xe + c[4] * xw
        cross = c[5] * yne + c[6] * ynw + c[7] * yse + c[8] * ysw
        return own + cross

    image_u = image(cu, u, un, us, ue, uw, vne, vnw, vse, vsw)
    image_v = image(cv, v, vn, vs, ve, vw, une, unw, use, usw)
    return image_u, image_v


def chebyshev_pair(rhs_u, rhs_v, cu, cv, inv_u, inv_v):
    centre_value = 0.5 * (UPPER_BOUND + LOWER_BOUND)
    half_width = 0.5 * (UPPER_BOUND - LOWER_BOUND)
    ratio_value = centre_value / half_width
    weight_now = 1.0 / ratio_value
    res_u, res_v = rhs_u, rhs_v
    dir_u = inv_u * res_u / centre_value
    dir_v = inv_v * res_v / centre_value
    it_u = jnp.zeros_like(rhs_u)
    it_v = jnp.zeros_like(rhs_v)
    for sweep_no in range(SWEEPS + 1):
        it_u = it_u + dir_u
        it_v = it_v + dir_v
        if sweep_no < SWEEPS:
            img_u, img_v = stencil_pair(dir_u, dir_v, cu, cv)
            res_u = res_u - img_u
            res_v = res_v - img_v
            weight_next = 1.0 / (2.0 * ratio_value - weight_now)
            a = weight_next * weight_now
            b = 2.0 * weight_next / half_width
            dir_u = a * dir_u + b * (inv_u * res_u)
            dir_v = a * dir_v + b * (inv_v * res_v)
            weight_now = weight_next
    return it_u, it_v


def copy_in(pairs, sem):
    copies = [pltpu.make_async_copy(src, dst, sem.at[i]) for i, (src, dst) in enumerate(pairs)]
    for c in copies:
        c.start()
    return copies


def kernel(
    f_hbm, o_hbm, eta_hbm, fd_hbm, ice_hbm, ra_hbm, rb_hbm, ca_hbm, cb_hbm,
    vel_ref, grad_ref,
    f_ref, o_ref, eta_ref, fd_ref, ice_ref, ra_ref, rb_ref, ca_ref, cb_ref,
    field_ref, coef_ref, prod_ref, sem,
):
    epochs, comps, rows, cols = f_ref.shape
    h = HALO
    n = epochs * comps
    copies = copy_in(
        [
            (eta_hbm, eta_ref), (fd_hbm, fd_ref), (ra_hbm, ra_ref), (rb_hbm, rb_ref),
            (ca_hbm, ca_ref), (cb_hbm, cb_ref), (f_hbm, f_ref), (o_hbm, o_ref), (ice_hbm, ice_ref),
        ],
        sem,
    )
    for k in range(field_ref.shape[0]):
        field_ref[k, :, cols + h : 2 * cols - h] = jnp.zeros((rows + 2 * h, cols - 2 * h), jnp.float32)
    for c in copies[:6]:
        c.wait()

    def assemble(dst, centre, p):
        dst[0:rows, 0:cols] = centre
        dst[rows : rows + h, 0:cols] = ra_ref[p]
        dst[rows + h : rows + 2 * h, 0:cols] = rb_ref[p]
        dst[:, cols : cols + h] = ca_ref[p].T[0 : rows + 2 * h, :]
        dst[:, 2 * cols - h :] = cb_ref[p].T[0 : rows + 2 * h, :]

    assemble(field_ref.at[0], eta_ref[...], 2 * n)
    assemble(field_ref.at[1], fd_ref[0], 2 * n + 1)
    assemble(field_ref.at[2], fd_ref[1], 2 * n + 2)
    eta = field_ref[0]
    free = field_ref[1]
    drag = field_ref[2]
    node_drag = 0.25 * (sh(drag, -1, -1) + sh(drag, 0, -1) + sh(drag, -1, 0) + drag)
    north = sh(eta, 1, 0)
    south = sh(eta, -1, 0)
    east = sh(eta, 0, 1)
    west = sh(eta, 0, -1)
    face_np = 0.5 * (eta + north)
    face_sm = 0.5 * (eta + south)
    face_ep = 0.5 * (eta + east)
    face_wm = 0.5 * (eta + west)
    rows_sum = face_np + face_sm
    cols_sum = face_ep + face_wm
    diag_u = 4.0 * rows_sum + cols_sum + node_drag
    diag_v = rows_sum + 4.0 * cols_sum + node_drag
    inv_u = free / (diag_u + 1.0 - free)
    inv_v = free / (diag_v + 1.0 - free)

    def cross(wr, wc):
        a, b = 0.25 * wr, 0.25 * wc
        return [
            -(a * north + b * east),
            a * north + b * west,
            a * south + b * east,
            -(a * south + b * west),
        ]

    coefs = [diag_u, -4.0 * face_np, -4.0 * face_sm, -face_ep, -face_wm] + cross(2.0, 1.0)
    coefs += [diag_v, -face_np, -face_sm, -4.0 * face_ep, -4.0 * face_wm] + cross(1.0, 2.0)
    for k, val in enumerate(coefs + [inv_u, inv_v, free]):
        coef_ref[k] = val
    prod_ref[...] = jnp.zeros_like(prod_ref)
    for c in copies[6:]:
        c.wait()

    def epoch(e, carry):
        for comp in range(comps):
            p = e * comps + comp
            assemble(field_ref.at[3 + comp], f_ref[e, comp], p)
            assemble(field_ref.at[3 + comps + comp], o_ref[e, comp], n + p)
        cu = [coef_ref[k] for k in range(9)]
        cv = [coef_ref[9 + k] for k in range(9)]
        inv_u = coef_ref[18]
        inv_v = coef_ref[19]
        free = coef_ref[20]
        vel_u, vel_v = chebyshev_pair(free * field_ref[3], free * field_ref[4], cu, cv, inv_u, inv_v)
        vel_ref[e, 0] = vel_u[0:rows, 0:cols]
        vel_ref[e, 1] = vel_v[0:rows, 0:cols]
        mis_u = free * (vel_u - field_ref[5])
        mis_v = free * (vel_v - field_ref[6])
        adj_u, adj_v = chebyshev_pair(mis_u, mis_v, cu, cv, inv_u, inv_v)
        prod_ref[...] += adj_u * vel_u + adj_v * vel_v
        return carry

    lax.fori_loop(0, epochs, epoch, 0)
    product = prod_ref[...]
    rows_sum = product + sh(product, 1, 0)
    total = rows_sum + sh(rows_sum, 0, 1)
    grounded = (ice_ref[...] == 2).astype(jnp.float32)
    grad_ref[...] = -0.25 * grounded * total[0:rows, 0:cols]


def prep_kernel(
    f_hbm, o_hbm, eta_hbm, fric_hbm, ice_hbm, dir_hbm,
    lo_hbm, hi_hbm, clo_hbm, chi_hbm, fd_hbm,
    f_ref, o_ref, eta_ref, fric_ref, ice_ref, dir_ref, lo_ref, hi_ref, clo_ref, chi_ref, fd_ref,
    sem, out_sem,
):
    epochs, comps, rows, cols = f_ref.shape
    h = HALO
    n = epochs * comps
    copies = copy_in(
        [
            (ice_hbm, ice_ref), (dir_hbm, dir_ref), (fric_hbm, fric_ref), (eta_hbm, eta_ref),
            (f_hbm, f_ref), (o_hbm, o_ref),
        ],
        sem,
    )
    for c in copies[:4]:
        c.wait()
    ice = ice_ref[...]
    free = (1 - dir_ref[...]).astype(jnp.float32)
    drag = jnp.where(ice == 2, fric_ref[...], jnp.where(ice == 0, FREE_DRAG, 0.0))
    fd_ref[0] = free
    fd_ref[1] = drag
    for c in copies[4:]:
        c.wait()
    planes = []
    for e in range(epochs):
        for comp in range(comps):
            planes.append(f_ref.at[e, comp])
    for e in range(epochs):
        for comp in range(comps):
            planes.append(o_ref.at[e, comp])
    for p, ref in enumerate(planes):
        lo_ref[p] = ref[0:h, :]
        hi_ref[p] = ref[rows - h : rows, :]
    for k, val in enumerate([eta_ref[...], free, drag]):
        lo_ref[2 * n + k] = val[0:h]
        hi_ref[2 * n + k] = val[rows - h : rows]
    out = copy_in([(lo_ref, lo_hbm), (hi_ref, hi_hbm), (fd_ref, fd_hbm)], out_sem)
    for p, ref in enumerate(planes):
        t = ref[...].T
        clo_ref[p] = t[0:h]
        chi_ref[p] = t[cols - h : cols]
    for k, val in enumerate([eta_ref[...], free, drag]):
        t = val.T
        clo_ref[2 * n + k] = t[0:h]
        chi_ref[2 * n + k] = t[cols - h : cols]
    out += copy_in([(clo_ref, clo_hbm), (chi_ref, chi_hbm)], out_sem.at[3:])
    for c in out:
        c.wait()


def scratch_like(*arrays):
    return [pltpu.VMEM(a.shape, a.dtype) for a in arrays]


def prep(forcing, observed, viscosity, friction, ice_mask, dirichlet):
    epochs, comps, rows, cols = forcing.shape
    planes = 2 * epochs * comps + 3
    hbm = pl.BlockSpec(memory_space=pltpu.HBM)
    slab = jax.ShapeDtypeStruct((planes, HALO, cols), jnp.float32)
    cslab = jax.ShapeDtypeStruct((planes, HALO, rows), jnp.float32)
    fd = jax.ShapeDtypeStruct((2, rows, cols), jnp.float32)
    outs = (slab, slab, cslab, cslab, fd)
    args = (forcing, observed, viscosity, friction, ice_mask, dirichlet)
    return pl.pallas_call(
        prep_kernel,
        out_shape=outs,
        in_specs=[hbm] * 6,
        out_specs=(hbm,) * 5,
        scratch_shapes=scratch_like(*args, *outs)
        + [pltpu.SemaphoreType.DMA((6,)), pltpu.SemaphoreType.DMA((5,))],
    )(*args)


def local_solve(forcing, observed, eta, fd, ice_mask, ra, rb, ca, cb):
    epochs, comps, rows, cols = forcing.shape
    full = (rows + 2 * HALO, 2 * cols)
    vmem = pl.BlockSpec(memory_space=pltpu.VMEM)
    anywhere = pl.BlockSpec(memory_space=pltpu.HBM)
    nodes = full[0] * full[1]
    args = (forcing, observed, eta, fd, ice_mask, ra, rb, ca, cb)
    return pl.pallas_call(
        kernel,
        out_shape=(
            jax.ShapeDtypeStruct(forcing.shape, jnp.float32),
            jax.ShapeDtypeStruct((rows, cols), jnp.float32),
        ),
        in_specs=[anywhere] * 9,
        out_specs=(vmem, vmem),
        scratch_shapes=scratch_like(*args)
        + [
            pltpu.VMEM((3 + 2 * comps,) + full, jnp.float32),
            pltpu.VMEM((21,) + full, jnp.float32),
            pltpu.VMEM(full, jnp.float32),
            pltpu.SemaphoreType.DMA((9,)),
        ],
        cost_estimate=pl.CostEstimate(
            flops=epochs * 2 * SWEEPS * comps * 60 * nodes,
            bytes_accessed=4 * (3 * epochs * comps + 40) * rows * cols,
            transcendentals=0,
        ),
    )(*args)


def body(forcing, observed, viscosity, friction, ice_mask, dirichlet):
    epochs, comps, rows, cols = forcing.shape
    h = HALO
    lo, hi, clo, chi, fd = prep(forcing, observed, viscosity, friction, ice_mask, dirichlet)
    ra, rb = exchange(lo, hi, "gx")

    def corners(slab, a, b):
        edge = jnp.concatenate([ra[:, :, a:b], rb[:, :, a:b]], axis=1)
        gap = jnp.zeros((slab.shape[0], h, cols - rows - 2 * h), jnp.float32)
        return jnp.concatenate([slab, jnp.swapaxes(edge, 1, 2), gap], axis=2)

    ca, cb = exchange(corners(clo, 0, h), corners(chi, cols - h, cols), "gy")
    return local_solve(forcing, observed, viscosity, fd, ice_mask, ra, rb, ca, cb)


def solution(mesh):
    return jax.shard_map(
        body,
        mesh=mesh,
        in_specs=(
            P(None, None, "gx", "gy"),
            P(None, None, "gx", "gy"),
            P("gx", "gy"),
            P("gx", "gy"),
            P("gx", "gy"),
            P("gx", "gy"),
        ),
        out_specs=(P(None, None, "gx", "gy"), P("gx", "gy")),
        check_vma=False,
    )
```

```python
import functools

import jax
import jax.numpy as jnp
from jax import lax
from jax.experimental import pallas as pl
from jax.experimental.pallas import tpu as pltpu
from jax.sharding import PartitionSpec as P

SWEEPS = 3

UPPER_BOUND = 2.4
LOWER_BOUND = 0.05
FREE_DRAG = 4.0

HALO = 2 * SWEEPS + 2


def exchange(slab_low, slab_high, axis):
    size = lax.axis_size(axis)
    up = [(i, i + 1) for i in range(size - 1)]
    down = [(i + 1, i) for i in range(size - 1)]
    after = lax.ppermute(slab_low, axis, down)
    before = lax.ppermute(slab_high, axis, up)
    return after, before


def sh(x, di, dj):
    if di:
        x = pltpu.roll(x, (-di) % x.shape[0], 0)
    if dj:
        x = pltpu.roll(x, (-dj) % x.shape[1], 1)
    return x


def stencil_pair(u, v, c):
    north, south, east, west, face_np, face_sm, face_ep, face_wm, node_drag = c

    def normal_part(values, weight_rows, weight_cols):
        middle = values
        rows_part = face_np * (sh(values, 1, 0) - middle) - face_sm * (middle - sh(values, -1, 0))
        cols_part = face_ep * (sh(values, 0, 1) - middle) - face_wm * (middle - sh(values, 0, -1))
        return weight_rows * rows_part + weight_cols * cols_part

    def cross_part(values, weight_rows, weight_cols):
        slope_cols = 0.5 * (sh(values, 0, 1) - sh(values, 0, -1))
        slope_rows = 0.5 * (sh(values, 1, 0) - sh(values, -1, 0))
        first = 0.5 * weight_rows * (north * sh(slope_cols, 1, 0) - south * sh(slope_cols, -1, 0))
        second = 0.5 * weight_cols * (east * sh(slope_rows, 0, 1) - west * sh(slope_rows, 0, -1))
        return first + second

    image_u = node_drag * u - normal_part(u, 4.0, 1.0) - cross_part(v, 2.0, 1.0)
    image_v = node_drag * v - normal_part(v, 1.0, 4.0) - cross_part(u, 1.0, 2.0)
    return image_u, image_v


def chebyshev_pair(rhs_u, rhs_v, c, inv_u, inv_v):
    centre_value = 0.5 * (UPPER_BOUND + LOWER_BOUND)
    half_width = 0.5 * (UPPER_BOUND - LOWER_BOUND)
    ratio_value = centre_value / half_width
    weight_now = 1.0 / ratio_value
    res_u, res_v = rhs_u, rhs_v
    dir_u = inv_u * res_u / centre_value
    dir_v = inv_v * res_v / centre_value
    it_u = jnp.zeros_like(rhs_u)
    it_v = jnp.zeros_like(rhs_v)
    for sweep_no in range(SWEEPS + 1):
        it_u = it_u + dir_u
        it_v = it_v + dir_v
        if sweep_no < SWEEPS:
            img_u, img_v = stencil_pair(dir_u, dir_v, c)
            res_u = res_u - img_u
            res_v = res_v - img_v
            weight_next = 1.0 / (2.0 * ratio_value - weight_now)
            a = weight_next * weight_now
            b = 2.0 * weight_next / half_width
            dir_u = a * dir_u + b * (inv_u * res_u)
            dir_v = a * dir_v + b * (inv_v * res_v)
            weight_now = weight_next
    return it_u, it_v


def copy_in(pairs, sem):
    copies = [pltpu.make_async_copy(src, dst, sem.at[i]) for i, (src, dst) in enumerate(pairs)]
    for c in copies:
        c.start()
    return copies


def kernel(
    f_hbm, o_hbm, eta_hbm, fd_hbm, ice_hbm, ra_hbm, rb_hbm, ca_hbm, cb_hbm,
    vel_ref, grad_ref,
    f_ref, o_ref, eta_ref, fd_ref, ice_ref, ra_ref, rb_ref, ca_ref, cb_ref,
    field_ref, coef_ref, prod_ref, sem,
):
    epochs, comps, rows, cols = f_ref.shape
    h = HALO
    n = epochs * comps
    copies = copy_in(
        [
            (eta_hbm, eta_ref), (fd_hbm, fd_ref), (ra_hbm, ra_ref), (rb_hbm, rb_ref),
            (ca_hbm, ca_ref), (cb_hbm, cb_ref), (f_hbm, f_ref), (o_hbm, o_ref), (ice_hbm, ice_ref),
        ],
        sem,
    )
    for k in range(field_ref.shape[0]):
        field_ref[k, :, cols + h : 2 * cols - h] = jnp.zeros((rows + 2 * h, cols - 2 * h), jnp.float32)
    for c in copies[:6]:
        c.wait()

    def assemble(dst, centre, p):
        dst[0:rows, 0:cols] = centre
        dst[rows : rows + h, 0:cols] = ra_ref[p]
        dst[rows + h : rows + 2 * h, 0:cols] = rb_ref[p]
        dst[:, cols : cols + h] = ca_ref[p].T[0 : rows + 2 * h, :]
        dst[:, 2 * cols - h :] = cb_ref[p].T[0 : rows + 2 * h, :]

    assemble(field_ref.at[0], eta_ref[...], 2 * n)
    assemble(field_ref.at[1], fd_ref[0], 2 * n + 1)
    assemble(field_ref.at[2], fd_ref[1], 2 * n + 2)
    eta = field_ref[0]
    free = field_ref[1]
    drag = field_ref[2]
    node_drag = 0.25 * (sh(drag, -1, -1) + sh(drag, 0, -1) + sh(drag, -1, 0) + drag)
    north = sh(eta, 1, 0)
    south = sh(eta, -1, 0)
    east = sh(eta, 0, 1)
    west = sh(eta, 0, -1)
    face_np = 0.5 * (eta + north)
    face_sm = 0.5 * (eta + south)
    face_ep = 0.5 * (eta + east)
    face_wm = 0.5 * (eta + west)
    rows_sum = face_np + face_sm
    cols_sum = face_ep + face_wm
    inv_u = free / (4.0 * rows_sum + cols_sum + node_drag + 1.0 - free)
    inv_v = free / (rows_sum + 4.0 * cols_sum + node_drag + 1.0 - free)
    for k, val in enumerate(
        [north, south, east, west, face_np, face_sm, face_ep, face_wm, node_drag, inv_u, inv_v, free]
    ):
        coef_ref[k] = val
    prod_ref[...] = jnp.zeros_like(prod_ref)
    for c in copies[6:]:
        c.wait()

    def epoch(e, carry):
        for comp in range(comps):
            p = e * comps + comp
            assemble(field_ref.at[3 + comp], f_ref[e, comp], p)
            assemble(field_ref.at[3 + comps + comp], o_ref[e, comp], n + p)
        c = tuple(coef_ref[k] for k in range(9))
        inv_u = coef_ref[9]
        inv_v = coef_ref[10]
        free = coef_ref[11]
        vel_u, vel_v = chebyshev_pair(free * field_ref[3], free * field_ref[4], c, inv_u, inv_v)
        vel_ref[e, 0] = vel_u[0:rows, 0:cols]
        vel_ref[e, 1] = vel_v[0:rows, 0:cols]
        mis_u = free * (vel_u - field_ref[5])
        mis_v = free * (vel_v - field_ref[6])
        adj_u, adj_v = chebyshev_pair(mis_u, mis_v, c, inv_u, inv_v)
        prod_ref[...] += adj_u * vel_u + adj_v * vel_v
        return carry

    lax.fori_loop(0, epochs, epoch, 0)
    product = prod_ref[...]
    rows_sum = product + sh(product, 1, 0)
    total = rows_sum + sh(rows_sum, 0, 1)
    grounded = (ice_ref[...] == 2).astype(jnp.float32)
    grad_ref[...] = -0.25 * grounded * total[0:rows, 0:cols]


def prep_kernel(
    f_hbm, o_hbm, eta_hbm, fric_hbm, ice_hbm, dir_hbm,
    lo_hbm, hi_hbm, fd_hbm,
    f_ref, o_ref, eta_ref, fric_ref, ice_ref, dir_ref, lo_ref, hi_ref, fd_ref,
    sem, out_sem,
):
    epochs, comps, rows, cols = f_ref.shape
    h = HALO
    n = epochs * comps
    copies = []
    for k, (src, dst) in enumerate([(f_hbm, f_ref), (o_hbm, o_ref)]):
        for j, (a, b) in enumerate([(0, h), (rows - h, rows)]):
            copies.append(
                pltpu.make_async_copy(
                    src.at[:, :, a:b], dst.at[:, :, a:b], sem.at[6 + 2 * k + j]
                )
            )
            copies[-1].start()
    copies += copy_in(
        [(ice_hbm, ice_ref), (dir_hbm, dir_ref), (fric_hbm, fric_ref), (eta_hbm, eta_ref)], sem
    )
    for c in copies[4:]:
        c.wait()
    ice = ice_ref[...]
    free = (1 - dir_ref[...]).astype(jnp.float32)
    drag = jnp.where(ice == 2, fric_ref[...], jnp.where(ice == 0, FREE_DRAG, 0.0))
    fd_ref[0] = free
    fd_ref[1] = drag
    for k, val in enumerate([eta_ref[...], free, drag]):
        lo_ref[2 * n + k] = val[0:h]
        hi_ref[2 * n + k] = val[rows - h : rows]
    for c in copies[:4]:
        c.wait()
    for e in range(epochs):
        for comp in range(comps):
            p = e * comps + comp
            lo_ref[p] = f_ref[e, comp, 0:h, :]
            hi_ref[p] = f_ref[e, comp, rows - h : rows, :]
            lo_ref[n + p] = o_ref[e, comp, 0:h, :]
            hi_ref[n + p] = o_ref[e, comp, rows - h : rows, :]
    out = copy_in([(lo_ref, lo_hbm), (hi_ref, hi_hbm), (fd_ref, fd_hbm)], out_sem)
    for c in out:
        c.wait()


def columns_kernel(
    f_hbm, o_hbm, eta_hbm, fd_hbm, clo_hbm, chi_hbm,
    f_ref, o_ref, eta_ref, fd_ref, clo_ref, chi_ref, sem, out_sem,
):
    epochs, comps, rows, cols = f_ref.shape
    h = HALO
    copies = copy_in([(eta_hbm, eta_ref), (fd_hbm, fd_ref), (f_hbm, f_ref), (o_hbm, o_ref)], sem)
    clo_ref[...] = jnp.zeros_like(clo_ref)
    chi_ref[...] = jnp.zeros_like(chi_ref)
    for c in copies:
        c.wait()
    planes = [f_ref.at[e, comp] for e in range(epochs) for comp in range(comps)]
    planes += [o_ref.at[e, comp] for e in range(epochs) for comp in range(comps)]
    planes += [eta_ref, fd_ref.at[0], fd_ref.at[1]]
    for p, ref in enumerate(planes):
        t = ref[...].T
        clo_ref[p, :, 0:rows] = t[0:h]
        chi_ref[p, :, 0:rows] = t[cols - h : cols]
    out = copy_in([(clo_ref, clo_hbm), (chi_ref, chi_hbm)], out_sem)
    for c in out:
        c.wait()


def corner_kernel(rows, clo_hbm, chi_hbm, ra_hbm, rb_hbm, lo_hbm, hi_hbm, clo, chi, ra, rb, sem, out_sem):
    planes, h, cols = ra.shape
    copies = copy_in([(clo_hbm, clo), (chi_hbm, chi), (ra_hbm, ra), (rb_hbm, rb)], sem)
    for c in copies:
        c.wait()
    for p in range(planes):
        ta = ra[p].T
        tb = rb[p].T
        clo[p, :, rows : rows + h] = ta[0:h]
        clo[p, :, rows + h : rows + 2 * h] = tb[0:h]
        chi[p, :, rows : rows + h] = ta[cols - h : cols]
        chi[p, :, rows + h : rows + 2 * h] = tb[cols - h : cols]
    out = copy_in([(clo, lo_hbm), (chi, hi_hbm)], out_sem)
    for c in out:
        c.wait()


def scratch_like(*arrays):
    return [pltpu.VMEM(a.shape, a.dtype) for a in arrays]


def local_solve(forcing, observed, eta, fd, ice_mask, ra, rb, ca, cb):
    epochs, comps, rows, cols = forcing.shape
    full = (rows + 2 * HALO, 2 * cols)
    vmem = pl.BlockSpec(memory_space=pltpu.VMEM)
    anywhere = pl.BlockSpec(memory_space=pltpu.HBM)
    nodes = full[0] * full[1]
    args = (forcing, observed, eta, fd, ice_mask, ra, rb, ca, cb)
    return pl.pallas_call(
        kernel,
        out_shape=(
            jax.ShapeDtypeStruct(forcing.shape, jnp.float32),
            jax.ShapeDtypeStruct((rows, cols), jnp.float32),
        ),
        in_specs=[anywhere] * 9,
        out_specs=(vmem, vmem),
        scratch_shapes=scratch_like(*args)
        + [
            pltpu.VMEM((3 + 2 * comps,) + full, jnp.float32),
            pltpu.VMEM((12,) + full, jnp.float32),
            pltpu.VMEM(full, jnp.float32),
            pltpu.SemaphoreType.DMA((9,)),
        ],
        cost_estimate=pl.CostEstimate(
            flops=epochs * 2 * SWEEPS * comps * 60 * nodes,
            bytes_accessed=4 * (3 * epochs * comps + 40) * rows * cols,
            transcendentals=0,
        ),
    )(*args)


def body(forcing, observed, viscosity, friction, ice_mask, dirichlet):
    epochs, comps, rows, cols = forcing.shape
    h = HALO
    planes = 2 * epochs * comps + 3
    slab = jax.ShapeDtypeStruct((planes, h, cols), jnp.float32)
    fd_shape = jax.ShapeDtypeStruct((2, rows, cols), jnp.float32)
    args = (forcing, observed, viscosity, friction, ice_mask, dirichlet)
    hbm = pl.BlockSpec(memory_space=pltpu.HBM)
    lo, hi, fd = pl.pallas_call(
        prep_kernel,
        out_shape=(slab, slab, fd_shape),
        in_specs=[hbm] * 6,
        out_specs=(hbm,) * 3,
        scratch_shapes=scratch_like(*args, slab, slab, fd_shape)
        + [pltpu.SemaphoreType.DMA((10,)), pltpu.SemaphoreType.DMA((3,))],
    )(*args)
    ra, rb = exchange(lo, hi, "gx")
    cargs = (forcing, observed, viscosity, fd)
    clo, chi = pl.pallas_call(
        columns_kernel,
        out_shape=(slab, slab),
        in_specs=[hbm] * 4,
        out_specs=(hbm, hbm),
        scratch_shapes=scratch_like(*cargs, slab, slab)
        + [pltpu.SemaphoreType.DMA((4,)), pltpu.SemaphoreType.DMA((2,))],
    )(*cargs)
    xargs = (clo, chi, ra, rb)
    clo, chi = pl.pallas_call(
        functools.partial(corner_kernel, rows),
        out_shape=(slab, slab),
        in_specs=[hbm] * 4,
        out_specs=(hbm, hbm),
        scratch_shapes=scratch_like(*xargs)
        + [pltpu.SemaphoreType.DMA((4,)), pltpu.SemaphoreType.DMA((2,))],
    )(*xargs)
    ca, cb = exchange(clo, chi, "gy")
    return local_solve(forcing, observed, viscosity, fd, ice_mask, ra, rb, ca, cb)


def solution(mesh):
    return jax.shard_map(
        body,
        mesh=mesh,
        in_specs=(
            P(None, None, "gx", "gy"),
            P(None, None, "gx", "gy"),
            P("gx", "gy"),
            P("gx", "gy"),
            P("gx", "gy"),
            P("gx", "gy"),
        ),
        out_specs=(P(None, None, "gx", "gy"), P("gx", "gy")),
        check_vma=False,
    )
```

```python
import functools

import jax
import jax.numpy as jnp
from jax import lax
from jax.experimental import pallas as pl
from jax.experimental.pallas import tpu as pltpu
from jax.sharding import PartitionSpec as P

SWEEPS = 3

UPPER_BOUND = 2.4
LOWER_BOUND = 0.05
FREE_DRAG = 4.0

HALO = 2 * SWEEPS + 2


def exchange(slab_low, slab_high, axis):
    size = lax.axis_size(axis)
    up = [(i, i + 1) for i in range(size - 1)]
    down = [(i + 1, i) for i in range(size - 1)]
    after = lax.ppermute(slab_low, axis, down)
    before = lax.ppermute(slab_high, axis, up)
    return after, before


def sh(x, di, dj):
    if di:
        x = pltpu.roll(x, (-di) % x.shape[0], 0)
    if dj:
        x = pltpu.roll(x, (-dj) % x.shape[1], 1)
    return x


def stencil_pair(u, v, c):
    north, south, east, west, face_np, face_sm, face_ep, face_wm, node_drag = c

    def normal_part(values, weight_rows, weight_cols):
        middle = values
        rows_part = face_np * (sh(values, 1, 0) - middle) - face_sm * (middle - sh(values, -1, 0))
        cols_part = face_ep * (sh(values, 0, 1) - middle) - face_wm * (middle - sh(values, 0, -1))
        return weight_rows * rows_part + weight_cols * cols_part

    def cross_part(values, weight_rows, weight_cols):
        slope_cols = 0.5 * (sh(values, 0, 1) - sh(values, 0, -1))
        slope_rows = 0.5 * (sh(values, 1, 0) - sh(values, -1, 0))
        first = 0.5 * weight_rows * (north * sh(slope_cols, 1, 0) - south * sh(slope_cols, -1, 0))
        second = 0.5 * weight_cols * (east * sh(slope_rows, 0, 1) - west * sh(slope_rows, 0, -1))
        return first + second

    image_u = node_drag * u - normal_part(u, 4.0, 1.0) - cross_part(v, 2.0, 1.0)
    image_v = node_drag * v - normal_part(v, 1.0, 4.0) - cross_part(u, 1.0, 2.0)
    return image_u, image_v


def chebyshev_pair(rhs_u, rhs_v, c, inv_u, inv_v):
    centre_value = 0.5 * (UPPER_BOUND + LOWER_BOUND)
    half_width = 0.5 * (UPPER_BOUND - LOWER_BOUND)
    ratio_value = centre_value / half_width
    weight_now = 1.0 / ratio_value
    res_u, res_v = rhs_u, rhs_v
    dir_u = inv_u * res_u / centre_value
    dir_v = inv_v * res_v / centre_value
    it_u = jnp.zeros_like(rhs_u)
    it_v = jnp.zeros_like(rhs_v)
    for sweep_no in range(SWEEPS + 1):
        it_u = it_u + dir_u
        it_v = it_v + dir_v
        if sweep_no < SWEEPS:
            img_u, img_v = stencil_pair(dir_u, dir_v, c)
            res_u = res_u - img_u
            res_v = res_v - img_v
            weight_next = 1.0 / (2.0 * ratio_value - weight_now)
            a = weight_next * weight_now
            b = 2.0 * weight_next / half_width
            dir_u = a * dir_u + b * (inv_u * res_u)
            dir_v = a * dir_v + b * (inv_v * res_v)
            weight_now = weight_next
    return it_u, it_v


def copy_in(pairs, sem):
    copies = [pltpu.make_async_copy(src, dst, sem.at[i]) for i, (src, dst) in enumerate(pairs)]
    for c in copies:
        c.start()
    return copies


def strip_sweep(dbuf, src, dst, res_ref, it_ref, coef_ref, a, b, strips):
    def strip(s, carry):
        r0 = pl.multiple_of(s * 8, 8)

        def rows_of(c):
            lo = dbuf[src, c, pl.ds(r0, 16), :]
            hi = dbuf[src, c, pl.ds(r0 + 8, 16), :]
            return hi[0:8], pltpu.roll(hi, 15, 0)[0:8], pltpu.roll(lo, 1, 0)[8:16]

        def cf(k):
            return coef_ref[k, pl.ds(r0, 8), :]

        north, south, east, west = cf(0), cf(1), cf(2), cf(3)
        face_np, face_sm, face_ep, face_wm, node_drag = cf(4), cf(5), cf(6), cf(7), cf(8)
        u, u_n, u_s = rows_of(0)
        v, v_n, v_s = rows_of(1)

        def normal_part(x, x_n, x_s, weight_rows, weight_cols):
            rows_part = face_np * (x_n - x) - face_sm * (x - x_s)
            cols_part = face_ep * (sh(x, 0, 1) - x) - face_wm * (x - sh(x, 0, -1))
            return weight_rows * rows_part + weight_cols * cols_part

        def cross_part(x, x_n, x_s, weight_rows, weight_cols):
            cols_n = 0.5 * (sh(x_n, 0, 1) - sh(x_n, 0, -1))
            cols_s = 0.5 * (sh(x_s, 0, 1) - sh(x_s, 0, -1))
            slope_rows = 0.5 * (x_n - x_s)
            first = 0.5 * weight_rows * (north * cols_n - south * cols_s)
            second = 0.5 * weight_cols * (east * sh(slope_rows, 0, 1) - west * sh(slope_rows, 0, -1))
            return first + second

        image_u = node_drag * u - normal_part(u, u_n, u_s, 4.0, 1.0) - cross_part(v, v_n, v_s, 2.0, 1.0)
        image_v = node_drag * v - normal_part(v, v_n, v_s, 1.0, 4.0) - cross_part(u, u_n, u_s, 1.0, 2.0)
        for c, (d, img) in enumerate([(u, image_u), (v, image_v)]):
            res = res_ref[c, pl.ds(r0, 8), :] - img
            res_ref[c, pl.ds(r0, 8), :] = res
            new = a * d + b * (cf(9 + c) * res)
            dbuf[dst, c, pl.ds(r0 + 8, 8), :] = new
            it_ref[c, pl.ds(r0, 8), :] = it_ref[c, pl.ds(r0, 8), :] + new
        return carry

    lax.fori_loop(0, strips, strip, 0)
    fill_pads(dbuf, dst, strips * 8)


def fill_pads(dbuf, k, rows):
    for c in range(dbuf.shape[1]):
        dbuf[k, c, 0:8] = dbuf[k, c, rows : rows + 8]
        dbuf[k, c, rows + 8 : rows + 16] = dbuf[k, c, 8:16]


def chebyshev_strips(rhs, dbuf, res_ref, it_ref, coef_ref):
    full_rows = res_ref.shape[1]
    centre_value = 0.5 * (UPPER_BOUND + LOWER_BOUND)
    half_width = 0.5 * (UPPER_BOUND - LOWER_BOUND)
    ratio_value = centre_value / half_width
    weight_now = 1.0 / ratio_value
    for c in range(2):
        res_ref[c] = rhs[c]
        direction = coef_ref[9 + c] * rhs[c] / centre_value
        dbuf[0, c, 8 : 8 + full_rows] = direction
        it_ref[c] = jnp.zeros_like(direction) + direction
    fill_pads(dbuf, 0, full_rows)
    for sweep_no in range(SWEEPS):
        weight_next = 1.0 / (2.0 * ratio_value - weight_now)
        a = weight_next * weight_now
        b = 2.0 * weight_next / half_width
        strip_sweep(dbuf, sweep_no % 2, (sweep_no + 1) % 2, res_ref, it_ref, coef_ref, a, b, full_rows // 8)
        weight_now = weight_next


def kernel(
    f_hbm, o_hbm, eta_hbm, fd_hbm, ice_hbm, ra_hbm, rb_hbm, ca_hbm, cb_hbm,
    vel_ref, grad_ref,
    f_ref, o_ref, eta_ref, fd_ref, ice_ref, ra_ref, rb_ref, ca_ref, cb_ref,
    field_ref, coef_ref, prod_ref, dbuf, res_ref, it_ref, vel_keep, sem,
):
    epochs, comps, rows, cols = f_ref.shape
    h = HALO
    n = epochs * comps
    copies = copy_in(
        [
            (eta_hbm, eta_ref), (fd_hbm, fd_ref), (ra_hbm, ra_ref), (rb_hbm, rb_ref),
            (ca_hbm, ca_ref), (cb_hbm, cb_ref), (f_hbm, f_ref), (o_hbm, o_ref), (ice_hbm, ice_ref),
        ],
        sem,
    )
    for k in range(field_ref.shape[0]):
        field_ref[k, :, cols + h : 2 * cols - h] = jnp.zeros((rows + 2 * h, cols - 2 * h), jnp.float32)
    for c in copies[:6]:
        c.wait()

    def assemble(dst, centre, p):
        dst[0:rows, 0:cols] = centre
        dst[rows : rows + h, 0:cols] = ra_ref[p]
        dst[rows + h : rows + 2 * h, 0:cols] = rb_ref[p]
        dst[:, cols : cols + h] = ca_ref[p].T[0 : rows + 2 * h, :]
        dst[:, 2 * cols - h :] = cb_ref[p].T[0 : rows + 2 * h, :]

    assemble(field_ref.at[0], eta_ref[...], 2 * n)
    assemble(field_ref.at[1], fd_ref[0], 2 * n + 1)
    assemble(field_ref.at[2], fd_ref[1], 2 * n + 2)
    eta = field_ref[0]
    free = field_ref[1]
    drag = field_ref[2]
    node_drag = 0.25 * (sh(drag, -1, -1) + sh(drag, 0, -1) + sh(drag, -1, 0) + drag)
    north = sh(eta, 1, 0)
    south = sh(eta, -1, 0)
    east = sh(eta, 0, 1)
    west = sh(eta, 0, -1)
    face_np = 0.5 * (eta + north)
    face_sm = 0.5 * (eta + south)
    face_ep = 0.5 * (eta + east)
    face_wm = 0.5 * (eta + west)
    rows_sum = face_np + face_sm
    cols_sum = face_ep + face_wm
    inv_u = free / (4.0 * rows_sum + cols_sum + node_drag + 1.0 - free)
    inv_v = free / (rows_sum + 4.0 * cols_sum + node_drag + 1.0 - free)
    for k, val in enumerate(
        [north, south, east, west, face_np, face_sm, face_ep, face_wm, node_drag, inv_u, inv_v, free]
    ):
        coef_ref[k] = val
    prod_ref[...] = jnp.zeros_like(prod_ref)
    for c in copies[6:]:
        c.wait()

    def epoch(e, carry):
        for comp in range(comps):
            p = e * comps + comp
            assemble(field_ref.at[3 + comp], f_ref[e, comp], p)
            assemble(field_ref.at[3 + comps + comp], o_ref[e, comp], n + p)
        free = coef_ref[11]
        chebyshev_strips([free * field_ref[3], free * field_ref[4]], dbuf, res_ref, it_ref, coef_ref)
        for c in range(comps):
            vel_keep[c] = it_ref[c]
            vel_ref[e, c] = it_ref[c, 0:rows, 0:cols]
        misfit = [free * (vel_keep[c] - field_ref[5 + c]) for c in range(comps)]
        chebyshev_strips(misfit, dbuf, res_ref, it_ref, coef_ref)
        prod_ref[...] += it_ref[0] * vel_keep[0] + it_ref[1] * vel_keep[1]
        return carry

    lax.fori_loop(0, epochs, epoch, 0)
    product = prod_ref[...]
    rows_sum = product + sh(product, 1, 0)
    total = rows_sum + sh(rows_sum, 0, 1)
    grounded = (ice_ref[...] == 2).astype(jnp.float32)
    grad_ref[...] = -0.25 * grounded * total[0:rows, 0:cols]


def prep_kernel(
    f_hbm, o_hbm, eta_hbm, fric_hbm, ice_hbm, dir_hbm,
    lo_hbm, hi_hbm, clo_hbm, chi_hbm, fd_hbm,
    f_ref, o_ref, eta_ref, fric_ref, ice_ref, dir_ref, lo_ref, hi_ref, clo_ref, chi_ref, fd_ref,
    sem, out_sem,
):
    epochs, comps, rows, cols = f_ref.shape
    h = HALO
    n = epochs * comps
    copies = copy_in(
        [
            (ice_hbm, ice_ref), (dir_hbm, dir_ref), (fric_hbm, fric_ref), (eta_hbm, eta_ref),
            (f_hbm, f_ref), (o_hbm, o_ref),
        ],
        sem,
    )
    for c in copies[:4]:
        c.wait()
    ice = ice_ref[...]
    free = (1 - dir_ref[...]).astype(jnp.float32)
    drag = jnp.where(ice == 2, fric_ref[...], jnp.where(ice == 0, FREE_DRAG, 0.0))
    fd_ref[0] = free
    fd_ref[1] = drag
    for c in copies[4:]:
        c.wait()
    planes = []
    for e in range(epochs):
        for comp in range(comps):
            planes.append(f_ref.at[e, comp])
    for e in range(epochs):
        for comp in range(comps):
            planes.append(o_ref.at[e, comp])
    for p, ref in enumerate(planes):
        lo_ref[p] = ref[0:h, :]
        hi_ref[p] = ref[rows - h : rows, :]
    for k, val in enumerate([eta_ref[...], free, drag]):
        lo_ref[2 * n + k] = val[0:h]
        hi_ref[2 * n + k] = val[rows - h : rows]
    out = copy_in([(lo_ref, lo_hbm), (hi_ref, hi_hbm), (fd_ref, fd_hbm)], out_sem)
    for p, ref in enumerate(planes):
        t = ref[...].T
        clo_ref[p] = t[0:h]
        chi_ref[p] = t[cols - h : cols]
    for k, val in enumerate([eta_ref[...], free, drag]):
        t = val.T
        clo_ref[2 * n + k] = t[0:h]
        chi_ref[2 * n + k] = t[cols - h : cols]
    out += copy_in([(clo_ref, clo_hbm), (chi_ref, chi_hbm)], out_sem.at[3:])
    for c in out:
        c.wait()


def scratch_like(*arrays):
    return [pltpu.VMEM(a.shape, a.dtype) for a in arrays]


def prep(forcing, observed, viscosity, friction, ice_mask, dirichlet):
    epochs, comps, rows, cols = forcing.shape
    planes = 2 * epochs * comps + 3
    hbm = pl.BlockSpec(memory_space=pltpu.HBM)
    slab = jax.ShapeDtypeStruct((planes, HALO, cols), jnp.float32)
    cslab = jax.ShapeDtypeStruct((planes, HALO, rows), jnp.float32)
    fd = jax.ShapeDtypeStruct((2, rows, cols), jnp.float32)
    outs = (slab, slab, cslab, cslab, fd)
    args = (forcing, observed, viscosity, friction, ice_mask, dirichlet)
    return pl.pallas_call(
        prep_kernel,
        out_shape=outs,
        in_specs=[hbm] * 6,
        out_specs=(hbm,) * 5,
        scratch_shapes=scratch_like(*args, *outs)
        + [pltpu.SemaphoreType.DMA((6,)), pltpu.SemaphoreType.DMA((5,))],
    )(*args)


def local_solve(forcing, observed, eta, fd, ice_mask, ra, rb, ca, cb):
    epochs, comps, rows, cols = forcing.shape
    full = (rows + 2 * HALO, 2 * cols)
    vmem = pl.BlockSpec(memory_space=pltpu.VMEM)
    anywhere = pl.BlockSpec(memory_space=pltpu.HBM)
    nodes = full[0] * full[1]
    args = (forcing, observed, eta, fd, ice_mask, ra, rb, ca, cb)
    return pl.pallas_call(
        kernel,
        out_shape=(
            jax.ShapeDtypeStruct(forcing.shape, jnp.float32),
            jax.ShapeDtypeStruct((rows, cols), jnp.float32),
        ),
        in_specs=[anywhere] * 9,
        out_specs=(vmem, vmem),
        scratch_shapes=scratch_like(*args)
        + [
            pltpu.VMEM((3 + 2 * comps,) + full, jnp.float32),
            pltpu.VMEM((12,) + full, jnp.float32),
            pltpu.VMEM(full, jnp.float32),
            pltpu.VMEM((2, comps, full[0] + 16, full[1]), jnp.float32),
            pltpu.VMEM((comps,) + full, jnp.float32),
            pltpu.VMEM((comps,) + full, jnp.float32),
            pltpu.VMEM((comps,) + full, jnp.float32),
            pltpu.SemaphoreType.DMA((9,)),
        ],
        cost_estimate=pl.CostEstimate(
            flops=epochs * 2 * SWEEPS * comps * 60 * nodes,
            bytes_accessed=4 * (3 * epochs * comps + 40) * rows * cols,
            transcendentals=0,
        ),
    )(*args)


def body(forcing, observed, viscosity, friction, ice_mask, dirichlet):
    epochs, comps, rows, cols = forcing.shape
    h = HALO
    lo, hi, clo, chi, fd = prep(forcing, observed, viscosity, friction, ice_mask, dirichlet)
    ra, rb = exchange(lo, hi, "gx")

    def corners(slab, a, b):
        edge = jnp.concatenate([ra[:, :, a:b], rb[:, :, a:b]], axis=1)
        gap = jnp.zeros((slab.shape[0], h, cols - rows - 2 * h), jnp.float32)
        return jnp.concatenate([slab, jnp.swapaxes(edge, 1, 2), gap], axis=2)

    ca, cb = exchange(corners(clo, 0, h), corners(chi, cols - h, cols), "gy")
    return local_solve(forcing, observed, viscosity, fd, ice_mask, ra, rb, ca, cb)


def solution(mesh):
    return jax.shard_map(
        body,
        mesh=mesh,
        in_specs=(
            P(None, None, "gx", "gy"),
            P(None, None, "gx", "gy"),
            P("gx", "gy"),
            P("gx", "gy"),
            P("gx", "gy"),
            P("gx", "gy"),
        ),
        out_specs=(P(None, None, "gx", "gy"), P("gx", "gy")),
        check_vma=False,
    )
```

```python
import functools

import jax
import jax.numpy as jnp
from jax import lax
from jax.experimental import pallas as pl
from jax.experimental.pallas import tpu as pltpu
from jax.sharding import PartitionSpec as P

SWEEPS = 3

UPPER_BOUND = 2.4
LOWER_BOUND = 0.05
FREE_DRAG = 4.0

HALO = 2 * SWEEPS + 2


def exchange(slab_low, slab_high, axis):
    size = lax.axis_size(axis)
    up = [(i, i + 1) for i in range(size - 1)]
    down = [(i + 1, i) for i in range(size - 1)]
    after = lax.ppermute(slab_low, axis, down)
    before = lax.ppermute(slab_high, axis, up)
    return after, before


def sh(x, di, dj):
    if di:
        x = pltpu.roll(x, (-di) % x.shape[0], 0)
    if dj:
        x = pltpu.roll(x, (-dj) % x.shape[1], 1)
    return x


def stencil_pair(u, v, c):
    north, south, east, west, face_np, face_sm, face_ep, face_wm, node_drag = c

    def normal_part(values, weight_rows, weight_cols):
        middle = values
        rows_part = face_np * (sh(values, 1, 0) - middle) - face_sm * (middle - sh(values, -1, 0))
        cols_part = face_ep * (sh(values, 0, 1) - middle) - face_wm * (middle - sh(values, 0, -1))
        return weight_rows * rows_part + weight_cols * cols_part

    def cross_part(values, weight_rows, weight_cols):
        slope_cols = 0.5 * (sh(values, 0, 1) - sh(values, 0, -1))
        slope_rows = 0.5 * (sh(values, 1, 0) - sh(values, -1, 0))
        first = 0.5 * weight_rows * (north * sh(slope_cols, 1, 0) - south * sh(slope_cols, -1, 0))
        second = 0.5 * weight_cols * (east * sh(slope_rows, 0, 1) - west * sh(slope_rows, 0, -1))
        return first + second

    image_u = node_drag * u - normal_part(u, 4.0, 1.0) - cross_part(v, 2.0, 1.0)
    image_v = node_drag * v - normal_part(v, 1.0, 4.0) - cross_part(u, 1.0, 2.0)
    return image_u, image_v


def chebyshev_pair(rhs_u, rhs_v, c, inv_u, inv_v):
    centre_value = 0.5 * (UPPER_BOUND + LOWER_BOUND)
    half_width = 0.5 * (UPPER_BOUND - LOWER_BOUND)
    ratio_value = centre_value / half_width
    weight_now = 1.0 / ratio_value
    res_u, res_v = rhs_u, rhs_v
    dir_u = inv_u * res_u / centre_value
    dir_v = inv_v * res_v / centre_value
    it_u = jnp.zeros_like(rhs_u)
    it_v = jnp.zeros_like(rhs_v)
    for sweep_no in range(SWEEPS + 1):
        it_u = it_u + dir_u
        it_v = it_v + dir_v
        if sweep_no < SWEEPS:
            img_u, img_v = stencil_pair(dir_u, dir_v, c)
            res_u = res_u - img_u
            res_v = res_v - img_v
            weight_next = 1.0 / (2.0 * ratio_value - weight_now)
            a = weight_next * weight_now
            b = 2.0 * weight_next / half_width
            dir_u = a * dir_u + b * (inv_u * res_u)
            dir_v = a * dir_v + b * (inv_v * res_v)
            weight_now = weight_next
    return it_u, it_v


def copy_in(pairs, sem):
    copies = [pltpu.make_async_copy(src, dst, sem.at[i]) for i, (src, dst) in enumerate(pairs)]
    for c in copies:
        c.start()
    return copies


def kernel(
    f_hbm, o_hbm, eta_hbm, fd_hbm, ice_hbm, ra_hbm, rb_hbm, ca_hbm, cb_hbm,
    vel_ref, grad_ref,
    f_ref, o_ref, eta_ref, fd_ref, ice_ref, ra_ref, rb_ref, ca_ref, cb_ref,
    field_ref, coef_ref, prod_ref, sem,
):
    epochs, comps, rows, cols = f_ref.shape
    h = HALO
    n = epochs * comps
    copies = copy_in(
        [
            (eta_hbm, eta_ref), (fd_hbm, fd_ref), (ra_hbm, ra_ref), (rb_hbm, rb_ref),
            (ca_hbm, ca_ref), (cb_hbm, cb_ref), (f_hbm, f_ref), (o_hbm, o_ref), (ice_hbm, ice_ref),
        ],
        sem,
    )
    for k in range(field_ref.shape[0]):
        field_ref[k, :, cols + h : 2 * cols - h] = jnp.zeros((rows + 2 * h, cols - 2 * h), jnp.float32)
    for c in copies[:6]:
        c.wait()

    def assemble(dst, centre, p):
        dst[0:rows, 0:cols] = centre
        dst[rows : rows + h, 0:cols] = ra_ref[p]
        dst[rows + h : rows + 2 * h, 0:cols] = rb_ref[p]
        dst[:, cols : cols + h] = ca_ref[p].T[0 : rows + 2 * h, :]
        dst[:, 2 * cols - h :] = cb_ref[p].T[0 : rows + 2 * h, :]

    assemble(field_ref.at[0], eta_ref[...], 2 * n)
    assemble(field_ref.at[1], fd_ref[0], 2 * n + 1)
    assemble(field_ref.at[2], fd_ref[1], 2 * n + 2)
    eta = field_ref[0]
    free = field_ref[1]
    drag = field_ref[2]
    node_drag = 0.25 * (sh(drag, -1, -1) + sh(drag, 0, -1) + sh(drag, -1, 0) + drag)
    north = sh(eta, 1, 0)
    south = sh(eta, -1, 0)
    east = sh(eta, 0, 1)
    west = sh(eta, 0, -1)
    face_np = 0.5 * (eta + north)
    face_sm = 0.5 * (eta + south)
    face_ep = 0.5 * (eta + east)
    face_wm = 0.5 * (eta + west)
    rows_sum = face_np + face_sm
    cols_sum = face_ep + face_wm
    inv_u = free / (4.0 * rows_sum + cols_sum + node_drag + 1.0 - free)
    inv_v = free / (rows_sum + 4.0 * cols_sum + node_drag + 1.0 - free)
    for k, val in enumerate(
        [north, south, east, west, face_np, face_sm, face_ep, face_wm, node_drag, inv_u, inv_v, free]
    ):
        coef_ref[k] = val
    prod_ref[...] = jnp.zeros_like(prod_ref)
    for c in copies[6:]:
        c.wait()

    def epoch(e, carry):
        for comp in range(comps):
            p = e * comps + comp
            assemble(field_ref.at[3 + comp], f_ref[e, comp], p)
            assemble(field_ref.at[3 + comps + comp], o_ref[e, comp], n + p)
        c = tuple(coef_ref[k] for k in range(9))
        inv_u = coef_ref[9]
        inv_v = coef_ref[10]
        free = coef_ref[11]
        vel_u, vel_v = chebyshev_pair(free * field_ref[3], free * field_ref[4], c, inv_u, inv_v)
        vel_ref[e, 0] = vel_u[0:rows, 0:cols]
        vel_ref[e, 1] = vel_v[0:rows, 0:cols]
        mis_u = free * (vel_u - field_ref[5])
        mis_v = free * (vel_v - field_ref[6])
        adj_u, adj_v = chebyshev_pair(mis_u, mis_v, c, inv_u, inv_v)
        prod_ref[...] += adj_u * vel_u + adj_v * vel_v
        return carry

    for e in range(epochs):
        epoch(e, 0)
    product = prod_ref[...]
    rows_sum = product + sh(product, 1, 0)
    total = rows_sum + sh(rows_sum, 0, 1)
    grounded = (ice_ref[...] == 2).astype(jnp.float32)
    grad_ref[...] = -0.25 * grounded * total[0:rows, 0:cols]


def prep_kernel(
    f_hbm, o_hbm, eta_hbm, fric_hbm, ice_hbm, dir_hbm,
    lo_hbm, hi_hbm, clo_hbm, chi_hbm, fd_hbm,
    f_ref, o_ref, eta_ref, fric_ref, ice_ref, dir_ref, lo_ref, hi_ref, clo_ref, chi_ref, fd_ref,
    sem, out_sem,
):
    epochs, comps, rows, cols = f_ref.shape
    h = HALO
    n = epochs * comps
    copies = copy_in(
        [
            (ice_hbm, ice_ref), (dir_hbm, dir_ref), (fric_hbm, fric_ref), (eta_hbm, eta_ref),
            (f_hbm, f_ref), (o_hbm, o_ref),
        ],
        sem,
    )
    for c in copies[:4]:
        c.wait()
    ice = ice_ref[...]
    free = (1 - dir_ref[...]).astype(jnp.float32)
    drag = jnp.where(ice == 2, fric_ref[...], jnp.where(ice == 0, FREE_DRAG, 0.0))
    fd_ref[0] = free
    fd_ref[1] = drag
    for c in copies[4:]:
        c.wait()
    planes = []
    for e in range(epochs):
        for comp in range(comps):
            planes.append(f_ref.at[e, comp])
    for e in range(epochs):
        for comp in range(comps):
            planes.append(o_ref.at[e, comp])
    for p, ref in enumerate(planes):
        lo_ref[p] = ref[0:h, :]
        hi_ref[p] = ref[rows - h : rows, :]
    for k, val in enumerate([eta_ref[...], free, drag]):
        lo_ref[2 * n + k] = val[0:h]
        hi_ref[2 * n + k] = val[rows - h : rows]
    out = copy_in([(lo_ref, lo_hbm), (hi_ref, hi_hbm), (fd_ref, fd_hbm)], out_sem)
    for p, ref in enumerate(planes):
        t = ref[...].T
        clo_ref[p] = t[0:h]
        chi_ref[p] = t[cols - h : cols]
    for k, val in enumerate([eta_ref[...], free, drag]):
        t = val.T
        clo_ref[2 * n + k] = t[0:h]
        chi_ref[2 * n + k] = t[cols - h : cols]
    out += copy_in([(clo_ref, clo_hbm), (chi_ref, chi_hbm)], out_sem.at[3:])
    for c in out:
        c.wait()


def scratch_like(*arrays):
    return [pltpu.VMEM(a.shape, a.dtype) for a in arrays]


def prep(forcing, observed, viscosity, friction, ice_mask, dirichlet):
    epochs, comps, rows, cols = forcing.shape
    planes = 2 * epochs * comps + 3
    hbm = pl.BlockSpec(memory_space=pltpu.HBM)
    slab = jax.ShapeDtypeStruct((planes, HALO, cols), jnp.float32)
    cslab = jax.ShapeDtypeStruct((planes, HALO, rows), jnp.float32)
    fd = jax.ShapeDtypeStruct((2, rows, cols), jnp.float32)
    outs = (slab, slab, cslab, cslab, fd)
    args = (forcing, observed, viscosity, friction, ice_mask, dirichlet)
    return pl.pallas_call(
        prep_kernel,
        out_shape=outs,
        in_specs=[hbm] * 6,
        out_specs=(hbm,) * 5,
        scratch_shapes=scratch_like(*args, *outs)
        + [pltpu.SemaphoreType.DMA((6,)), pltpu.SemaphoreType.DMA((5,))],
    )(*args)


def local_solve(forcing, observed, eta, fd, ice_mask, ra, rb, ca, cb):
    epochs, comps, rows, cols = forcing.shape
    full = (rows + 2 * HALO, 2 * cols)
    vmem = pl.BlockSpec(memory_space=pltpu.VMEM)
    anywhere = pl.BlockSpec(memory_space=pltpu.HBM)
    nodes = full[0] * full[1]
    args = (forcing, observed, eta, fd, ice_mask, ra, rb, ca, cb)
    return pl.pallas_call(
        kernel,
        out_shape=(
            jax.ShapeDtypeStruct(forcing.shape, jnp.float32),
            jax.ShapeDtypeStruct((rows, cols), jnp.float32),
        ),
        in_specs=[anywhere] * 9,
        out_specs=(vmem, vmem),
        scratch_shapes=scratch_like(*args)
        + [
            pltpu.VMEM((3 + 2 * comps,) + full, jnp.float32),
            pltpu.VMEM((12,) + full, jnp.float32),
            pltpu.VMEM(full, jnp.float32),
            pltpu.SemaphoreType.DMA((9,)),
        ],
        cost_estimate=pl.CostEstimate(
            flops=epochs * 2 * SWEEPS * comps * 60 * nodes,
            bytes_accessed=4 * (3 * epochs * comps + 40) * rows * cols,
            transcendentals=0,
        ),
    )(*args)


def body(forcing, observed, viscosity, friction, ice_mask, dirichlet):
    epochs, comps, rows, cols = forcing.shape
    h = HALO
    lo, hi, clo, chi, fd = prep(forcing, observed, viscosity, friction, ice_mask, dirichlet)
    ra, rb = exchange(lo, hi, "gx")

    def corners(slab, a, b):
        edge = jnp.concatenate([ra[:, :, a:b], rb[:, :, a:b]], axis=1)
        gap = jnp.zeros((slab.shape[0], h, cols - rows - 2 * h), jnp.float32)
        return jnp.concatenate([slab, jnp.swapaxes(edge, 1, 2), gap], axis=2)

    ca, cb = exchange(corners(clo, 0, h), corners(chi, cols - h, cols), "gy")
    return local_solve(forcing, observed, viscosity, fd, ice_mask, ra, rb, ca, cb)


def solution(mesh):
    return jax.shard_map(
        body,
        mesh=mesh,
        in_specs=(
            P(None, None, "gx", "gy"),
            P(None, None, "gx", "gy"),
            P("gx", "gy"),
            P("gx", "gy"),
            P("gx", "gy"),
            P("gx", "gy"),
        ),
        out_specs=(P(None, None, "gx", "gy"), P("gx", "gy")),
        check_vma=False,
    )
```

```python
import functools

import jax
import jax.numpy as jnp
from jax import lax
from jax.experimental import pallas as pl
from jax.experimental.pallas import tpu as pltpu
from jax.sharding import PartitionSpec as P

SWEEPS = 3

UPPER_BOUND = 2.4
LOWER_BOUND = 0.05
FREE_DRAG = 4.0

HALO = 2 * SWEEPS + 2


def exchange(slab_low, slab_high, axis):
    size = lax.axis_size(axis)
    up = [(i, i + 1) for i in range(size - 1)]
    down = [(i + 1, i) for i in range(size - 1)]
    after = lax.ppermute(slab_low, axis, down)
    before = lax.ppermute(slab_high, axis, up)
    return after, before


def sh(x, di, dj):
    if di:
        x = pltpu.roll(x, (-di) % x.shape[0], 0)
    if dj:
        x = pltpu.roll(x, (-dj) % x.shape[1], 1)
    return x


def stencil_pair(u, v, c):
    (face_np, face_sm, face_ep, face_wm, face_np4, face_sm4, face_ep4, face_wm4, node_drag,
     north_u, south_u, east_u, west_u, north_v, south_v, east_v, west_v) = c

    def normal_part(values, fn, fs, fe, fw):
        middle = values
        rows_part = fn * (sh(values, 1, 0) - middle) - fs * (middle - sh(values, -1, 0))
        cols_part = fe * (sh(values, 0, 1) - middle) - fw * (middle - sh(values, 0, -1))
        return rows_part + cols_part

    def cross_part(values, n, s, e, w):
        across = sh(values, 0, 1) - sh(values, 0, -1)
        along = sh(values, 1, 0) - sh(values, -1, 0)
        first = n * sh(across, 1, 0) - s * sh(across, -1, 0)
        second = e * sh(along, 0, 1) - w * sh(along, 0, -1)
        return first + second

    image_u = (
        node_drag * u
        - normal_part(u, face_np4, face_sm4, face_ep, face_wm)
        - cross_part(v, north_u, south_u, east_u, west_u)
    )
    image_v = (
        node_drag * v
        - normal_part(v, face_np, face_sm, face_ep4, face_wm4)
        - cross_part(u, north_v, south_v, east_v, west_v)
    )
    return image_u, image_v


def chebyshev_pair(rhs_u, rhs_v, c, inv_u, inv_v):
    centre_value = 0.5 * (UPPER_BOUND + LOWER_BOUND)
    half_width = 0.5 * (UPPER_BOUND - LOWER_BOUND)
    ratio_value = centre_value / half_width
    weight_now = 1.0 / ratio_value
    res_u, res_v = rhs_u, rhs_v
    dir_u = inv_u * res_u / centre_value
    dir_v = inv_v * res_v / centre_value
    it_u = jnp.zeros_like(rhs_u)
    it_v = jnp.zeros_like(rhs_v)
    for sweep_no in range(SWEEPS + 1):
        it_u = it_u + dir_u
        it_v = it_v + dir_v
        if sweep_no < SWEEPS:
            img_u, img_v = stencil_pair(dir_u, dir_v, c)
            res_u = res_u - img_u
            res_v = res_v - img_v
            weight_next = 1.0 / (2.0 * ratio_value - weight_now)
            a = weight_next * weight_now
            b = 2.0 * weight_next / half_width
            dir_u = a * dir_u + b * (inv_u * res_u)
            dir_v = a * dir_v + b * (inv_v * res_v)
            weight_now = weight_next
    return it_u, it_v


def copy_in(pairs, sem):
    copies = [pltpu.make_async_copy(src, dst, sem.at[i]) for i, (src, dst) in enumerate(pairs)]
    for c in copies:
        c.start()
    return copies


def kernel(
    f_hbm, o_hbm, eta_hbm, fd_hbm, ice_hbm, ra_hbm, rb_hbm, ca_hbm, cb_hbm,
    vel_ref, grad_ref,
    f_ref, o_ref, eta_ref, fd_ref, ice_ref, ra_ref, rb_ref, ca_ref, cb_ref,
    field_ref, coef_ref, prod_ref, sem,
):
    epochs, comps, rows, cols = f_ref.shape
    h = HALO
    n = epochs * comps
    copies = copy_in(
        [
            (eta_hbm, eta_ref), (fd_hbm, fd_ref), (ra_hbm, ra_ref), (rb_hbm, rb_ref),
            (ca_hbm, ca_ref), (cb_hbm, cb_ref), (f_hbm, f_ref), (o_hbm, o_ref), (ice_hbm, ice_ref),
        ],
        sem,
    )
    for k in range(field_ref.shape[0]):
        field_ref[k, :, cols + h : 2 * cols - h] = jnp.zeros((rows + 2 * h, cols - 2 * h), jnp.float32)
    for c in copies[:6]:
        c.wait()

    def assemble(dst, centre, p):
        dst[0:rows, 0:cols] = centre
        dst[rows : rows + h, 0:cols] = ra_ref[p]
        dst[rows + h : rows + 2 * h, 0:cols] = rb_ref[p]
        dst[:, cols : cols + h] = ca_ref[p].T[0 : rows + 2 * h, :]
        dst[:, 2 * cols - h :] = cb_ref[p].T[0 : rows + 2 * h, :]

    assemble(field_ref.at[0], eta_ref[...], 2 * n)
    assemble(field_ref.at[1], fd_ref[0], 2 * n + 1)
    assemble(field_ref.at[2], fd_ref[1], 2 * n + 2)
    eta = field_ref[0]
    free = field_ref[1]
    drag = field_ref[2]
    node_drag = 0.25 * (sh(drag, -1, -1) + sh(drag, 0, -1) + sh(drag, -1, 0) + drag)
    north = sh(eta, 1, 0)
    south = sh(eta, -1, 0)
    east = sh(eta, 0, 1)
    west = sh(eta, 0, -1)
    face_np = 0.5 * (eta + north)
    face_sm = 0.5 * (eta + south)
    face_ep = 0.5 * (eta + east)
    face_wm = 0.5 * (eta + west)
    rows_sum = face_np + face_sm
    cols_sum = face_ep + face_wm
    inv_u = free / (4.0 * rows_sum + cols_sum + node_drag + 1.0 - free)
    inv_v = free / (rows_sum + 4.0 * cols_sum + node_drag + 1.0 - free)
    coefs = [face_np, face_sm, face_ep, face_wm]
    coefs += [4.0 * face_np, 4.0 * face_sm, 4.0 * face_ep, 4.0 * face_wm, node_drag]
    coefs += [0.5 * north, 0.5 * south, 0.25 * east, 0.25 * west]
    coefs += [0.25 * north, 0.25 * south, 0.5 * east, 0.5 * west]
    for k, val in enumerate(coefs + [inv_u, inv_v, free]):
        coef_ref[k] = val
    prod_ref[...] = jnp.zeros_like(prod_ref)
    for c in copies[6:]:
        c.wait()

    def epoch(e, carry):
        for comp in range(comps):
            p = e * comps + comp
            assemble(field_ref.at[3 + comp], f_ref[e, comp], p)
            assemble(field_ref.at[3 + comps + comp], o_ref[e, comp], n + p)
        c = tuple(coef_ref[k] for k in range(17))
        inv_u = coef_ref[17]
        inv_v = coef_ref[18]
        free = coef_ref[19]
        vel_u, vel_v = chebyshev_pair(free * field_ref[3], free * field_ref[4], c, inv_u, inv_v)
        vel_ref[e, 0] = vel_u[0:rows, 0:cols]
        vel_ref[e, 1] = vel_v[0:rows, 0:cols]
        mis_u = free * (vel_u - field_ref[5])
        mis_v = free * (vel_v - field_ref[6])
        adj_u, adj_v = chebyshev_pair(mis_u, mis_v, c, inv_u, inv_v)
        prod_ref[...] += adj_u * vel_u + adj_v * vel_v
        return carry

    lax.fori_loop(0, epochs, epoch, 0)
    product = prod_ref[...]
    rows_sum = product + sh(product, 1, 0)
    total = rows_sum + sh(rows_sum, 0, 1)
    grounded = (ice_ref[...] == 2).astype(jnp.float32)
    grad_ref[...] = -0.25 * grounded * total[0:rows, 0:cols]


def prep_kernel(
    f_hbm, o_hbm, eta_hbm, fric_hbm, ice_hbm, dir_hbm,
    lo_hbm, hi_hbm, clo_hbm, chi_hbm, fd_hbm,
    f_ref, o_ref, eta_ref, fric_ref, ice_ref, dir_ref, lo_ref, hi_ref, clo_ref, chi_ref, fd_ref,
    sem, out_sem,
):
    epochs, comps, rows, cols = f_ref.shape
    h = HALO
    n = epochs * comps
    copies = copy_in(
        [
            (ice_hbm, ice_ref), (dir_hbm, dir_ref), (fric_hbm, fric_ref), (eta_hbm, eta_ref),
            (f_hbm, f_ref), (o_hbm, o_ref),
        ],
        sem,
    )
    for c in copies[:4]:
        c.wait()
    ice = ice_ref[...]
    free = (1 - dir_ref[...]).astype(jnp.float32)
    drag = jnp.where(ice == 2, fric_ref[...], jnp.where(ice == 0, FREE_DRAG, 0.0))
    fd_ref[0] = free
    fd_ref[1] = drag
    for c in copies[4:]:
        c.wait()
    planes = []
    for e in range(epochs):
        for comp in range(comps):
            planes.append(f_ref.at[e, comp])
    for e in range(epochs):
        for comp in range(comps):
            planes.append(o_ref.at[e, comp])
    for p, ref in enumerate(planes):
        lo_ref[p] = ref[0:h, :]
        hi_ref[p] = ref[rows - h : rows, :]
    for k, val in enumerate([eta_ref[...], free, drag]):
        lo_ref[2 * n + k] = val[0:h]
        hi_ref[2 * n + k] = val[rows - h : rows]
    out = copy_in([(lo_ref, lo_hbm), (hi_ref, hi_hbm), (fd_ref, fd_hbm)], out_sem)
    for p, ref in enumerate(planes):
        t = ref[...].T
        clo_ref[p] = t[0:h]
        chi_ref[p] = t[cols - h : cols]
    for k, val in enumerate([eta_ref[...], free, drag]):
        t = val.T
        clo_ref[2 * n + k] = t[0:h]
        chi_ref[2 * n + k] = t[cols - h : cols]
    out += copy_in([(clo_ref, clo_hbm), (chi_ref, chi_hbm)], out_sem.at[3:])
    for c in out:
        c.wait()


def scratch_like(*arrays):
    return [pltpu.VMEM(a.shape, a.dtype) for a in arrays]


def prep(forcing, observed, viscosity, friction, ice_mask, dirichlet):
    epochs, comps, rows, cols = forcing.shape
    planes = 2 * epochs * comps + 3
    hbm = pl.BlockSpec(memory_space=pltpu.HBM)
    slab = jax.ShapeDtypeStruct((planes, HALO, cols), jnp.float32)
    cslab = jax.ShapeDtypeStruct((planes, HALO, rows), jnp.float32)
    fd = jax.ShapeDtypeStruct((2, rows, cols), jnp.float32)
    outs = (slab, slab, cslab, cslab, fd)
    args = (forcing, observed, viscosity, friction, ice_mask, dirichlet)
    return pl.pallas_call(
        prep_kernel,
        out_shape=outs,
        in_specs=[hbm] * 6,
        out_specs=(hbm,) * 5,
        scratch_shapes=scratch_like(*args, *outs)
        + [pltpu.SemaphoreType.DMA((6,)), pltpu.SemaphoreType.DMA((5,))],
    )(*args)


def local_solve(forcing, observed, eta, fd, ice_mask, ra, rb, ca, cb):
    epochs, comps, rows, cols = forcing.shape
    full = (rows + 2 * HALO, 2 * cols)
    vmem = pl.BlockSpec(memory_space=pltpu.VMEM)
    anywhere = pl.BlockSpec(memory_space=pltpu.HBM)
    nodes = full[0] * full[1]
    args = (forcing, observed, eta, fd, ice_mask, ra, rb, ca, cb)
    return pl.pallas_call(
        kernel,
        out_shape=(
            jax.ShapeDtypeStruct(forcing.shape, jnp.float32),
            jax.ShapeDtypeStruct((rows, cols), jnp.float32),
        ),
        in_specs=[anywhere] * 9,
        out_specs=(vmem, vmem),
        scratch_shapes=scratch_like(*args)
        + [
            pltpu.VMEM((3 + 2 * comps,) + full, jnp.float32),
            pltpu.VMEM((20,) + full, jnp.float32),
            pltpu.VMEM(full, jnp.float32),
            pltpu.SemaphoreType.DMA((9,)),
        ],
        cost_estimate=pl.CostEstimate(
            flops=epochs * 2 * SWEEPS * comps * 60 * nodes,
            bytes_accessed=4 * (3 * epochs * comps + 40) * rows * cols,
            transcendentals=0,
        ),
    )(*args)


def body(forcing, observed, viscosity, friction, ice_mask, dirichlet):
    epochs, comps, rows, cols = forcing.shape
    h = HALO
    lo, hi, clo, chi, fd = prep(forcing, observed, viscosity, friction, ice_mask, dirichlet)
    ra, rb = exchange(lo, hi, "gx")

    def corners(slab, a, b):
        edge = jnp.concatenate([ra[:, :, a:b], rb[:, :, a:b]], axis=1)
        gap = jnp.zeros((slab.shape[0], h, cols - rows - 2 * h), jnp.float32)
        return jnp.concatenate([slab, jnp.swapaxes(edge, 1, 2), gap], axis=2)

    ca, cb = exchange(corners(clo, 0, h), corners(chi, cols - h, cols), "gy")
    return local_solve(forcing, observed, viscosity, fd, ice_mask, ra, rb, ca, cb)


def solution(mesh):
    return jax.shard_map(
        body,
        mesh=mesh,
        in_specs=(
            P(None, None, "gx", "gy"),
            P(None, None, "gx", "gy"),
            P("gx", "gy"),
            P("gx", "gy"),
            P("gx", "gy"),
            P("gx", "gy"),
        ),
        out_specs=(P(None, None, "gx", "gy"), P("gx", "gy")),
        check_vma=False,
    )
```

```python
import functools

import jax
import jax.numpy as jnp
from jax import lax
from jax.experimental import pallas as pl
from jax.experimental.pallas import tpu as pltpu
from jax.sharding import PartitionSpec as P

SWEEPS = 3

UPPER_BOUND = 2.4
LOWER_BOUND = 0.05
FREE_DRAG = 4.0

HALO = 2 * SWEEPS + 2


def exchange(slab_low, slab_high, axis):
    size = lax.axis_size(axis)
    up = [(i, i + 1) for i in range(size - 1)]
    down = [(i + 1, i) for i in range(size - 1)]
    after = lax.ppermute(slab_low, axis, down)
    before = lax.ppermute(slab_high, axis, up)
    return after, before


def sh(x, di, dj):
    if di:
        x = pltpu.roll(x, (-di) % x.shape[0], 0)
    if dj:
        x = pltpu.roll(x, (-dj) % x.shape[1], 1)
    return x


def stencil_pair(u, v, c):
    (face_np, face_sm, face_ep, face_wm, face_np4, face_sm4, face_ep4, face_wm4, node_drag,
     north_u, south_u, east_u, west_u, north_v, south_v, east_v, west_v) = c

    def normal_part(values, fn, fs, fe, fw):
        middle = values
        rows_part = fn * (sh(values, 1, 0) - middle) - fs * (middle - sh(values, -1, 0))
        cols_part = fe * (sh(values, 0, 1) - middle) - fw * (middle - sh(values, 0, -1))
        return rows_part + cols_part

    def cross_part(values, n, s, e, w):
        across = sh(values, 0, 1) - sh(values, 0, -1)
        along = sh(values, 1, 0) - sh(values, -1, 0)
        first = n * sh(across, 1, 0) - s * sh(across, -1, 0)
        second = e * sh(along, 0, 1) - w * sh(along, 0, -1)
        return first + second

    image_u = (
        node_drag * u
        - normal_part(u, face_np4, face_sm4, face_ep, face_wm)
        - cross_part(v, north_u, south_u, east_u, west_u)
    )
    image_v = (
        node_drag * v
        - normal_part(v, face_np, face_sm, face_ep4, face_wm4)
        - cross_part(u, north_v, south_v, east_v, west_v)
    )
    return image_u, image_v


def chebyshev_pair(rhs_u, rhs_v, c, inv_u, inv_v):
    centre_value = 0.5 * (UPPER_BOUND + LOWER_BOUND)
    half_width = 0.5 * (UPPER_BOUND - LOWER_BOUND)
    ratio_value = centre_value / half_width
    weight_now = 1.0 / ratio_value
    res_u, res_v = rhs_u, rhs_v
    dir_u = inv_u * res_u / centre_value
    dir_v = inv_v * res_v / centre_value
    it_u = jnp.zeros_like(rhs_u)
    it_v = jnp.zeros_like(rhs_v)
    for sweep_no in range(SWEEPS + 1):
        it_u = it_u + dir_u
        it_v = it_v + dir_v
        if sweep_no < SWEEPS:
            img_u, img_v = stencil_pair(dir_u, dir_v, c)
            res_u = res_u - img_u
            res_v = res_v - img_v
            weight_next = 1.0 / (2.0 * ratio_value - weight_now)
            a = weight_next * weight_now
            b = 2.0 * weight_next / half_width
            dir_u = a * dir_u + b * (inv_u * res_u)
            dir_v = a * dir_v + b * (inv_v * res_v)
            weight_now = weight_next
    return it_u, it_v


def copy_in(pairs, sem):
    copies = [pltpu.make_async_copy(src, dst, sem.at[i]) for i, (src, dst) in enumerate(pairs)]
    for c in copies:
        c.start()
    return copies


def kernel(
    f_hbm, o_hbm, eta_hbm, fd_hbm, ice_hbm, ra_hbm, rb_hbm, ca_hbm, cb_hbm,
    vel_ref, grad_ref,
    f_ref, o_ref, eta_ref, fd_ref, ice_ref, ra_ref, rb_ref, ca_ref, cb_ref,
    field_ref, coef_ref, prod_ref, sem,
):
    epochs, comps, rows, cols = f_ref.shape
    h = HALO
    n = epochs * comps
    copies = copy_in(
        [
            (eta_hbm, eta_ref), (fd_hbm, fd_ref), (ra_hbm, ra_ref), (rb_hbm, rb_ref),
            (ca_hbm, ca_ref), (cb_hbm, cb_ref), (f_hbm, f_ref), (o_hbm, o_ref), (ice_hbm, ice_ref),
        ],
        sem,
    )
    for k in range(field_ref.shape[0]):
        field_ref[k, :, cols + h : 2 * cols - h] = jnp.zeros((rows + 2 * h, cols - 2 * h), jnp.float32)
    for c in copies[:6]:
        c.wait()

    def assemble(dst, centre, p):
        dst[0:rows, 0:cols] = centre
        dst[rows : rows + h, 0:cols] = ra_ref[p]
        dst[rows + h : rows + 2 * h, 0:cols] = rb_ref[p]
        dst[:, cols : cols + h] = ca_ref[p].T[0 : rows + 2 * h, :]
        dst[:, 2 * cols - h :] = cb_ref[p].T[0 : rows + 2 * h, :]

    assemble(field_ref.at[0], eta_ref[...], 2 * n)
    assemble(field_ref.at[1], fd_ref[0], 2 * n + 1)
    assemble(field_ref.at[2], fd_ref[1], 2 * n + 2)
    eta = field_ref[0]
    free = field_ref[1]
    drag = field_ref[2]
    node_drag = 0.25 * (sh(drag, -1, -1) + sh(drag, 0, -1) + sh(drag, -1, 0) + drag)
    north = sh(eta, 1, 0)
    south = sh(eta, -1, 0)
    east = sh(eta, 0, 1)
    west = sh(eta, 0, -1)
    face_np = 0.5 * (eta + north)
    face_sm = 0.5 * (eta + south)
    face_ep = 0.5 * (eta + east)
    face_wm = 0.5 * (eta + west)
    rows_sum = face_np + face_sm
    cols_sum = face_ep + face_wm
    inv_u = free / (4.0 * rows_sum + cols_sum + node_drag + 1.0 - free)
    inv_v = free / (rows_sum + 4.0 * cols_sum + node_drag + 1.0 - free)
    coefs = [face_np, face_sm, face_ep, face_wm]
    coefs += [4.0 * face_np, 4.0 * face_sm, 4.0 * face_ep, 4.0 * face_wm, node_drag]
    coefs += [0.5 * north, 0.5 * south, 0.25 * east, 0.25 * west]
    coefs += [0.25 * north, 0.25 * south, 0.5 * east, 0.5 * west]
    for k, val in enumerate(coefs + [inv_u, inv_v, free]):
        coef_ref[k] = val
    prod_ref[...] = jnp.zeros_like(prod_ref)
    for c in copies[6:]:
        c.wait()

    def epoch(e, carry):
        for comp in range(comps):
            p = e * comps + comp
            assemble(field_ref.at[3 + comp], f_ref[e, comp], p)
            assemble(field_ref.at[3 + comps + comp], o_ref[e, comp], n + p)
        c = tuple(coef_ref[k] for k in range(17))
        inv_u = coef_ref[17]
        inv_v = coef_ref[18]
        free = coef_ref[19]
        vel_u, vel_v = chebyshev_pair(free * field_ref[3], free * field_ref[4], c, inv_u, inv_v)
        vel_ref[e, 0] = vel_u[0:rows, 0:cols]
        vel_ref[e, 1] = vel_v[0:rows, 0:cols]
        mis_u = free * (vel_u - field_ref[5])
        mis_v = free * (vel_v - field_ref[6])
        adj_u, adj_v = chebyshev_pair(mis_u, mis_v, c, inv_u, inv_v)
        prod_ref[...] += adj_u * vel_u + adj_v * vel_v
        return carry

    lax.fori_loop(0, epochs, epoch, 0)
    product = prod_ref[...]
    rows_sum = product + sh(product, 1, 0)
    total = rows_sum + sh(rows_sum, 0, 1)
    grounded = (ice_ref[...] == 2).astype(jnp.float32)
    grad_ref[...] = -0.25 * grounded * total[0:rows, 0:cols]


def prep_kernel(
    f_hbm, o_hbm, eta_hbm, fric_hbm, ice_hbm, dir_hbm,
    lo_hbm, hi_hbm, fd_hbm,
    f_ref, o_ref, eta_ref, fric_ref, ice_ref, dir_ref, lo_ref, hi_ref, fd_ref,
    sem, out_sem,
):
    epochs, comps, rows, cols = f_ref.shape
    h = HALO
    n = epochs * comps
    copies = []
    for k, (src, dst) in enumerate([(f_hbm, f_ref), (o_hbm, o_ref)]):
        for j, (a, b) in enumerate([(0, h), (rows - h, rows)]):
            copies.append(
                pltpu.make_async_copy(
                    src.at[:, :, a:b], dst.at[:, :, a:b], sem.at[6 + 2 * k + j]
                )
            )
            copies[-1].start()
    copies += copy_in(
        [(ice_hbm, ice_ref), (dir_hbm, dir_ref), (fric_hbm, fric_ref), (eta_hbm, eta_ref)], sem
    )
    for c in copies[4:]:
        c.wait()
    ice = ice_ref[...]
    free = (1 - dir_ref[...]).astype(jnp.float32)
    drag = jnp.where(ice == 2, fric_ref[...], jnp.where(ice == 0, FREE_DRAG, 0.0))
    fd_ref[0] = free
    fd_ref[1] = drag
    for k, val in enumerate([eta_ref[...], free, drag]):
        lo_ref[2 * n + k] = val[0:h]
        hi_ref[2 * n + k] = val[rows - h : rows]
    for c in copies[:4]:
        c.wait()
    for e in range(epochs):
        for comp in range(comps):
            p = e * comps + comp
            lo_ref[p] = f_ref[e, comp, 0:h, :]
            hi_ref[p] = f_ref[e, comp, rows - h : rows, :]
            lo_ref[n + p] = o_ref[e, comp, 0:h, :]
            hi_ref[n + p] = o_ref[e, comp, rows - h : rows, :]
    out = copy_in([(lo_ref, lo_hbm), (hi_ref, hi_hbm), (fd_ref, fd_hbm)], out_sem)
    for c in out:
        c.wait()


def columns_kernel(
    f_hbm, o_hbm, eta_hbm, fd_hbm, clo_ref, chi_ref, f_ref, o_ref, eta_ref, fd_ref, sem,
):
    epochs, comps, rows, cols = f_ref.shape
    h = HALO
    copies = copy_in([(eta_hbm, eta_ref), (fd_hbm, fd_ref), (f_hbm, f_ref), (o_hbm, o_ref)], sem)
    for c in copies:
        c.wait()
    planes = [f_ref.at[e, comp] for e in range(epochs) for comp in range(comps)]
    planes += [o_ref.at[e, comp] for e in range(epochs) for comp in range(comps)]
    planes += [eta_ref, fd_ref.at[0], fd_ref.at[1]]
    for p, ref in enumerate(planes):
        t = ref[...].T
        clo_ref[p] = t[0:h]
        chi_ref[p] = t[cols - h : cols]


def scratch_like(*arrays):
    return [pltpu.VMEM(a.shape, a.dtype) for a in arrays]


def local_solve(forcing, observed, eta, fd, ice_mask, ra, rb, ca, cb):
    epochs, comps, rows, cols = forcing.shape
    full = (rows + 2 * HALO, 2 * cols)
    vmem = pl.BlockSpec(memory_space=pltpu.VMEM)
    anywhere = pl.BlockSpec(memory_space=pltpu.HBM)
    nodes = full[0] * full[1]
    args = (forcing, observed, eta, fd, ice_mask, ra, rb, ca, cb)
    return pl.pallas_call(
        kernel,
        out_shape=(
            jax.ShapeDtypeStruct(forcing.shape, jnp.float32),
            jax.ShapeDtypeStruct((rows, cols), jnp.float32),
        ),
        in_specs=[anywhere] * 9,
        out_specs=(vmem, vmem),
        scratch_shapes=scratch_like(*args)
        + [
            pltpu.VMEM((3 + 2 * comps,) + full, jnp.float32),
            pltpu.VMEM((20,) + full, jnp.float32),
            pltpu.VMEM(full, jnp.float32),
            pltpu.SemaphoreType.DMA((9,)),
        ],
        cost_estimate=pl.CostEstimate(
            flops=epochs * 2 * SWEEPS * comps * 60 * nodes,
            bytes_accessed=4 * (3 * epochs * comps + 40) * rows * cols,
            transcendentals=0,
        ),
    )(*args)


def body(forcing, observed, viscosity, friction, ice_mask, dirichlet):
    epochs, comps, rows, cols = forcing.shape
    h = HALO
    planes = 2 * epochs * comps + 3
    slab = jax.ShapeDtypeStruct((planes, h, cols), jnp.float32)
    cslab = jax.ShapeDtypeStruct((planes, h, rows), jnp.float32)
    fd_shape = jax.ShapeDtypeStruct((2, rows, cols), jnp.float32)
    args = (forcing, observed, viscosity, friction, ice_mask, dirichlet)
    hbm = pl.BlockSpec(memory_space=pltpu.HBM)
    vmem = pl.BlockSpec(memory_space=pltpu.VMEM)
    lo, hi, fd = pl.pallas_call(
        prep_kernel,
        out_shape=(slab, slab, fd_shape),
        in_specs=[hbm] * 6,
        out_specs=(hbm,) * 3,
        scratch_shapes=scratch_like(*args, slab, slab, fd_shape)
        + [pltpu.SemaphoreType.DMA((10,)), pltpu.SemaphoreType.DMA((3,))],
    )(*args)
    ra, rb = exchange(lo, hi, "gx")
    cargs = (forcing, observed, viscosity, fd)
    clo, chi = pl.pallas_call(
        columns_kernel,
        out_shape=(cslab, cslab),
        in_specs=[hbm] * 4,
        out_specs=(vmem, vmem),
        scratch_shapes=scratch_like(*cargs) + [pltpu.SemaphoreType.DMA((4,))],
    )(*cargs)

    def corners(slab, a, b):
        edge = jnp.concatenate([ra[:, :, a:b], rb[:, :, a:b]], axis=1)
        gap = jnp.zeros((slab.shape[0], h, cols - rows - 2 * h), jnp.float32)
        return jnp.concatenate([slab, jnp.swapaxes(edge, 1, 2), gap], axis=2)

    ca, cb = exchange(corners(clo, 0, h), corners(chi, cols - h, cols), "gy")
    return local_solve(forcing, observed, viscosity, fd, ice_mask, ra, rb, ca, cb)


def solution(mesh):
    return jax.shard_map(
        body,
        mesh=mesh,
        in_specs=(
            P(None, None, "gx", "gy"),
            P(None, None, "gx", "gy"),
            P("gx", "gy"),
            P("gx", "gy"),
            P("gx", "gy"),
            P("gx", "gy"),
        ),
        out_specs=(P(None, None, "gx", "gy"), P("gx", "gy")),
        check_vma=False,
    )
```

```python
import functools

import jax
import jax.numpy as jnp
from jax import lax
from jax.experimental import pallas as pl
from jax.experimental.pallas import tpu as pltpu
from jax.sharding import PartitionSpec as P

SWEEPS = 3

UPPER_BOUND = 2.4
LOWER_BOUND = 0.05
FREE_DRAG = 4.0

HALO = 2 * SWEEPS + 2


def exchange(slab_low, slab_high, axis):
    size = lax.axis_size(axis)
    up = [(i, i + 1) for i in range(size - 1)]
    down = [(i + 1, i) for i in range(size - 1)]
    after = lax.ppermute(slab_low, axis, down)
    before = lax.ppermute(slab_high, axis, up)
    return after, before


def sh(x, di, dj):
    if di:
        x = pltpu.roll(x, (-di) % x.shape[0], 0)
    if dj:
        x = pltpu.roll(x, (-dj) % x.shape[1], 1)
    return x


def stencil_pair(u, v, c):
    (face_np, face_sm, face_ep, face_wm, face_np4, face_sm4, face_ep4, face_wm4, node_drag,
     north_u, south_u, east_u, west_u, north_v, south_v, east_v, west_v) = c

    def normal_part(values, fn, fs, fe, fw):
        middle = values
        rows_part = fn * (sh(values, 1, 0) - middle) - fs * (middle - sh(values, -1, 0))
        cols_part = fe * (sh(values, 0, 1) - middle) - fw * (middle - sh(values, 0, -1))
        return rows_part + cols_part

    def cross_part(values, n, s, e, w):
        across = sh(values, 0, 1) - sh(values, 0, -1)
        along = sh(values, 1, 0) - sh(values, -1, 0)
        first = n * sh(across, 1, 0) - s * sh(across, -1, 0)
        second = e * sh(along, 0, 1) - w * sh(along, 0, -1)
        return first + second

    image_u = (
        node_drag * u
        - normal_part(u, face_np4, face_sm4, face_ep, face_wm)
        - cross_part(v, north_u, south_u, east_u, west_u)
    )
    image_v = (
        node_drag * v
        - normal_part(v, face_np, face_sm, face_ep4, face_wm4)
        - cross_part(u, north_v, south_v, east_v, west_v)
    )
    return image_u, image_v


def chebyshev_pair(rhs_u, rhs_v, c, inv_u, inv_v):
    centre_value = 0.5 * (UPPER_BOUND + LOWER_BOUND)
    half_width = 0.5 * (UPPER_BOUND - LOWER_BOUND)
    ratio_value = centre_value / half_width
    weight_now = 1.0 / ratio_value
    res_u, res_v = rhs_u, rhs_v
    dir_u = inv_u * res_u / centre_value
    dir_v = inv_v * res_v / centre_value
    it_u = jnp.zeros_like(rhs_u)
    it_v = jnp.zeros_like(rhs_v)
    for sweep_no in range(SWEEPS + 1):
        it_u = it_u + dir_u
        it_v = it_v + dir_v
        if sweep_no < SWEEPS:
            img_u, img_v = stencil_pair(dir_u, dir_v, c)
            res_u = res_u - img_u
            res_v = res_v - img_v
            weight_next = 1.0 / (2.0 * ratio_value - weight_now)
            a = weight_next * weight_now
            b = 2.0 * weight_next / half_width
            dir_u = a * dir_u + b * (inv_u * res_u)
            dir_v = a * dir_v + b * (inv_v * res_v)
            weight_now = weight_next
    return it_u, it_v


def copy_in(pairs, sem):
    copies = [pltpu.make_async_copy(src, dst, sem.at[i]) for i, (src, dst) in enumerate(pairs)]
    for c in copies:
        c.start()
    return copies


def kernel(
    f_hbm, o_hbm, eta_hbm, fd_hbm, ice_hbm, rx_hbm, cx_hbm,
    vel_ref, grad_ref,
    f_ref, o_ref, eta_ref, fd_ref, ice_ref, rx_ref, cx_ref,
    field_ref, coef_ref, prod_ref, sem,
):
    epochs, comps, rows, cols = f_ref.shape
    h = HALO
    n = epochs * comps
    copies = copy_in(
        [
            (eta_hbm, eta_ref), (fd_hbm, fd_ref), (rx_hbm, rx_ref), (cx_hbm, cx_ref),
            (f_hbm, f_ref), (o_hbm, o_ref), (ice_hbm, ice_ref),
        ],
        sem,
    )
    for k in range(field_ref.shape[0]):
        field_ref[k, :, cols + h : 2 * cols - h] = jnp.zeros((rows + 2 * h, cols - 2 * h), jnp.float32)
    for c in copies[:4]:
        c.wait()
    ra_ref, rb_ref = rx_ref.at[0], rx_ref.at[1]
    ca_ref, cb_ref = cx_ref.at[0], cx_ref.at[1]

    def assemble(dst, centre, p):
        dst[0:rows, 0:cols] = centre
        dst[rows : rows + h, 0:cols] = ra_ref[p]
        dst[rows + h : rows + 2 * h, 0:cols] = rb_ref[p]
        dst[:, cols : cols + h] = ca_ref[p].T[0 : rows + 2 * h, :]
        dst[:, 2 * cols - h :] = cb_ref[p].T[0 : rows + 2 * h, :]

    assemble(field_ref.at[0], eta_ref[...], 2 * n)
    assemble(field_ref.at[1], fd_ref[0], 2 * n + 1)
    assemble(field_ref.at[2], fd_ref[1], 2 * n + 2)
    eta = field_ref[0]
    free = field_ref[1]
    drag = field_ref[2]
    node_drag = 0.25 * (sh(drag, -1, -1) + sh(drag, 0, -1) + sh(drag, -1, 0) + drag)
    north = sh(eta, 1, 0)
    south = sh(eta, -1, 0)
    east = sh(eta, 0, 1)
    west = sh(eta, 0, -1)
    face_np = 0.5 * (eta + north)
    face_sm = 0.5 * (eta + south)
    face_ep = 0.5 * (eta + east)
    face_wm = 0.5 * (eta + west)
    rows_sum = face_np + face_sm
    cols_sum = face_ep + face_wm
    inv_u = free / (4.0 * rows_sum + cols_sum + node_drag + 1.0 - free)
    inv_v = free / (rows_sum + 4.0 * cols_sum + node_drag + 1.0 - free)
    coefs = [face_np, face_sm, face_ep, face_wm]
    coefs += [4.0 * face_np, 4.0 * face_sm, 4.0 * face_ep, 4.0 * face_wm, node_drag]
    coefs += [0.5 * north, 0.5 * south, 0.25 * east, 0.25 * west]
    coefs += [0.25 * north, 0.25 * south, 0.5 * east, 0.5 * west]
    for k, val in enumerate(coefs + [inv_u, inv_v, free]):
        coef_ref[k] = val
    prod_ref[...] = jnp.zeros_like(prod_ref)
    for c in copies[4:]:
        c.wait()

    def epoch(e, carry):
        for comp in range(comps):
            p = e * comps + comp
            assemble(field_ref.at[3 + comp], f_ref[e, comp], p)
            assemble(field_ref.at[3 + comps + comp], o_ref[e, comp], n + p)
        c = tuple(coef_ref[k] for k in range(17))
        inv_u = coef_ref[17]
        inv_v = coef_ref[18]
        free = coef_ref[19]
        vel_u, vel_v = chebyshev_pair(free * field_ref[3], free * field_ref[4], c, inv_u, inv_v)
        vel_ref[e, 0] = vel_u[0:rows, 0:cols]
        vel_ref[e, 1] = vel_v[0:rows, 0:cols]
        mis_u = free * (vel_u - field_ref[5])
        mis_v = free * (vel_v - field_ref[6])
        adj_u, adj_v = chebyshev_pair(mis_u, mis_v, c, inv_u, inv_v)
        prod_ref[...] += adj_u * vel_u + adj_v * vel_v
        return carry

    lax.fori_loop(0, epochs, epoch, 0)
    product = prod_ref[...]
    rows_sum = product + sh(product, 1, 0)
    total = rows_sum + sh(rows_sum, 0, 1)
    grounded = (ice_ref[...] == 2).astype(jnp.float32)
    grad_ref[...] = -0.25 * grounded * total[0:rows, 0:cols]


def prep_kernel(
    f_hbm, o_hbm, eta_hbm, fric_hbm, ice_hbm, dir_hbm,
    lo_hbm, hi_hbm, clo_hbm, chi_hbm, fd_hbm,
    f_ref, o_ref, eta_ref, fric_ref, ice_ref, dir_ref, lo_ref, hi_ref, clo_ref, chi_ref, fd_ref,
    sem, out_sem,
):
    epochs, comps, rows, cols = f_ref.shape
    h = HALO
    n = epochs * comps
    copies = copy_in(
        [
            (ice_hbm, ice_ref), (dir_hbm, dir_ref), (fric_hbm, fric_ref), (eta_hbm, eta_ref),
            (f_hbm, f_ref), (o_hbm, o_ref),
        ],
        sem,
    )
    for c in copies[:4]:
        c.wait()
    ice = ice_ref[...]
    free = (1 - dir_ref[...]).astype(jnp.float32)
    drag = jnp.where(ice == 2, fric_ref[...], jnp.where(ice == 0, FREE_DRAG, 0.0))
    fd_ref[0] = free
    fd_ref[1] = drag
    for c in copies[4:]:
        c.wait()
    planes = []
    for e in range(epochs):
        for comp in range(comps):
            planes.append(f_ref.at[e, comp])
    for e in range(epochs):
        for comp in range(comps):
            planes.append(o_ref.at[e, comp])
    for p, ref in enumerate(planes):
        lo_ref[p] = ref[0:h, :]
        hi_ref[p] = ref[rows - h : rows, :]
    for k, val in enumerate([eta_ref[...], free, drag]):
        lo_ref[2 * n + k] = val[0:h]
        hi_ref[2 * n + k] = val[rows - h : rows]
    out = copy_in([(lo_ref, lo_hbm), (hi_ref, hi_hbm), (fd_ref, fd_hbm)], out_sem)
    for p, ref in enumerate(planes):
        t = ref[...].T
        clo_ref[p] = t[0:h]
        chi_ref[p] = t[cols - h : cols]
    for k, val in enumerate([eta_ref[...], free, drag]):
        t = val.T
        clo_ref[2 * n + k] = t[0:h]
        chi_ref[2 * n + k] = t[cols - h : cols]
    out += copy_in([(clo_ref, clo_hbm), (chi_ref, chi_hbm)], out_sem.at[3:])
    for c in out:
        c.wait()


def scratch_like(*arrays):
    return [pltpu.VMEM(a.shape, a.dtype) for a in arrays]


def prep(forcing, observed, viscosity, friction, ice_mask, dirichlet):
    epochs, comps, rows, cols = forcing.shape
    planes = 2 * epochs * comps + 3
    hbm = pl.BlockSpec(memory_space=pltpu.HBM)
    slab = jax.ShapeDtypeStruct((planes, HALO, cols), jnp.float32)
    cslab = jax.ShapeDtypeStruct((planes, HALO, rows), jnp.float32)
    fd = jax.ShapeDtypeStruct((2, rows, cols), jnp.float32)
    outs = (slab, slab, cslab, cslab, fd)
    args = (forcing, observed, viscosity, friction, ice_mask, dirichlet)
    return pl.pallas_call(
        prep_kernel,
        out_shape=outs,
        in_specs=[hbm] * 6,
        out_specs=(hbm,) * 5,
        scratch_shapes=scratch_like(*args, *outs)
        + [pltpu.SemaphoreType.DMA((6,)), pltpu.SemaphoreType.DMA((5,))],
    )(*args)


def local_solve(forcing, observed, eta, fd, ice_mask, rows_x, cols_x):
    epochs, comps, rows, cols = forcing.shape
    full = (rows + 2 * HALO, 2 * cols)
    vmem = pl.BlockSpec(memory_space=pltpu.VMEM)
    anywhere = pl.BlockSpec(memory_space=pltpu.HBM)
    nodes = full[0] * full[1]
    args = (forcing, observed, eta, fd, ice_mask, rows_x, cols_x)
    return pl.pallas_call(
        kernel,
        out_shape=(
            jax.ShapeDtypeStruct(forcing.shape, jnp.float32),
            jax.ShapeDtypeStruct((rows, cols), jnp.float32),
        ),
        in_specs=[anywhere] * len(args),
        out_specs=(vmem, vmem),
        scratch_shapes=scratch_like(*args)
        + [
            pltpu.VMEM((3 + 2 * comps,) + full, jnp.float32),
            pltpu.VMEM((20,) + full, jnp.float32),
            pltpu.VMEM(full, jnp.float32),
            pltpu.SemaphoreType.DMA((7,)),
        ],
        cost_estimate=pl.CostEstimate(
            flops=epochs * 2 * SWEEPS * comps * 60 * nodes,
            bytes_accessed=4 * (3 * epochs * comps + 40) * rows * cols,
            transcendentals=0,
        ),
    )(*args)


def body(forcing, observed, viscosity, friction, ice_mask, dirichlet):
    epochs, comps, rows, cols = forcing.shape
    h = HALO
    lo, hi, clo, chi, fd = prep(forcing, observed, viscosity, friction, ice_mask, dirichlet)
    ra, rb = exchange(lo, hi, "gx")

    def corners(slab, a, b):
        edge = jnp.concatenate([ra[:, :, a:b], rb[:, :, a:b]], axis=1)
        gap = jnp.zeros((slab.shape[0], h, cols - rows - 2 * h), jnp.float32)
        return jnp.concatenate([slab, jnp.swapaxes(edge, 1, 2), gap], axis=2)

    ca, cb = exchange(corners(clo, 0, h), corners(chi, cols - h, cols), "gy")
    return local_solve(forcing, observed, viscosity, fd, ice_mask, jnp.stack([ra, rb]), jnp.stack([ca, cb]))


def solution(mesh):
    return jax.shard_map(
        body,
        mesh=mesh,
        in_specs=(
            P(None, None, "gx", "gy"),
            P(None, None, "gx", "gy"),
            P("gx", "gy"),
            P("gx", "gy"),
            P("gx", "gy"),
            P("gx", "gy"),
        ),
        out_specs=(P(None, None, "gx", "gy"), P("gx", "gy")),
        check_vma=False,
    )
```

```python
import functools

import jax
import jax.numpy as jnp
from jax import lax
from jax.experimental import pallas as pl
from jax.experimental.pallas import tpu as pltpu
from jax.sharding import PartitionSpec as P

SWEEPS = 3

UPPER_BOUND = 2.4
LOWER_BOUND = 0.05
FREE_DRAG = 4.0

HALO = 2 * SWEEPS + 2


def exchange(slab_low, slab_high, axis):
    size = lax.axis_size(axis)
    up = [(i, i + 1) for i in range(size - 1)]
    down = [(i + 1, i) for i in range(size - 1)]
    after = lax.ppermute(slab_low, axis, down)
    before = lax.ppermute(slab_high, axis, up)
    return after, before


def sh(x, di, dj):
    if di:
        x = pltpu.roll(x, (-di) % x.shape[0], 0)
    if dj:
        x = pltpu.roll(x, (-dj) % x.shape[1], 1)
    return x


def stencil_pair(u, v, c):
    (face_np, face_sm, face_ep, face_wm, face_np4, face_sm4, face_ep4, face_wm4, node_drag,
     north_u, south_u, east_u, west_u, north_v, south_v, east_v, west_v) = c

    def normal_part(values, fn, fs, fe, fw):
        middle = values
        rows_part = fn * (sh(values, 1, 0) - middle) - fs * (middle - sh(values, -1, 0))
        cols_part = fe * (sh(values, 0, 1) - middle) - fw * (middle - sh(values, 0, -1))
        return rows_part + cols_part

    def cross_part(values, n, s, e, w):
        across = sh(values, 0, 1) - sh(values, 0, -1)
        along = sh(values, 1, 0) - sh(values, -1, 0)
        first = n * sh(across, 1, 0) - s * sh(across, -1, 0)
        second = e * sh(along, 0, 1) - w * sh(along, 0, -1)
        return first + second

    image_u = (
        node_drag * u
        - normal_part(u, face_np4, face_sm4, face_ep, face_wm)
        - cross_part(v, north_u, south_u, east_u, west_u)
    )
    image_v = (
        node_drag * v
        - normal_part(v, face_np, face_sm, face_ep4, face_wm4)
        - cross_part(u, north_v, south_v, east_v, west_v)
    )
    return image_u, image_v


def chebyshev_pair(rhs_u, rhs_v, c, inv_u, inv_v):
    centre_value = 0.5 * (UPPER_BOUND + LOWER_BOUND)
    half_width = 0.5 * (UPPER_BOUND - LOWER_BOUND)
    ratio_value = centre_value / half_width
    weight_now = 1.0 / ratio_value
    res_u, res_v = rhs_u, rhs_v
    dir_u = inv_u * res_u / centre_value
    dir_v = inv_v * res_v / centre_value
    it_u = jnp.zeros_like(rhs_u)
    it_v = jnp.zeros_like(rhs_v)
    for sweep_no in range(SWEEPS + 1):
        it_u = it_u + dir_u
        it_v = it_v + dir_v
        if sweep_no < SWEEPS:
            img_u, img_v = stencil_pair(dir_u, dir_v, c)
            res_u = res_u - img_u
            res_v = res_v - img_v
            weight_next = 1.0 / (2.0 * ratio_value - weight_now)
            a = weight_next * weight_now
            b = 2.0 * weight_next / half_width
            dir_u = a * dir_u + b * (inv_u * res_u)
            dir_v = a * dir_v + b * (inv_v * res_v)
            weight_now = weight_next
    return it_u, it_v


def copy_in(pairs, sem):
    copies = [pltpu.make_async_copy(src, dst, sem.at[i]) for i, (src, dst) in enumerate(pairs)]
    for c in copies:
        c.start()
    return copies


def kernel(
    f_hbm, o_hbm, eta_hbm, fd_hbm, ice_hbm, rx_hbm, cx_hbm,
    vel_ref, grad_ref,
    f_ref, o_ref, eta_ref, fd_ref, ice_ref, rx_ref, cx_ref,
    field_ref, coef_ref, prod_ref, sem,
):
    epochs, comps, rows, cols = f_ref.shape
    h = HALO
    n = epochs * comps
    copies = copy_in(
        [
            (eta_hbm, eta_ref), (fd_hbm, fd_ref), (rx_hbm, rx_ref), (cx_hbm, cx_ref),
            (f_hbm, f_ref), (o_hbm, o_ref), (ice_hbm, ice_ref),
        ],
        sem,
    )
    for k in range(field_ref.shape[0]):
        field_ref[k, :, cols + h : 2 * cols - h] = jnp.zeros((rows + 2 * h, cols - 2 * h), jnp.float32)
    for c in copies[:4]:
        c.wait()
    ra_ref, rb_ref = rx_ref.at[0], rx_ref.at[1]
    ca_ref, cb_ref = cx_ref.at[0], cx_ref.at[1]

    def assemble(dst, centre, p):
        dst[0:rows, 0:cols] = centre
        dst[rows : rows + h, 0:cols] = ra_ref[p]
        dst[rows + h : rows + 2 * h, 0:cols] = rb_ref[p]
        dst[:, cols : cols + h] = ca_ref[p].T[0 : rows + 2 * h, :]
        dst[:, 2 * cols - h :] = cb_ref[p].T[0 : rows + 2 * h, :]

    assemble(field_ref.at[0], eta_ref[...], 2 * n)
    assemble(field_ref.at[1], fd_ref[0], 2 * n + 1)
    assemble(field_ref.at[2], fd_ref[1], 2 * n + 2)
    eta = field_ref[0]
    free = field_ref[1]
    drag = field_ref[2]
    node_drag = 0.25 * (sh(drag, -1, -1) + sh(drag, 0, -1) + sh(drag, -1, 0) + drag)
    north = sh(eta, 1, 0)
    south = sh(eta, -1, 0)
    east = sh(eta, 0, 1)
    west = sh(eta, 0, -1)
    face_np = 0.5 * (eta + north)
    face_sm = 0.5 * (eta + south)
    face_ep = 0.5 * (eta + east)
    face_wm = 0.5 * (eta + west)
    rows_sum = face_np + face_sm
    cols_sum = face_ep + face_wm
    inv_u = free / (4.0 * rows_sum + cols_sum + node_drag + 1.0 - free)
    inv_v = free / (rows_sum + 4.0 * cols_sum + node_drag + 1.0 - free)
    coefs = [face_np, face_sm, face_ep, face_wm]
    coefs += [4.0 * face_np, 4.0 * face_sm, 4.0 * face_ep, 4.0 * face_wm, node_drag]
    coefs += [0.5 * north, 0.5 * south, 0.25 * east, 0.25 * west]
    coefs += [0.25 * north, 0.25 * south, 0.5 * east, 0.5 * west]
    for k, val in enumerate(coefs + [inv_u, inv_v, free]):
        coef_ref[k] = val
    prod_ref[...] = jnp.zeros_like(prod_ref)
    for c in copies[4:]:
        c.wait()

    def epoch(e, carry):
        for comp in range(comps):
            p = e * comps + comp
            assemble(field_ref.at[3 + comp], f_ref[e, comp], p)
            assemble(field_ref.at[3 + comps + comp], o_ref[e, comp], n + p)
        c = tuple(coef_ref[k] for k in range(17))
        inv_u = coef_ref[17]
        inv_v = coef_ref[18]
        free = coef_ref[19]
        vel_u, vel_v = chebyshev_pair(free * field_ref[3], free * field_ref[4], c, inv_u, inv_v)
        vel_ref[e, 0] = vel_u[0:rows, 0:cols]
        vel_ref[e, 1] = vel_v[0:rows, 0:cols]
        mis_u = free * (vel_u - field_ref[5])
        mis_v = free * (vel_v - field_ref[6])
        adj_u, adj_v = chebyshev_pair(mis_u, mis_v, c, inv_u, inv_v)
        prod_ref[...] += adj_u * vel_u + adj_v * vel_v
        return carry

    lax.fori_loop(0, epochs, epoch, 0)
    product = prod_ref[...]
    rows_sum = product + sh(product, 1, 0)
    total = rows_sum + sh(rows_sum, 0, 1)
    grounded = (ice_ref[...] == 2).astype(jnp.float32)
    grad_ref[...] = -0.25 * grounded * total[0:rows, 0:cols]


def prep_kernel(
    f_hbm, o_hbm, eta_hbm, fric_hbm, ice_hbm, dir_hbm,
    lo_hbm, hi_hbm, clo_hbm, chi_hbm, fd_hbm,
    f_ref, o_ref, eta_ref, fric_ref, ice_ref, dir_ref, lo_ref, hi_ref, clo_ref, chi_ref, fd_ref,
    sem, out_sem,
):
    epochs, comps, rows, cols = f_ref.shape
    h = HALO
    n = epochs * comps
    copies = copy_in(
        [
            (ice_hbm, ice_ref), (dir_hbm, dir_ref), (fric_hbm, fric_ref), (eta_hbm, eta_ref),
            (f_hbm, f_ref), (o_hbm, o_ref),
        ],
        sem,
    )
    for c in copies[:4]:
        c.wait()
    ice = ice_ref[...]
    free = (1 - dir_ref[...]).astype(jnp.float32)
    drag = jnp.where(ice == 2, fric_ref[...], jnp.where(ice == 0, FREE_DRAG, 0.0))
    fd_ref[0] = free
    fd_ref[1] = drag
    for c in copies[4:]:
        c.wait()
    planes = []
    for e in range(epochs):
        for comp in range(comps):
            planes.append(f_ref.at[e, comp])
    for e in range(epochs):
        for comp in range(comps):
            planes.append(o_ref.at[e, comp])
    for p, ref in enumerate(planes):
        lo_ref[p] = ref[0:h, :]
        hi_ref[p] = ref[rows - h : rows, :]
    for k, val in enumerate([eta_ref[...], free, drag]):
        lo_ref[2 * n + k] = val[0:h]
        hi_ref[2 * n + k] = val[rows - h : rows]
    out = copy_in([(lo_ref, lo_hbm), (hi_ref, hi_hbm), (fd_ref, fd_hbm)], out_sem)
    values = [ref[...] for ref in planes] + [eta_ref[...], free, drag]
    lane = lax.broadcasted_iota(jnp.int32, (rows, cols), 1)
    group = cols // (2 * h)
    for g in range(0, len(values), group):
        packed = jnp.zeros((rows, cols), jnp.float32)
        for k, x in enumerate(values[g : g + group]):
            left = pltpu.roll(x, 2 * h * k, 1)
            right = pltpu.roll(x, (2 * h * k + 2 * h - cols) % cols, 1)
            packed = jnp.where((lane >= 2 * h * k) & (lane < 2 * h * k + h), left, packed)
            packed = jnp.where((lane >= 2 * h * k + h) & (lane < 2 * h * k + 2 * h), right, packed)
        t = packed.T
        for k in range(len(values[g : g + group])):
            clo_ref[g + k] = t[2 * h * k : 2 * h * k + h]
            chi_ref[g + k] = t[2 * h * k + h : 2 * h * k + 2 * h]
    out += copy_in([(clo_ref, clo_hbm), (chi_ref, chi_hbm)], out_sem.at[3:])
    for c in out:
        c.wait()


def scratch_like(*arrays):
    return [pltpu.VMEM(a.shape, a.dtype) for a in arrays]


def prep(forcing, observed, viscosity, friction, ice_mask, dirichlet):
    epochs, comps, rows, cols = forcing.shape
    planes = 2 * epochs * comps + 3
    hbm = pl.BlockSpec(memory_space=pltpu.HBM)
    slab = jax.ShapeDtypeStruct((planes, HALO, cols), jnp.float32)
    cslab = jax.ShapeDtypeStruct((planes, HALO, rows), jnp.float32)
    fd = jax.ShapeDtypeStruct((2, rows, cols), jnp.float32)
    outs = (slab, slab, cslab, cslab, fd)
    args = (forcing, observed, viscosity, friction, ice_mask, dirichlet)
    return pl.pallas_call(
        prep_kernel,
        out_shape=outs,
        in_specs=[hbm] * 6,
        out_specs=(hbm,) * 5,
        scratch_shapes=scratch_like(*args, *outs)
        + [pltpu.SemaphoreType.DMA((6,)), pltpu.SemaphoreType.DMA((5,))],
    )(*args)


def local_solve(forcing, observed, eta, fd, ice_mask, rows_x, cols_x):
    epochs, comps, rows, cols = forcing.shape
    full = (rows + 2 * HALO, 2 * cols)
    vmem = pl.BlockSpec(memory_space=pltpu.VMEM)
    anywhere = pl.BlockSpec(memory_space=pltpu.HBM)
    nodes = full[0] * full[1]
    args = (forcing, observed, eta, fd, ice_mask, rows_x, cols_x)
    return pl.pallas_call(
        kernel,
        out_shape=(
            jax.ShapeDtypeStruct(forcing.shape, jnp.float32),
            jax.ShapeDtypeStruct((rows, cols), jnp.float32),
        ),
        in_specs=[anywhere] * len(args),
        out_specs=(vmem, vmem),
        scratch_shapes=scratch_like(*args)
        + [
            pltpu.VMEM((3 + 2 * comps,) + full, jnp.float32),
            pltpu.VMEM((20,) + full, jnp.float32),
            pltpu.VMEM(full, jnp.float32),
            pltpu.SemaphoreType.DMA((7,)),
        ],
        cost_estimate=pl.CostEstimate(
            flops=epochs * 2 * SWEEPS * comps * 60 * nodes,
            bytes_accessed=4 * (3 * epochs * comps + 40) * rows * cols,
            transcendentals=0,
        ),
    )(*args)


def body(forcing, observed, viscosity, friction, ice_mask, dirichlet):
    epochs, comps, rows, cols = forcing.shape
    h = HALO
    lo, hi, clo, chi, fd = prep(forcing, observed, viscosity, friction, ice_mask, dirichlet)
    ra, rb = exchange(lo, hi, "gx")

    def corners(slab, a, b):
        edge = jnp.concatenate([ra[:, :, a:b], rb[:, :, a:b]], axis=1)
        gap = jnp.zeros((slab.shape[0], h, cols - rows - 2 * h), jnp.float32)
        return jnp.concatenate([slab, jnp.swapaxes(edge, 1, 2), gap], axis=2)

    ca, cb = exchange(corners(clo, 0, h), corners(chi, cols - h, cols), "gy")
    return local_solve(forcing, observed, viscosity, fd, ice_mask, jnp.stack([ra, rb]), jnp.stack([ca, cb]))


def solution(mesh):
    return jax.shard_map(
        body,
        mesh=mesh,
        in_specs=(
            P(None, None, "gx", "gy"),
            P(None, None, "gx", "gy"),
            P("gx", "gy"),
            P("gx", "gy"),
            P("gx", "gy"),
            P("gx", "gy"),
        ),
        out_specs=(P(None, None, "gx", "gy"), P("gx", "gy")),
        check_vma=False,
    )
```

```python
import functools

import jax
import jax.numpy as jnp
from jax import lax
from jax.experimental import pallas as pl
from jax.experimental.pallas import tpu as pltpu
from jax.sharding import PartitionSpec as P

SWEEPS = 3

UPPER_BOUND = 2.4
LOWER_BOUND = 0.05
FREE_DRAG = 4.0

HALO = 2 * SWEEPS + 2


def exchange(slab_low, slab_high, axis):
    size = lax.axis_size(axis)
    up = [(i, i + 1) for i in range(size - 1)]
    down = [(i + 1, i) for i in range(size - 1)]
    after = lax.ppermute(slab_low, axis, down)
    before = lax.ppermute(slab_high, axis, up)
    return after, before


def sh(x, di, dj):
    if di:
        x = pltpu.roll(x, (-di) % x.shape[0], 0)
    if dj:
        x = pltpu.roll(x, (-dj) % x.shape[1], 1)
    return x


def stencil_pair(u, v, c):
    (face_np, face_sm, face_ep, face_wm, face_np4, face_sm4, face_ep4, face_wm4, node_drag,
     north_u, south_u, east_u, west_u, north_v, south_v, east_v, west_v) = c

    def normal_part(values, fn, fs, fe, fw):
        middle = values
        rows_part = fn * (sh(values, 1, 0) - middle) - fs * (middle - sh(values, -1, 0))
        cols_part = fe * (sh(values, 0, 1) - middle) - fw * (middle - sh(values, 0, -1))
        return rows_part + cols_part

    def cross_part(values, n, s, e, w):
        across = sh(values, 0, 1) - sh(values, 0, -1)
        along = sh(values, 1, 0) - sh(values, -1, 0)
        first = n * sh(across, 1, 0) - s * sh(across, -1, 0)
        second = e * sh(along, 0, 1) - w * sh(along, 0, -1)
        return first + second

    image_u = (
        node_drag * u
        - normal_part(u, face_np4, face_sm4, face_ep, face_wm)
        - cross_part(v, north_u, south_u, east_u, west_u)
    )
    image_v = (
        node_drag * v
        - normal_part(v, face_np, face_sm, face_ep4, face_wm4)
        - cross_part(u, north_v, south_v, east_v, west_v)
    )
    return image_u, image_v


def chebyshev_pair(rhs_u, rhs_v, c, inv_u, inv_v):
    centre_value = 0.5 * (UPPER_BOUND + LOWER_BOUND)
    half_width = 0.5 * (UPPER_BOUND - LOWER_BOUND)
    ratio_value = centre_value / half_width
    weight_now = 1.0 / ratio_value
    res_u, res_v = rhs_u, rhs_v
    dir_u = inv_u * res_u / centre_value
    dir_v = inv_v * res_v / centre_value
    it_u = jnp.zeros_like(rhs_u)
    it_v = jnp.zeros_like(rhs_v)
    for sweep_no in range(SWEEPS + 1):
        it_u = it_u + dir_u
        it_v = it_v + dir_v
        if sweep_no < SWEEPS:
            img_u, img_v = stencil_pair(dir_u, dir_v, c)
            res_u = res_u - img_u
            res_v = res_v - img_v
            weight_next = 1.0 / (2.0 * ratio_value - weight_now)
            a = weight_next * weight_now
            b = 2.0 * weight_next / half_width
            dir_u = a * dir_u + b * (inv_u * res_u)
            dir_v = a * dir_v + b * (inv_v * res_v)
            weight_now = weight_next
    return it_u, it_v


def copy_in(pairs, sem):
    copies = [pltpu.make_async_copy(src, dst, sem.at[i]) for i, (src, dst) in enumerate(pairs)]
    for c in copies:
        c.start()
    return copies


def kernel(
    f_hbm, o_hbm, eta_hbm, fd_hbm, ice_hbm, rx_hbm, cx_hbm,
    vel_hbm, grad_ref,
    f_ref, o_ref, eta_ref, fd_ref, ice_ref, rx_ref, cx_ref,
    field_ref, coef_ref, prod_ref, vel_ref, sem, vel_sem,
):
    epochs, comps, rows, cols = f_ref.shape
    h = HALO
    n = epochs * comps
    copies = copy_in(
        [
            (eta_hbm, eta_ref), (fd_hbm, fd_ref), (rx_hbm, rx_ref), (cx_hbm, cx_ref),
            (f_hbm, f_ref), (o_hbm, o_ref), (ice_hbm, ice_ref),
        ],
        sem,
    )
    for k in range(field_ref.shape[0]):
        field_ref[k, :, cols + h : 2 * cols - h] = jnp.zeros((rows + 2 * h, cols - 2 * h), jnp.float32)
    for c in copies[:4]:
        c.wait()
    ra_ref, rb_ref = rx_ref.at[0], rx_ref.at[1]
    ca_ref, cb_ref = cx_ref.at[0], cx_ref.at[1]

    def assemble(dst, centre, p):
        dst[0:rows, 0:cols] = centre
        dst[rows : rows + h, 0:cols] = ra_ref[p]
        dst[rows + h : rows + 2 * h, 0:cols] = rb_ref[p]
        dst[:, cols : cols + h] = ca_ref[p].T[0 : rows + 2 * h, :]
        dst[:, 2 * cols - h :] = cb_ref[p].T[0 : rows + 2 * h, :]

    assemble(field_ref.at[0], eta_ref[...], 2 * n)
    assemble(field_ref.at[1], fd_ref[0], 2 * n + 1)
    assemble(field_ref.at[2], fd_ref[1], 2 * n + 2)
    eta = field_ref[0]
    free = field_ref[1]
    drag = field_ref[2]
    node_drag = 0.25 * (sh(drag, -1, -1) + sh(drag, 0, -1) + sh(drag, -1, 0) + drag)
    north = sh(eta, 1, 0)
    south = sh(eta, -1, 0)
    east = sh(eta, 0, 1)
    west = sh(eta, 0, -1)
    face_np = 0.5 * (eta + north)
    face_sm = 0.5 * (eta + south)
    face_ep = 0.5 * (eta + east)
    face_wm = 0.5 * (eta + west)
    rows_sum = face_np + face_sm
    cols_sum = face_ep + face_wm
    inv_u = free / (4.0 * rows_sum + cols_sum + node_drag + 1.0 - free)
    inv_v = free / (rows_sum + 4.0 * cols_sum + node_drag + 1.0 - free)
    coefs = [face_np, face_sm, face_ep, face_wm]
    coefs += [4.0 * face_np, 4.0 * face_sm, 4.0 * face_ep, 4.0 * face_wm, node_drag]
    coefs += [0.5 * north, 0.5 * south, 0.25 * east, 0.25 * west]
    coefs += [0.25 * north, 0.25 * south, 0.5 * east, 0.5 * west]
    for k, val in enumerate(coefs + [inv_u, inv_v, free]):
        coef_ref[k] = val
    prod_ref[...] = jnp.zeros_like(prod_ref)
    for c in copies[4:]:
        c.wait()

    def epoch(e, carry):
        for comp in range(comps):
            p = e * comps + comp
            assemble(field_ref.at[3 + comp], f_ref[e, comp], p)
            assemble(field_ref.at[3 + comps + comp], o_ref[e, comp], n + p)
        c = tuple(coef_ref[k] for k in range(17))
        inv_u = coef_ref[17]
        inv_v = coef_ref[18]
        free = coef_ref[19]
        vel_u, vel_v = chebyshev_pair(free * field_ref[3], free * field_ref[4], c, inv_u, inv_v)
        vel_ref[e, 0] = vel_u[0:rows, 0:cols]
        vel_ref[e, 1] = vel_v[0:rows, 0:cols]
        pltpu.make_async_copy(vel_ref.at[e], vel_hbm.at[e], vel_sem.at[e]).start()
        mis_u = free * (vel_u - field_ref[5])
        mis_v = free * (vel_v - field_ref[6])
        adj_u, adj_v = chebyshev_pair(mis_u, mis_v, c, inv_u, inv_v)
        prod_ref[...] += adj_u * vel_u + adj_v * vel_v
        return carry

    lax.fori_loop(0, epochs, epoch, 0)
    product = prod_ref[...]
    for e in range(epochs):
        pltpu.make_async_copy(vel_ref.at[e], vel_hbm.at[e], vel_sem.at[e]).wait()
    rows_sum = product + sh(product, 1, 0)
    total = rows_sum + sh(rows_sum, 0, 1)
    grounded = (ice_ref[...] == 2).astype(jnp.float32)
    grad_ref[...] = -0.25 * grounded * total[0:rows, 0:cols]


def prep_kernel(
    f_hbm, o_hbm, eta_hbm, fric_hbm, ice_hbm, dir_hbm,
    lo_hbm, hi_hbm, clo_hbm, chi_hbm, fd_hbm,
    f_ref, o_ref, eta_ref, fric_ref, ice_ref, dir_ref, lo_ref, hi_ref, clo_ref, chi_ref, fd_ref,
    sem, out_sem,
):
    epochs, comps, rows, cols = f_ref.shape
    h = HALO
    n = epochs * comps
    copies = copy_in(
        [
            (ice_hbm, ice_ref), (dir_hbm, dir_ref), (fric_hbm, fric_ref), (eta_hbm, eta_ref),
            (f_hbm, f_ref), (o_hbm, o_ref),
        ],
        sem,
    )
    for c in copies[:4]:
        c.wait()
    ice = ice_ref[...]
    free = (1 - dir_ref[...]).astype(jnp.float32)
    drag = jnp.where(ice == 2, fric_ref[...], jnp.where(ice == 0, FREE_DRAG, 0.0))
    fd_ref[0] = free
    fd_ref[1] = drag
    for c in copies[4:]:
        c.wait()
    planes = []
    for e in range(epochs):
        for comp in range(comps):
            planes.append(f_ref.at[e, comp])
    for e in range(epochs):
        for comp in range(comps):
            planes.append(o_ref.at[e, comp])
    for p, ref in enumerate(planes):
        lo_ref[p] = ref[0:h, :]
        hi_ref[p] = ref[rows - h : rows, :]
    for k, val in enumerate([eta_ref[...], free, drag]):
        lo_ref[2 * n + k] = val[0:h]
        hi_ref[2 * n + k] = val[rows - h : rows]
    out = copy_in([(lo_ref, lo_hbm), (hi_ref, hi_hbm), (fd_ref, fd_hbm)], out_sem)
    for p, ref in enumerate(planes):
        t = ref[...].T
        clo_ref[p] = t[0:h]
        chi_ref[p] = t[cols - h : cols]
    for k, val in enumerate([eta_ref[...], free, drag]):
        t = val.T
        clo_ref[2 * n + k] = t[0:h]
        chi_ref[2 * n + k] = t[cols - h : cols]
    out += copy_in([(clo_ref, clo_hbm), (chi_ref, chi_hbm)], out_sem.at[3:])
    for c in out:
        c.wait()


def scratch_like(*arrays):
    return [pltpu.VMEM(a.shape, a.dtype) for a in arrays]


def prep(forcing, observed, viscosity, friction, ice_mask, dirichlet):
    epochs, comps, rows, cols = forcing.shape
    planes = 2 * epochs * comps + 3
    hbm = pl.BlockSpec(memory_space=pltpu.HBM)
    slab = jax.ShapeDtypeStruct((planes, HALO, cols), jnp.float32)
    cslab = jax.ShapeDtypeStruct((planes, HALO, rows), jnp.float32)
    fd = jax.ShapeDtypeStruct((2, rows, cols), jnp.float32)
    outs = (slab, slab, cslab, cslab, fd)
    args = (forcing, observed, viscosity, friction, ice_mask, dirichlet)
    return pl.pallas_call(
        prep_kernel,
        out_shape=outs,
        in_specs=[hbm] * 6,
        out_specs=(hbm,) * 5,
        scratch_shapes=scratch_like(*args, *outs)
        + [pltpu.SemaphoreType.DMA((6,)), pltpu.SemaphoreType.DMA((5,))],
    )(*args)


def local_solve(forcing, observed, eta, fd, ice_mask, rows_x, cols_x):
    epochs, comps, rows, cols = forcing.shape
    full = (rows + 2 * HALO, 2 * cols)
    vmem = pl.BlockSpec(memory_space=pltpu.VMEM)
    anywhere = pl.BlockSpec(memory_space=pltpu.HBM)
    nodes = full[0] * full[1]
    args = (forcing, observed, eta, fd, ice_mask, rows_x, cols_x)
    return pl.pallas_call(
        kernel,
        out_shape=(
            jax.ShapeDtypeStruct(forcing.shape, jnp.float32),
            jax.ShapeDtypeStruct((rows, cols), jnp.float32),
        ),
        in_specs=[anywhere] * len(args),
        out_specs=(anywhere, vmem),
        scratch_shapes=scratch_like(*args)
        + [
            pltpu.VMEM((3 + 2 * comps,) + full, jnp.float32),
            pltpu.VMEM((20,) + full, jnp.float32),
            pltpu.VMEM(full, jnp.float32),
            pltpu.VMEM(forcing.shape, jnp.float32),
            pltpu.SemaphoreType.DMA((7,)),
            pltpu.SemaphoreType.DMA((epochs,)),
        ],
        cost_estimate=pl.CostEstimate(
            flops=epochs * 2 * SWEEPS * comps * 60 * nodes,
            bytes_accessed=4 * (3 * epochs * comps + 40) * rows * cols,
            transcendentals=0,
        ),
    )(*args)


def body(forcing, observed, viscosity, friction, ice_mask, dirichlet):
    epochs, comps, rows, cols = forcing.shape
    h = HALO
    lo, hi, clo, chi, fd = prep(forcing, observed, viscosity, friction, ice_mask, dirichlet)
    ra, rb = exchange(lo, hi, "gx")

    def corners(slab, a, b):
        edge = jnp.concatenate([ra[:, :, a:b], rb[:, :, a:b]], axis=1)
        gap = jnp.zeros((slab.shape[0], h, cols - rows - 2 * h), jnp.float32)
        return jnp.concatenate([slab, jnp.swapaxes(edge, 1, 2), gap], axis=2)

    ca, cb = exchange(corners(clo, 0, h), corners(chi, cols - h, cols), "gy")
    return local_solve(forcing, observed, viscosity, fd, ice_mask, jnp.stack([ra, rb]), jnp.stack([ca, cb]))


def solution(mesh):
    return jax.shard_map(
        body,
        mesh=mesh,
        in_specs=(
            P(None, None, "gx", "gy"),
            P(None, None, "gx", "gy"),
            P("gx", "gy"),
            P("gx", "gy"),
            P("gx", "gy"),
            P("gx", "gy"),
        ),
        out_specs=(P(None, None, "gx", "gy"), P("gx", "gy")),
        check_vma=False,
    )
```

```python
import functools

import jax
import jax.numpy as jnp
from jax import lax
from jax.experimental import pallas as pl
from jax.experimental.pallas import tpu as pltpu
from jax.sharding import PartitionSpec as P

SWEEPS = 3

UPPER_BOUND = 2.4
LOWER_BOUND = 0.05
FREE_DRAG = 4.0

HALO = 2 * SWEEPS + 2


def exchange(slab_low, slab_high, axis):
    size = lax.axis_size(axis)
    up = [(i, i + 1) for i in range(size - 1)]
    down = [(i + 1, i) for i in range(size - 1)]
    after = lax.ppermute(slab_low, axis, down)
    before = lax.ppermute(slab_high, axis, up)
    return after, before


def sh(x, di, dj):
    if di:
        x = pltpu.roll(x, (-di) % x.shape[0], 0)
    if dj:
        x = pltpu.roll(x, (-dj) % x.shape[1], 1)
    return x


def stencil_pair(u, v, c):
    (face_np, face_sm, face_ep, face_wm, face_np4, face_sm4, face_ep4, face_wm4, node_drag,
     north_u, south_u, east_u, west_u, north_v, south_v, east_v, west_v) = c

    def normal_part(values, fn, fs, fe, fw):
        middle = values
        rows_part = fn * (sh(values, 1, 0) - middle) - fs * (middle - sh(values, -1, 0))
        cols_part = fe * (sh(values, 0, 1) - middle) - fw * (middle - sh(values, 0, -1))
        return rows_part + cols_part

    def cross_part(values, n, s, e, w):
        across = sh(values, 0, 1) - sh(values, 0, -1)
        along = sh(values, 1, 0) - sh(values, -1, 0)
        first = n * sh(across, 1, 0) - s * sh(across, -1, 0)
        second = e * sh(along, 0, 1) - w * sh(along, 0, -1)
        return first + second

    image_u = (
        node_drag * u
        - normal_part(u, face_np4, face_sm4, face_ep, face_wm)
        - cross_part(v, north_u, south_u, east_u, west_u)
    )
    image_v = (
        node_drag * v
        - normal_part(v, face_np, face_sm, face_ep4, face_wm4)
        - cross_part(u, north_v, south_v, east_v, west_v)
    )
    return image_u, image_v


def chebyshev_pair(rhs_u, rhs_v, c, inv_u, inv_v):
    centre_value = 0.5 * (UPPER_BOUND + LOWER_BOUND)
    half_width = 0.5 * (UPPER_BOUND - LOWER_BOUND)
    ratio_value = centre_value / half_width
    weight_now = 1.0 / ratio_value
    res_u, res_v = rhs_u, rhs_v
    dir_u = inv_u * res_u / centre_value
    dir_v = inv_v * res_v / centre_value
    it_u = jnp.zeros_like(rhs_u)
    it_v = jnp.zeros_like(rhs_v)
    for sweep_no in range(SWEEPS + 1):
        it_u = it_u + dir_u
        it_v = it_v + dir_v
        if sweep_no < SWEEPS:
            img_u, img_v = stencil_pair(dir_u, dir_v, c)
            res_u = res_u - img_u
            res_v = res_v - img_v
            weight_next = 1.0 / (2.0 * ratio_value - weight_now)
            a = weight_next * weight_now
            b = 2.0 * weight_next / half_width
            dir_u = a * dir_u + b * (inv_u * res_u)
            dir_v = a * dir_v + b * (inv_v * res_v)
            weight_now = weight_next
    return it_u, it_v


def copy_in(pairs, sem):
    copies = [pltpu.make_async_copy(src, dst, sem.at[i]) for i, (src, dst) in enumerate(pairs)]
    for c in copies:
        c.start()
    return copies


def kernel(
    f_hbm, o_hbm, eta_hbm, fd_hbm, ice_hbm, rx_hbm, cx_hbm,
    vel_hbm, grad_ref,
    f_ref, o_ref, eta_ref, fd_ref, ice_ref, rx_ref, cx_ref,
    field_ref, coef_ref, prod_ref, vel_ref, sem, vel_sem,
):
    epochs, comps, rows, cols = f_ref.shape
    h = HALO
    n = epochs * comps
    copies = copy_in(
        [
            (eta_hbm, eta_ref), (fd_hbm, fd_ref), (rx_hbm, rx_ref), (cx_hbm, cx_ref),
            (f_hbm, f_ref), (o_hbm, o_ref), (ice_hbm, ice_ref),
        ],
        sem,
    )
    for k in range(field_ref.shape[0]):
        field_ref[k, :, cols + h : 2 * cols - h] = jnp.zeros((rows + 2 * h, cols - 2 * h), jnp.float32)
    for c in copies[:3]:
        c.wait()
    ra_ref, rb_ref = rx_ref.at[0], rx_ref.at[1]
    ca_ref, cb_ref = cx_ref.at[0], cx_ref.at[1]

    def assemble_rows(dst, centre, p):
        dst[0:rows, 0:cols] = centre
        dst[rows : rows + h, 0:cols] = ra_ref[p]
        dst[rows + h : rows + 2 * h, 0:cols] = rb_ref[p]

    def assemble_cols(dst, p):
        dst[:, cols : cols + h] = ca_ref[p].T[0 : rows + 2 * h, :]
        dst[:, 2 * cols - h :] = cb_ref[p].T[0 : rows + 2 * h, :]

    def assemble(dst, centre, p):
        assemble_rows(dst, centre, p)
        assemble_cols(dst, p)

    assemble_rows(field_ref.at[0], eta_ref[...], 2 * n)
    assemble_rows(field_ref.at[1], fd_ref[0], 2 * n + 1)
    assemble_rows(field_ref.at[2], fd_ref[1], 2 * n + 2)
    copies[3].wait()
    for k in range(3):
        assemble_cols(field_ref.at[k], 2 * n + k)
    eta = field_ref[0]
    free = field_ref[1]
    drag = field_ref[2]
    node_drag = 0.25 * (sh(drag, -1, -1) + sh(drag, 0, -1) + sh(drag, -1, 0) + drag)
    north = sh(eta, 1, 0)
    south = sh(eta, -1, 0)
    east = sh(eta, 0, 1)
    west = sh(eta, 0, -1)
    face_np = 0.5 * (eta + north)
    face_sm = 0.5 * (eta + south)
    face_ep = 0.5 * (eta + east)
    face_wm = 0.5 * (eta + west)
    rows_sum = face_np + face_sm
    cols_sum = face_ep + face_wm
    inv_u = free / (4.0 * rows_sum + cols_sum + node_drag + 1.0 - free)
    inv_v = free / (rows_sum + 4.0 * cols_sum + node_drag + 1.0 - free)
    coefs = [face_np, face_sm, face_ep, face_wm]
    coefs += [4.0 * face_np, 4.0 * face_sm, 4.0 * face_ep, 4.0 * face_wm, node_drag]
    coefs += [0.5 * north, 0.5 * south, 0.25 * east, 0.25 * west]
    coefs += [0.25 * north, 0.25 * south, 0.5 * east, 0.5 * west]
    for k, val in enumerate(coefs + [inv_u, inv_v, free]):
        coef_ref[k] = val
    prod_ref[...] = jnp.zeros_like(prod_ref)
    for c in copies[4:]:
        c.wait()

    def epoch(e, carry):
        for comp in range(comps):
            p = e * comps + comp
            assemble(field_ref.at[3 + comp], f_ref[e, comp], p)
            assemble(field_ref.at[3 + comps + comp], o_ref[e, comp], n + p)
        c = tuple(coef_ref[k] for k in range(17))
        inv_u = coef_ref[17]
        inv_v = coef_ref[18]
        free = coef_ref[19]
        vel_u, vel_v = chebyshev_pair(free * field_ref[3], free * field_ref[4], c, inv_u, inv_v)
        vel_ref[e, 0] = vel_u[0:rows, 0:cols]
        vel_ref[e, 1] = vel_v[0:rows, 0:cols]
        pltpu.make_async_copy(vel_ref.at[e], vel_hbm.at[e], vel_sem.at[e]).start()
        mis_u = free * (vel_u - field_ref[5])
        mis_v = free * (vel_v - field_ref[6])
        adj_u, adj_v = chebyshev_pair(mis_u, mis_v, c, inv_u, inv_v)
        prod_ref[...] += adj_u * vel_u + adj_v * vel_v
        return carry

    lax.fori_loop(0, epochs, epoch, 0)
    product = prod_ref[...]
    for e in range(epochs):
        pltpu.make_async_copy(vel_ref.at[e], vel_hbm.at[e], vel_sem.at[e]).wait()
    rows_sum = product + sh(product, 1, 0)
    total = rows_sum + sh(rows_sum, 0, 1)
    grounded = (ice_ref[...] == 2).astype(jnp.float32)
    grad_ref[...] = -0.25 * grounded * total[0:rows, 0:cols]


def prep_kernel(
    f_hbm, o_hbm, eta_hbm, fric_hbm, ice_hbm, dir_hbm,
    lo_hbm, hi_hbm, clo_hbm, chi_hbm, fd_hbm,
    f_ref, o_ref, eta_ref, fric_ref, ice_ref, dir_ref, lo_ref, hi_ref, clo_ref, chi_ref, fd_ref,
    sem, out_sem,
):
    epochs, comps, rows, cols = f_ref.shape
    h = HALO
    n = epochs * comps
    copies = copy_in(
        [
            (ice_hbm, ice_ref), (dir_hbm, dir_ref), (fric_hbm, fric_ref), (eta_hbm, eta_ref),
            (f_hbm, f_ref), (o_hbm, o_ref),
        ],
        sem,
    )
    for c in copies[:4]:
        c.wait()
    ice = ice_ref[...]
    free = (1 - dir_ref[...]).astype(jnp.float32)
    drag = jnp.where(ice == 2, fric_ref[...], jnp.where(ice == 0, FREE_DRAG, 0.0))
    fd_ref[0] = free
    fd_ref[1] = drag
    for c in copies[4:]:
        c.wait()
    planes = []
    for e in range(epochs):
        for comp in range(comps):
            planes.append(f_ref.at[e, comp])
    for e in range(epochs):
        for comp in range(comps):
            planes.append(o_ref.at[e, comp])
    for p, ref in enumerate(planes):
        lo_ref[p] = ref[0:h, :]
        hi_ref[p] = ref[rows - h : rows, :]
    for k, val in enumerate([eta_ref[...], free, drag]):
        lo_ref[2 * n + k] = val[0:h]
        hi_ref[2 * n + k] = val[rows - h : rows]
    out = copy_in([(lo_ref, lo_hbm), (hi_ref, hi_hbm), (fd_ref, fd_hbm)], out_sem)
    for p, ref in enumerate(planes):
        t = ref[...].T
        clo_ref[p] = t[0:h]
        chi_ref[p] = t[cols - h : cols]
    for k, val in enumerate([eta_ref[...], free, drag]):
        t = val.T
        clo_ref[2 * n + k] = t[0:h]
        chi_ref[2 * n + k] = t[cols - h : cols]
    out += copy_in([(clo_ref, clo_hbm), (chi_ref, chi_hbm)], out_sem.at[3:])
    for c in out:
        c.wait()


def scratch_like(*arrays):
    return [pltpu.VMEM(a.shape, a.dtype) for a in arrays]


def prep(forcing, observed, viscosity, friction, ice_mask, dirichlet):
    epochs, comps, rows, cols = forcing.shape
    planes = 2 * epochs * comps + 3
    hbm = pl.BlockSpec(memory_space=pltpu.HBM)
    slab = jax.ShapeDtypeStruct((planes, HALO, cols), jnp.float32)
    cslab = jax.ShapeDtypeStruct((planes, HALO, rows), jnp.float32)
    fd = jax.ShapeDtypeStruct((2, rows, cols), jnp.float32)
    outs = (slab, slab, cslab, cslab, fd)
    args = (forcing, observed, viscosity, friction, ice_mask, dirichlet)
    return pl.pallas_call(
        prep_kernel,
        out_shape=outs,
        in_specs=[hbm] * 6,
        out_specs=(hbm,) * 5,
        scratch_shapes=scratch_like(*args, *outs)
        + [pltpu.SemaphoreType.DMA((6,)), pltpu.SemaphoreType.DMA((5,))],
    )(*args)


def local_solve(forcing, observed, eta, fd, ice_mask, rows_x, cols_x):
    epochs, comps, rows, cols = forcing.shape
    full = (rows + 2 * HALO, 2 * cols)
    vmem = pl.BlockSpec(memory_space=pltpu.VMEM)
    anywhere = pl.BlockSpec(memory_space=pltpu.HBM)
    nodes = full[0] * full[1]
    args = (forcing, observed, eta, fd, ice_mask, rows_x, cols_x)
    return pl.pallas_call(
        kernel,
        out_shape=(
            jax.ShapeDtypeStruct(forcing.shape, jnp.float32),
            jax.ShapeDtypeStruct((rows, cols), jnp.float32),
        ),
        in_specs=[anywhere] * len(args),
        out_specs=(anywhere, vmem),
        scratch_shapes=scratch_like(*args)
        + [
            pltpu.VMEM((3 + 2 * comps,) + full, jnp.float32),
            pltpu.VMEM((20,) + full, jnp.float32),
            pltpu.VMEM(full, jnp.float32),
            pltpu.VMEM(forcing.shape, jnp.float32),
            pltpu.SemaphoreType.DMA((7,)),
            pltpu.SemaphoreType.DMA((epochs,)),
        ],
        cost_estimate=pl.CostEstimate(
            flops=epochs * 2 * SWEEPS * comps * 60 * nodes,
            bytes_accessed=4 * (3 * epochs * comps + 40) * rows * cols,
            transcendentals=0,
        ),
    )(*args)


def body(forcing, observed, viscosity, friction, ice_mask, dirichlet):
    epochs, comps, rows, cols = forcing.shape
    h = HALO
    lo, hi, clo, chi, fd = prep(forcing, observed, viscosity, friction, ice_mask, dirichlet)
    ra, rb = exchange(lo, hi, "gx")

    def corners(slab, a, b):
        edge = jnp.concatenate([ra[:, :, a:b], rb[:, :, a:b]], axis=1)
        gap = jnp.zeros((slab.shape[0], h, cols - rows - 2 * h), jnp.float32)
        return jnp.concatenate([slab, jnp.swapaxes(edge, 1, 2), gap], axis=2)

    ca, cb = exchange(corners(clo, 0, h), corners(chi, cols - h, cols), "gy")
    return local_solve(forcing, observed, viscosity, fd, ice_mask, jnp.stack([ra, rb]), jnp.stack([ca, cb]))


def solution(mesh):
    return jax.shard_map(
        body,
        mesh=mesh,
        in_specs=(
            P(None, None, "gx", "gy"),
            P(None, None, "gx", "gy"),
            P("gx", "gy"),
            P("gx", "gy"),
            P("gx", "gy"),
            P("gx", "gy"),
        ),
        out_specs=(P(None, None, "gx", "gy"), P("gx", "gy")),
        check_vma=False,
    )
```

```python
import functools

import jax
import jax.numpy as jnp
from jax import lax
from jax.experimental import pallas as pl
from jax.experimental.pallas import tpu as pltpu
from jax.sharding import PartitionSpec as P

SWEEPS = 3

UPPER_BOUND = 2.4
LOWER_BOUND = 0.05
FREE_DRAG = 4.0

HALO = 2 * SWEEPS + 2


def exchange(slab_low, slab_high, axis):
    size = lax.axis_size(axis)
    up = [(i, i + 1) for i in range(size - 1)]
    down = [(i + 1, i) for i in range(size - 1)]
    after = lax.ppermute(slab_low, axis, down)
    before = lax.ppermute(slab_high, axis, up)
    return after, before


def sh(x, di, dj):
    if di:
        x = pltpu.roll(x, (-di) % x.shape[0], 0)
    if dj:
        x = pltpu.roll(x, (-dj) % x.shape[1], 1)
    return x


def stencil_pair(u, v, c):
    (face_np, face_sm, face_ep, face_wm, face_np4, face_sm4, face_ep4, face_wm4, node_drag,
     north_u, south_u, east_u, west_u, north_v, south_v, east_v, west_v) = c

    def normal_part(values, fn, fs, fe, fw):
        middle = values
        rows_part = fn * (sh(values, 1, 0) - middle) - fs * (middle - sh(values, -1, 0))
        cols_part = fe * (sh(values, 0, 1) - middle) - fw * (middle - sh(values, 0, -1))
        return rows_part + cols_part

    def cross_part(values, n, s, e, w):
        across = sh(values, 0, 1) - sh(values, 0, -1)
        along = sh(values, 1, 0) - sh(values, -1, 0)
        first = n * sh(across, 1, 0) - s * sh(across, -1, 0)
        second = e * sh(along, 0, 1) - w * sh(along, 0, -1)
        return first + second

    image_u = (
        node_drag * u
        - normal_part(u, face_np4, face_sm4, face_ep, face_wm)
        - cross_part(v, north_u, south_u, east_u, west_u)
    )
    image_v = (
        node_drag * v
        - normal_part(v, face_np, face_sm, face_ep4, face_wm4)
        - cross_part(u, north_v, south_v, east_v, west_v)
    )
    return image_u, image_v


def chebyshev_pair(rhs_u, rhs_v, c, inv_u, inv_v):
    centre_value = 0.5 * (UPPER_BOUND + LOWER_BOUND)
    half_width = 0.5 * (UPPER_BOUND - LOWER_BOUND)
    ratio_value = centre_value / half_width
    weight_now = 1.0 / ratio_value
    res_u, res_v = rhs_u, rhs_v
    dir_u = inv_u * res_u * (1.0 / centre_value)
    dir_v = inv_v * res_v * (1.0 / centre_value)
    it_u = jnp.zeros_like(rhs_u)
    it_v = jnp.zeros_like(rhs_v)
    for sweep_no in range(SWEEPS + 1):
        it_u = it_u + dir_u
        it_v = it_v + dir_v
        if sweep_no < SWEEPS:
            img_u, img_v = stencil_pair(dir_u, dir_v, c)
            res_u = res_u - img_u
            res_v = res_v - img_v
            weight_next = 1.0 / (2.0 * ratio_value - weight_now)
            a = weight_next * weight_now
            b = 2.0 * weight_next / half_width
            dir_u = a * dir_u + b * (inv_u * res_u)
            dir_v = a * dir_v + b * (inv_v * res_v)
            weight_now = weight_next
    return it_u, it_v


def copy_in(pairs, sem):
    copies = [pltpu.make_async_copy(src, dst, sem.at[i]) for i, (src, dst) in enumerate(pairs)]
    for c in copies:
        c.start()
    return copies


def kernel(
    f_hbm, o_hbm, eta_hbm, fd_hbm, ice_hbm, rx_hbm, cx_hbm,
    vel_hbm, grad_ref,
    f_ref, o_ref, eta_ref, fd_ref, ice_ref, rx_ref, cx_ref,
    field_ref, coef_ref, prod_ref, vel_ref, sem, vel_sem,
):
    epochs, comps, rows, cols = f_ref.shape
    h = HALO
    n = epochs * comps
    copies = copy_in(
        [
            (eta_hbm, eta_ref), (fd_hbm, fd_ref), (rx_hbm, rx_ref), (cx_hbm, cx_ref),
            (f_hbm, f_ref), (o_hbm, o_ref), (ice_hbm, ice_ref),
        ],
        sem,
    )
    for k in range(field_ref.shape[0]):
        field_ref[k, :, cols + h : 2 * cols - h] = jnp.zeros((rows + 2 * h, cols - 2 * h), jnp.float32)
    for c in copies[:4]:
        c.wait()
    ra_ref, rb_ref = rx_ref.at[0], rx_ref.at[1]
    ca_ref, cb_ref = cx_ref.at[0], cx_ref.at[1]

    def assemble(dst, centre, p):
        dst[0:rows, 0:cols] = centre
        dst[rows : rows + h, 0:cols] = ra_ref[p]
        dst[rows + h : rows + 2 * h, 0:cols] = rb_ref[p]
        dst[:, cols : cols + h] = ca_ref[p].T[0 : rows + 2 * h, :]
        dst[:, 2 * cols - h :] = cb_ref[p].T[0 : rows + 2 * h, :]

    assemble(field_ref.at[0], eta_ref[...], 2 * n)
    assemble(field_ref.at[1], fd_ref[0], 2 * n + 1)
    assemble(field_ref.at[2], fd_ref[1], 2 * n + 2)
    eta = field_ref[0]
    free = field_ref[1]
    drag = field_ref[2]
    node_drag = 0.25 * (sh(drag, -1, -1) + sh(drag, 0, -1) + sh(drag, -1, 0) + drag)
    north = sh(eta, 1, 0)
    south = sh(eta, -1, 0)
    east = sh(eta, 0, 1)
    west = sh(eta, 0, -1)
    face_np = 0.5 * (eta + north)
    face_sm = 0.5 * (eta + south)
    face_ep = 0.5 * (eta + east)
    face_wm = 0.5 * (eta + west)
    rows_sum = face_np + face_sm
    cols_sum = face_ep + face_wm
    inv_u = free / (4.0 * rows_sum + cols_sum + node_drag + 1.0 - free)
    inv_v = free / (rows_sum + 4.0 * cols_sum + node_drag + 1.0 - free)
    coefs = [face_np, face_sm, face_ep, face_wm]
    coefs += [4.0 * face_np, 4.0 * face_sm, 4.0 * face_ep, 4.0 * face_wm, node_drag]
    coefs += [0.5 * north, 0.5 * south, 0.25 * east, 0.25 * west]
    coefs += [0.25 * north, 0.25 * south, 0.5 * east, 0.5 * west]
    for k, val in enumerate(coefs + [inv_u, inv_v, free]):
        coef_ref[k] = val
    prod_ref[...] = jnp.zeros_like(prod_ref)
    for c in copies[4:]:
        c.wait()

    def epoch(e, carry):
        for comp in range(comps):
            p = e * comps + comp
            assemble(field_ref.at[3 + comp], f_ref[e, comp], p)
            assemble(field_ref.at[3 + comps + comp], o_ref[e, comp], n + p)
        c = tuple(coef_ref[k] for k in range(17))
        inv_u = coef_ref[17]
        inv_v = coef_ref[18]
        free = coef_ref[19]
        vel_u, vel_v = chebyshev_pair(free * field_ref[3], free * field_ref[4], c, inv_u, inv_v)
        vel_ref[e, 0] = vel_u[0:rows, 0:cols]
        vel_ref[e, 1] = vel_v[0:rows, 0:cols]
        pltpu.make_async_copy(vel_ref.at[e], vel_hbm.at[e], vel_sem.at[e]).start()
        mis_u = free * (vel_u - field_ref[5])
        mis_v = free * (vel_v - field_ref[6])
        adj_u, adj_v = chebyshev_pair(mis_u, mis_v, c, inv_u, inv_v)
        prod_ref[...] += adj_u * vel_u + adj_v * vel_v
        return carry

    lax.fori_loop(0, epochs, epoch, 0)
    product = prod_ref[...]
    for e in range(epochs):
        pltpu.make_async_copy(vel_ref.at[e], vel_hbm.at[e], vel_sem.at[e]).wait()
    rows_sum = product + sh(product, 1, 0)
    total = rows_sum + sh(rows_sum, 0, 1)
    grounded = (ice_ref[...] == 2).astype(jnp.float32)
    grad_ref[...] = -0.25 * grounded * total[0:rows, 0:cols]


def prep_kernel(
    f_hbm, o_hbm, eta_hbm, fric_hbm, ice_hbm, dir_hbm,
    lo_hbm, hi_hbm, clo_hbm, chi_hbm, fd_hbm,
    f_ref, o_ref, eta_ref, fric_ref, ice_ref, dir_ref, lo_ref, hi_ref, clo_ref, chi_ref, fd_ref,
    sem, out_sem,
):
    epochs, comps, rows, cols = f_ref.shape
    h = HALO
    n = epochs * comps
    copies = copy_in(
        [
            (ice_hbm, ice_ref), (dir_hbm, dir_ref), (fric_hbm, fric_ref), (eta_hbm, eta_ref),
            (f_hbm, f_ref), (o_hbm, o_ref),
        ],
        sem,
    )
    for c in copies[:4]:
        c.wait()
    ice = ice_ref[...]
    free = (1 - dir_ref[...]).astype(jnp.float32)
    drag = jnp.where(ice == 2, fric_ref[...], jnp.where(ice == 0, FREE_DRAG, 0.0))
    fd_ref[0] = free
    fd_ref[1] = drag
    for c in copies[4:]:
        c.wait()
    planes = []
    for e in range(epochs):
        for comp in range(comps):
            planes.append(f_ref.at[e, comp])
    for e in range(epochs):
        for comp in range(comps):
            planes.append(o_ref.at[e, comp])
    for p, ref in enumerate(planes):
        lo_ref[p] = ref[0:h, :]
        hi_ref[p] = ref[rows - h : rows, :]
    for k, val in enumerate([eta_ref[...], free, drag]):
        lo_ref[2 * n + k] = val[0:h]
        hi_ref[2 * n + k] = val[rows - h : rows]
    out = copy_in([(lo_ref, lo_hbm), (hi_ref, hi_hbm), (fd_ref, fd_hbm)], out_sem)
    for p, ref in enumerate(planes):
        t = ref[...].T
        clo_ref[p] = t[0:h]
        chi_ref[p] = t[cols - h : cols]
    for k, val in enumerate([eta_ref[...], free, drag]):
        t = val.T
        clo_ref[2 * n + k] = t[0:h]
        chi_ref[2 * n + k] = t[cols - h : cols]
    out += copy_in([(clo_ref, clo_hbm), (chi_ref, chi_hbm)], out_sem.at[3:])
    for c in out:
        c.wait()


def scratch_like(*arrays):
    return [pltpu.VMEM(a.shape, a.dtype) for a in arrays]


def prep(forcing, observed, viscosity, friction, ice_mask, dirichlet):
    epochs, comps, rows, cols = forcing.shape
    planes = 2 * epochs * comps + 3
    hbm = pl.BlockSpec(memory_space=pltpu.HBM)
    slab = jax.ShapeDtypeStruct((planes, HALO, cols), jnp.float32)
    cslab = jax.ShapeDtypeStruct((planes, HALO, rows), jnp.float32)
    fd = jax.ShapeDtypeStruct((2, rows, cols), jnp.float32)
    outs = (slab, slab, cslab, cslab, fd)
    args = (forcing, observed, viscosity, friction, ice_mask, dirichlet)
    return pl.pallas_call(
        prep_kernel,
        out_shape=outs,
        in_specs=[hbm] * 6,
        out_specs=(hbm,) * 5,
        scratch_shapes=scratch_like(*args, *outs)
        + [pltpu.SemaphoreType.DMA((6,)), pltpu.SemaphoreType.DMA((5,))],
    )(*args)


def local_solve(forcing, observed, eta, fd, ice_mask, rows_x, cols_x):
    epochs, comps, rows, cols = forcing.shape
    full = (rows + 2 * HALO, 2 * cols)
    vmem = pl.BlockSpec(memory_space=pltpu.VMEM)
    anywhere = pl.BlockSpec(memory_space=pltpu.HBM)
    nodes = full[0] * full[1]
    args = (forcing, observed, eta, fd, ice_mask, rows_x, cols_x)
    return pl.pallas_call(
        kernel,
        out_shape=(
            jax.ShapeDtypeStruct(forcing.shape, jnp.float32),
            jax.ShapeDtypeStruct((rows, cols), jnp.float32),
        ),
        in_specs=[anywhere] * len(args),
        out_specs=(anywhere, vmem),
        scratch_shapes=scratch_like(*args)
        + [
            pltpu.VMEM((3 + 2 * comps,) + full, jnp.float32),
            pltpu.VMEM((20,) + full, jnp.float32),
            pltpu.VMEM(full, jnp.float32),
            pltpu.VMEM(forcing.shape, jnp.float32),
            pltpu.SemaphoreType.DMA((7,)),
            pltpu.SemaphoreType.DMA((epochs,)),
        ],
        cost_estimate=pl.CostEstimate(
            flops=epochs * 2 * SWEEPS * comps * 60 * nodes,
            bytes_accessed=4 * (3 * epochs * comps + 40) * rows * cols,
            transcendentals=0,
        ),
    )(*args)


def body(forcing, observed, viscosity, friction, ice_mask, dirichlet):
    epochs, comps, rows, cols = forcing.shape
    h = HALO
    lo, hi, clo, chi, fd = prep(forcing, observed, viscosity, friction, ice_mask, dirichlet)
    ra, rb = exchange(lo, hi, "gx")

    def corners(slab, a, b):
        edge = jnp.concatenate([ra[:, :, a:b], rb[:, :, a:b]], axis=1)
        gap = jnp.zeros((slab.shape[0], h, cols - rows - 2 * h), jnp.float32)
        return jnp.concatenate([slab, jnp.swapaxes(edge, 1, 2), gap], axis=2)

    ca, cb = exchange(corners(clo, 0, h), corners(chi, cols - h, cols), "gy")
    return local_solve(forcing, observed, viscosity, fd, ice_mask, jnp.stack([ra, rb]), jnp.stack([ca, cb]))


def solution(mesh):
    return jax.shard_map(
        body,
        mesh=mesh,
        in_specs=(
            P(None, None, "gx", "gy"),
            P(None, None, "gx", "gy"),
            P("gx", "gy"),
            P("gx", "gy"),
            P("gx", "gy"),
            P("gx", "gy"),
        ),
        out_specs=(P(None, None, "gx", "gy"), P("gx", "gy")),
        check_vma=False,
    )
```
